32 devices in a mesh: panel: 2 (over y), lat: 4 (over z), lon: 4 (over x, core).
Axes of the slice: x: 2, y: 2, z: 4, core: 2. Of those that a mesh axis runs over, the one named last changes fastest.
Arguments:
- state: float32 [2, 7, 2, 256, 512], P('panel', None, None, 'lat', 'lon'), may hold values from -4 to 4
- source_slot: int32 [2, 4, 4, 768], P('panel', 'lat', 'lon'), may hold values from 0 to 3071, as said below
- donor_cell: int32 [2, 4, 4, 192], P('panel', 'lat', 'lon'), may hold values from 0 to 8000
- donor_frac: float32 [2, 4, 4, 2, 192], P('panel', 'lat', 'lon'), may hold values from 0 to 1
- donor_turn: float32 [2, 4, 4, 192], P('panel', 'lat', 'lon'), may hold values from -3.140625 to 3.140625
Outputs:
- new_state: float32 [2, 7, 2, 256, 512], P('panel', None, None, 'lat', 'lon')
The draws below stay inside these ranges and needn't reach their ends.
Inputs may be any that keep to these rules, and one draw needn't show every extreme that they name: `source_slot`: entries name a partner panel donation (a * 4 + b) * 192 + s. For a device on an edge of its panel, the rim entries that lie on that edge name the donations that fill them; over a panel's whole border every donation of the partner panel is named exactly once. Other entries are unused.
All inputs are finite; a program needn't handle non-finite values.
Results may differ from the reference program's by a relative error of at most 0.00002.
Values sent between devices are 32-bit elements; how exact they have to be, the bound alone decides.
No kernel may reach another device: no remote copies, remote signals or barrier semaphores. Data moves between devices by JAX's collectives and lax.ppermute only.
A program may use at most 64 MiB of HBM per device.

```python
import jax
import jax.numpy as jnp

COMPS = 7
NR = 2
CLAT = 64
CLON = 128
LAT = 256
LON = 512
DON = 192
N_PANEL = 2
N_LAT = 4
N_LON = 4


def draw_source_slot(key, part):
    total = 4 * (N_LAT * CLAT + N_LON * CLON)
    rim_len = 4 * (CLAT + CLON)
    band = 2 * CLON
    side = 2 * CLAT

    def one_panel(sub):
        key_order, key_fill = jax.random.split(sub)
        order = jax.random.permutation(key_order, total).astype(jnp.int32)
        filler = jax.random.randint(key_fill, (N_LAT, N_LON, rim_len), 0, total, dtype=jnp.int32)
        rows_a = jnp.arange(N_LAT, dtype=jnp.int32)[:, None, None]
        cols_b = jnp.arange(N_LON, dtype=jnp.int32)[None, :, None]
        place = jnp.arange(rim_len, dtype=jnp.int32)[None, None, :]
        on_top = (rows_a == 0) & (place < band)
        on_bottom = (rows_a == N_LAT - 1) & (place >= band) & (place < 2 * band)
        on_left = (cols_b == 0) & (place >= 2 * band) & (place < 2 * band + side)
        on_right = (cols_b == N_LON - 1) & (place >= 2 * band + side)
        k_top = cols_b * band + place
        k_bottom = N_LON * band + cols_b * band + (place - band)
        k_left = 2 * N_LON * band + rows_a * side + (place - 2 * band)
        k_right = 2 * N_LON * band + N_LAT * side + rows_a * side + (place - 2 * band - side)
        border = jnp.where(on_top, k_top, jnp.where(on_bottom, k_bottom, jnp.where(on_left, k_left, k_right)))
        on_edge = on_top | on_bottom | on_left | on_right
        picked = jnp.take(order, jnp.clip(border, 0, total - 1))
        return jnp.where(on_edge, picked, filler)
    return jnp.stack([one_panel(jax.random.fold_in(key, 11)), one_panel(jax.random.fold_in(key, 12))])


def plant(array, rng, smallest, top_value):
    longest = array.shape.index(max(array.shape))
    spots = []
    for shift in (0, 1):
        where = [jax.random.randint(jax.random.fold_in(rng, axis), (), 0, length) for axis, length in enumerate(array.shape)]
        where[longest] = (where[longest] + shift) % array.shape[longest]
        spots.append(tuple(where))
    return array.at[spots[0]].set(smallest).at[spots[1]].set(top_value)


def steps_of(rng, shape, cuts, low, high):
    loudness, own = 1.0, jax.random.fold_in(rng, 6)
    for position, blocks in cuts:
        steps = jnp.exp(jax.random.uniform(jax.random.fold_in(own, position), (blocks,), jnp.float32, low / len(cuts), high / len(cuts)))
        loudness = loudness * jnp.repeat(steps, shape[position] // blocks).reshape([-1 if axis == position else 1 for axis in range(len(shape))])
    return loudness


def bell_draw(stream_key, shape, scale, most, shards=(), held_as=jnp.bfloat16):
    result = jax.random.normal(stream_key, shape, jnp.float32) * scale
    if len(shards) > 0:
        result = steps_of(stream_key, shape, shards, -0.22, 0.18) * result
    return jnp.clip(result, min=-most, max=most).astype(held_as)


def setup_inputs(seed: int = 0) -> dict:
    key_of = jax.random.split(jax.random.key(seed), 6)
    state = bell_draw(key_of[0], (N_PANEL, COMPS, NR, LAT, LON), 1.0, 4.0, ((0, 2), (3, 4), (4, 4)), jnp.float32)
    source_slot = draw_source_slot(jax.random.fold_in(key_of[5], 71), 0)
    donor_cell = plant(jax.random.randint(key_of[2], (N_PANEL, N_LAT, N_LON, DON), 0, (CLAT - 1) * (CLON - 1)), jax.random.fold_in(key_of[2], 1), 0, ((CLAT - 1) * (CLON - 1)) - 1).astype(jnp.int32)
    donor_frac = jnp.clip(1.0 * jax.random.uniform(key_of[3], (N_PANEL, N_LAT, N_LON, 2, DON), jnp.float32) ** steps_of(key_of[3], (N_PANEL, N_LAT, N_LON, 2, DON), ((0, 2), (1, 4), (2, 4)), -0.2, 0.2), 0.0, 1.0)
    donor_turn = jnp.clip(jax.random.uniform(key_of[4], (N_PANEL, N_LAT, N_LON, DON), jnp.float32, -3.140625, 3.140625), -3.140625, 3.140625)
    return {"state": state, "source_slot": source_slot, "donor_cell": donor_cell, "donor_frac": donor_frac, "donor_turn": donor_turn}


viscosity = 0.05
resistivity = 0.05
diffusivity = 0.05
buoyancy = 0.5
time_step = 0.25


def rate(ext):
    height = ext.shape[2] - 4
    width = ext.shape[3] - 4

    def lat_at(k):
        return ext[:, :, 2 + k:2 + k + height, 2:2 + width]

    def lon_at(k):
        return ext[:, :, 2:2 + height, 2 + k:2 + k + width]

    middle = lat_at(0)
    d_lat = (8.0 * (lat_at(1) - lat_at(-1)) - (lat_at(2) - lat_at(-2))) / 12.0
    d_lon = (8.0 * (lon_at(1) - lon_at(-1)) - (lon_at(2) - lon_at(-2))) / 12.0
    padded = jnp.pad(middle, ((0, 0), (1, 1), (0, 0), (0, 0)))
    lap = lat_at(1) + lat_at(-1) + lon_at(1) + lon_at(-1) - 4.0 * middle
    lap = lap + padded[:, 2:] + padded[:, :-2] - 2.0 * middle
    adv_u = middle[1:2] * d_lat + middle[2:3] * d_lon
    adv_b = middle[4:5] * d_lat + middle[5:6] * d_lon
    moment = -adv_u[0:3] + adv_b[3:6] + viscosity * lap[0:3]
    induct = adv_b[0:3] - adv_u[3:6] + resistivity * lap[3:6]
    heat = -adv_u[6:7] + diffusivity * lap[6:7]
    first = moment[0:1] + buoyancy * middle[6:7]
    return jnp.concatenate([first, moment[1:3], induct, heat], axis=0)


def rotate(values, turn):
    cosine = jnp.cos(turn)
    sine = jnp.sin(turn)
    parts = [values[0],
             cosine * values[1] - sine * values[2],
             sine * values[1] + cosine * values[2],
             values[3],
             cosine * values[4] - sine * values[5],
             sine * values[4] + cosine * values[5],
             values[6]]
    return jnp.stack(parts)


def donate(field, donor_cell, donor_frac, donor_turn):
    lat_dev = donor_cell.shape[0]
    lon_dev = donor_cell.shape[1]
    rows_a = jnp.arange(lat_dev, dtype=jnp.int32)[:, None, None]
    cols_b = jnp.arange(lon_dev, dtype=jnp.int32)[None, :, None]
    row = rows_a * CLAT + donor_cell // (CLON - 1)
    col = cols_b * CLON + donor_cell % (CLON - 1)
    index = (row * LON + col).reshape(-1).astype(jnp.int32)
    flat = field.reshape(COMPS, NR, LAT * LON)
    lower = jnp.take(flat, index, axis=2)
    lower_next = jnp.take(flat, index + 1, axis=2)
    upper = jnp.take(flat, index + LON, axis=2)
    upper_next = jnp.take(flat, index + LON + 1, axis=2)
    frac_t = donor_frac[:, :, 0, :].reshape(-1)
    frac_p = donor_frac[:, :, 1, :].reshape(-1)
    value = ((1.0 - frac_t) * (1.0 - frac_p) * lower + (1.0 - frac_t) * frac_p * lower_next
             + frac_t * (1.0 - frac_p) * upper + frac_t * frac_p * upper_next)
    return rotate(value, donor_turn.reshape(-1))


def extend(field, donation, slots):
    lat_dev = slots.shape[0]
    lon_dev = slots.shape[1]
    rim_values = jnp.take(donation, slots, axis=2)
    ext = jnp.pad(field, ((0, 0), (0, 0), (2, 2), (2, 2)))
    top = rim_values[:, :, 0, :, 0:2 * CLON].reshape(COMPS, NR, lon_dev, 2, CLON)
    top = jnp.transpose(top, (0, 1, 3, 2, 4)).reshape(COMPS, NR, 2, LON)
    bottom = rim_values[:, :, lat_dev - 1, :, 2 * CLON:4 * CLON].reshape(COMPS, NR, lon_dev, 2, CLON)
    bottom = jnp.transpose(bottom, (0, 1, 3, 2, 4)).reshape(COMPS, NR, 2, LON)
    left = rim_values[:, :, :, 0, 4 * CLON:4 * CLON + 2 * CLAT].reshape(COMPS, NR, lat_dev, 2, CLAT)
    left = jnp.transpose(left, (0, 1, 2, 4, 3)).reshape(COMPS, NR, LAT, 2)
    right = rim_values[:, :, :, lon_dev - 1, 4 * CLON + 2 * CLAT:].reshape(COMPS, NR, lat_dev, 2, CLAT)
    right = jnp.transpose(right, (0, 1, 2, 4, 3)).reshape(COMPS, NR, LAT, 2)
    ext = ext.at[:, :, 0:2, 2:2 + LON].set(top)
    ext = ext.at[:, :, LAT + 2:LAT + 4, 2:2 + LON].set(bottom)
    ext = ext.at[:, :, 2:2 + LAT, 0:2].set(left)
    ext = ext.at[:, :, 2:2 + LAT, LON + 2:LON + 4].set(right)
    return ext


def section_rate(fields, source_slot, donor_cell, donor_frac, donor_turn):
    given = [donate(fields[q], donor_cell[q], donor_frac[q], donor_turn[q]) for q in range(2)]
    rates = [rate(extend(fields[p], given[1 - p], source_slot[p])) for p in range(2)]
    return jnp.stack(rates)


def reference(state, source_slot, donor_cell, donor_frac, donor_turn):
    section_one = state + time_step * section_rate(state, source_slot, donor_cell, donor_frac, donor_turn)
    second = section_rate(section_one, source_slot, donor_cell, donor_frac, donor_turn)
    return 0.5 * state + 0.5 * (section_one + time_step * second)
```

```python
import jax
import jax.numpy as jnp
from jax import lax
from jax.sharding import PartitionSpec as P

viscosity = 0.05
resistivity = 0.05
diffusivity = 0.05
buoyancy = 0.5
time_step = 0.25

HIGHEST = lax.Precision.HIGHEST


def partner_2(block, axis, apart):
    count = lax.axis_size(axis)
    route = []
    for low in range(count):
        high = low | 1 << apart
        if high != low and high < count:
            route += [(low, high), (high, low)]
    return lax.ppermute(block, axis, route)


def shift(value, axis, step):
    size = lax.axis_size(axis)
    if step > 0:
        route = [(i, i + 1) for i in range(size - 1)]
    else:
        route = [(i + 1, i) for i in range(size - 1)]
    return lax.ppermute(value, axis, route)


def rate(up, mid, down, left, right):
    vert = jnp.concatenate([up, mid, down], axis=2)
    horz = jnp.concatenate([left, mid, right], axis=3)
    height = mid.shape[2]
    width = mid.shape[3]

    def lat_at(k):
        return vert[:, :, 2 + k : 2 + k + height, :]

    def lon_at(k):
        return horz[:, :, :, 2 + k : 2 + k + width]

    middle = mid
    d_lat = (8.0 * (lat_at(1) - lat_at(-1)) - (lat_at(2) - lat_at(-2))) / 12.0
    d_lon = (8.0 * (lon_at(1) - lon_at(-1)) - (lon_at(2) - lon_at(-2))) / 12.0
    padded = jnp.pad(middle, ((0, 0), (1, 1), (0, 0), (0, 0)))
    lap = lat_at(1) + lat_at(-1) + lon_at(1) + lon_at(-1) - 4.0 * middle
    lap = lap + padded[:, 2:] + padded[:, :-2] - 2.0 * middle
    adv_u = middle[1:2] * d_lat + middle[2:3] * d_lon
    adv_b = middle[4:5] * d_lat + middle[5:6] * d_lon
    moment = -adv_u[0:3] + adv_b[3:6] + viscosity * lap[0:3]
    induct = adv_b[0:3] - adv_u[3:6] + resistivity * lap[3:6]
    heat = -adv_u[6:7] + diffusivity * lap[6:7]
    first = moment[0:1] + buoyancy * middle[6:7]
    return jnp.concatenate([first, moment[1:3], induct, heat], axis=0)


def rotate(values, turn):
    cosine = jnp.cos(turn)
    sine = jnp.sin(turn)
    parts = [
        values[0],
        cosine * values[1] - sine * values[2],
        sine * values[1] + cosine * values[2],
        values[3],
        cosine * values[4] - sine * values[5],
        sine * values[4] + cosine * values[5],
        values[6],
    ]
    return jnp.stack(parts)


def per_device(state, source_slot, donor_cell, donor_frac, donor_turn):
    comps = state.shape[1]
    levels = state.shape[2]
    rows = state.shape[3]
    cols = state.shape[4]
    cells = donor_cell[0, 0, 0]
    frac_t = donor_frac[0, 0, 0, 0]
    frac_p = donor_frac[0, 0, 0, 1]
    turn = donor_turn[0, 0, 0]
    slots = source_slot[0, 0, 0]
    lat_pos = lax.axis_index("lat")
    lon_pos = lax.axis_index("lon")
    lat_count = lax.axis_size("lat")
    lon_count = lax.axis_size("lon")
    on_top = lat_pos == 0
    on_bottom = lat_pos == lat_count - 1
    on_left = lon_pos == 0
    on_right = lon_pos == lon_count - 1

    row = cells // (cols - 1)
    col = cells % (cols - 1)
    col_ids = jnp.arange(cols, dtype=jnp.int32)[None, :]
    row_ids = jnp.arange(rows, dtype=jnp.int32)[None, :]
    weight_lon = jnp.where(col_ids == col[:, None], (1.0 - frac_p)[:, None], 0.0) + jnp.where(
        col_ids == col[:, None] + 1, frac_p[:, None], 0.0
    )
    weight_lat = jnp.where(row_ids == row[:, None], (1.0 - frac_t)[:, None], 0.0) + jnp.where(
        row_ids == row[:, None] + 1, frac_t[:, None], 0.0
    )

    band = 2 * cols
    side = 2 * rows
    lat_slots = jnp.where(on_top, slots[0:band], slots[band : 2 * band])
    lon_slots = jnp.where(on_left, slots[2 * band : 2 * band + side], slots[2 * band + side :])
    wanted = jnp.concatenate([lat_slots, lon_slots])
    total = lax.axis_size("lat") * lax.axis_size("lon") * cells.shape[0]
    pick = (jnp.arange(total, dtype=jnp.int32)[:, None] == wanted[None, :]).astype(jnp.float32)

    def donate(field):
        flat = field.reshape(comps * levels, rows, cols)
        along = jnp.einsum("kij,sj->kis", flat, weight_lon, precision=HIGHEST)
        value = jnp.sum(along * weight_lat.T[None], axis=1)
        return rotate(value.reshape(comps, levels, -1), turn).reshape(comps * levels, -1)

    def receive(given):
        whole = lax.all_gather(given, ("lat", "lon"), axis=1, tiled=True)
        partner = partner_2(whole, "panel", 0)
        return jnp.dot(partner, pick, precision=HIGHEST)

    def section(field):
        up = shift(field[:, :, rows - 2 :, :], "lat", 1)
        down = shift(field[:, :, :2, :], "lat", -1)
        left = shift(field[:, :, :, cols - 2 :], "lon", 1)
        right = shift(field[:, :, :, :2], "lon", -1)
        rim = receive(donate(field)).reshape(comps, levels, -1)
        rim_lat = rim[:, :, :band].reshape(comps, levels, 2, cols)
        rim_lon = jnp.transpose(rim[:, :, band:].reshape(comps, levels, 2, rows), (0, 1, 3, 2))
        up = jnp.where(on_top, rim_lat, up)
        down = jnp.where(on_bottom, rim_lat, down)
        left = jnp.where(on_left, rim_lon, left)
        right = jnp.where(on_right, rim_lon, right)
        return rate(up, field, down, left, right)

    field = state[0]
    section_one = field + time_step * section(field)
    second = section(section_one)
    new_field = 0.5 * field + 0.5 * (section_one + time_step * second)
    return new_field[None]


def solution(mesh):
    in_specs = (
        P("panel", None, None, "lat", "lon"),
        P("panel", "lat", "lon", None),
        P("panel", "lat", "lon", None),
        P("panel", "lat", "lon", None, None),
        P("panel", "lat", "lon", None),
    )
    out_specs = P("panel", None, None, "lat", "lon")
    return jax.shard_map(
        per_device, mesh=mesh, in_specs=in_specs, out_specs=out_specs, check_vma=False
    )
```

```python
import jax
import jax.numpy as jnp
from jax import lax
from jax.sharding import PartitionSpec as P

viscosity = 0.05
resistivity = 0.05
diffusivity = 0.05
buoyancy = 0.5
time_step = 0.25

HIGHEST = lax.Precision.HIGHEST


def rate(up, mid, down, left, right):
    vert = jnp.concatenate([up, mid, down], axis=2)
    horz = jnp.concatenate([left, mid, right], axis=3)
    height = mid.shape[2]
    width = mid.shape[3]

    def lat_at(k):
        return vert[:, :, 2 + k : 2 + k + height, :]

    def lon_at(k):
        return horz[:, :, :, 2 + k : 2 + k + width]

    middle = mid
    d_lat = (8.0 * (lat_at(1) - lat_at(-1)) - (lat_at(2) - lat_at(-2))) / 12.0
    d_lon = (8.0 * (lon_at(1) - lon_at(-1)) - (lon_at(2) - lon_at(-2))) / 12.0
    padded = jnp.pad(middle, ((0, 0), (1, 1), (0, 0), (0, 0)))
    lap = lat_at(1) + lat_at(-1) + lon_at(1) + lon_at(-1) - 4.0 * middle
    lap = lap + padded[:, 2:] + padded[:, :-2] - 2.0 * middle
    adv_u = middle[1:2] * d_lat + middle[2:3] * d_lon
    adv_b = middle[4:5] * d_lat + middle[5:6] * d_lon
    moment = -adv_u[0:3] + adv_b[3:6] + viscosity * lap[0:3]
    induct = adv_b[0:3] - adv_u[3:6] + resistivity * lap[3:6]
    heat = -adv_u[6:7] + diffusivity * lap[6:7]
    first = moment[0:1] + buoyancy * middle[6:7]
    return jnp.concatenate([first, moment[1:3], induct, heat], axis=0)


def rotate(values, turn):
    cosine = jnp.cos(turn)
    sine = jnp.sin(turn)
    parts = [
        values[0],
        cosine * values[1] - sine * values[2],
        sine * values[1] + cosine * values[2],
        values[3],
        cosine * values[4] - sine * values[5],
        sine * values[4] + cosine * values[5],
        values[6],
    ]
    return jnp.stack(parts)


def per_device(state, source_slot, donor_cell, donor_frac, donor_turn):
    comps = state.shape[1]
    levels = state.shape[2]
    rows = state.shape[3]
    cols = state.shape[4]
    cells = donor_cell[0, 0, 0]
    frac_t = donor_frac[0, 0, 0, 0]
    frac_p = donor_frac[0, 0, 0, 1]
    turn = donor_turn[0, 0, 0]
    slots = source_slot[0, 0, 0]
    lat_pos = lax.axis_index("lat")
    lon_pos = lax.axis_index("lon")
    lat_count = lax.axis_size("lat")
    lon_count = lax.axis_size("lon")
    on_top = lat_pos == 0
    on_bottom = lat_pos == lat_count - 1
    on_left = lon_pos == 0
    on_right = lon_pos == lon_count - 1

    row = cells // (cols - 1)
    col = cells % (cols - 1)
    col_ids = jnp.arange(cols, dtype=jnp.int32)[None, :]
    row_ids = jnp.arange(rows, dtype=jnp.int32)[None, :]
    weight_lon = jnp.where(col_ids == col[:, None], (1.0 - frac_p)[:, None], 0.0) + jnp.where(
        col_ids == col[:, None] + 1, frac_p[:, None], 0.0
    )
    weight_lat = jnp.where(row_ids == row[:, None], (1.0 - frac_t)[:, None], 0.0) + jnp.where(
        row_ids == row[:, None] + 1, frac_t[:, None], 0.0
    )

    band = 2 * cols
    side = 2 * rows
    lat_slots = jnp.where(on_top, slots[0:band], slots[band : 2 * band])
    lon_slots = jnp.where(on_left, slots[2 * band : 2 * band + side], slots[2 * band + side :])
    wanted = jnp.concatenate([lat_slots, lon_slots])
    total = lax.axis_size("lat") * lax.axis_size("lon") * cells.shape[0]
    pick = (jnp.arange(total, dtype=jnp.int32)[:, None] == wanted[None, :]).astype(jnp.float32)

    def donate(field):
        flat = field.reshape(comps * levels, rows, cols)
        along = jnp.einsum("kij,sj->kis", flat, weight_lon, precision=HIGHEST)
        value = jnp.sum(along * weight_lat.T[None], axis=1)
        return rotate(value.reshape(comps, levels, -1), turn).reshape(comps * levels, -1)

    def gather(packet, axis):
        size = lax.axis_size(axis)
        pos = lax.axis_index(axis)
        held = packet[None]
        k = 1
        while k < size:
            other = lax.ppermute(held, axis, [(i, i ^ k) for i in range(size)])
            low = (pos // k) % 2 == 0
            held = jnp.where(low, jnp.concatenate([held, other]), jnp.concatenate([other, held]))
            k *= 2
        return held

    def section(field):
        flat = field.reshape(comps * levels, rows, cols)
        given = lax.ppermute(donate(field), "panel", [(0, 1), (1, 0)])
        dons = given.shape[1]
        side_cols = jnp.concatenate([flat[:, :, :2], flat[:, :, cols - 2 :]], axis=2)
        lon_packet = jnp.concatenate([given, side_cols.reshape(comps * levels, -1)], axis=1)
        lon_all = gather(lon_packet, "lon")
        row_given = jnp.transpose(lon_all[:, :, :dons], (1, 0, 2)).reshape(comps * levels, -1)
        side_cols = lon_all[:, :, dons:].reshape(lon_count, comps, levels, rows, 4)
        side_rows = jnp.concatenate([flat[:, :2, :], flat[:, rows - 2 :, :]], axis=1)
        lat_packet = jnp.concatenate([row_given, side_rows.reshape(comps * levels, -1)], axis=1)
        lat_all = gather(lat_packet, "lat")
        width = row_given.shape[1]
        partner = jnp.transpose(lat_all[:, :, :width], (1, 0, 2)).reshape(comps * levels, -1)
        side_rows = lat_all[:, :, width:].reshape(lat_count, comps, levels, 4, cols)
        up = lax.dynamic_index_in_dim(side_rows, jnp.maximum(lat_pos - 1, 0), keepdims=False)[:, :, 2:]
        down = lax.dynamic_index_in_dim(side_rows, jnp.minimum(lat_pos + 1, lat_count - 1), keepdims=False)[:, :, :2]
        left = lax.dynamic_index_in_dim(side_cols, jnp.maximum(lon_pos - 1, 0), keepdims=False)[..., 2:]
        right = lax.dynamic_index_in_dim(side_cols, jnp.minimum(lon_pos + 1, lon_count - 1), keepdims=False)[..., :2]
        rim = jnp.dot(partner, pick, precision=HIGHEST).reshape(comps, levels, -1)
        rim_lat = rim[:, :, :band].reshape(comps, levels, 2, cols)
        rim_lon = jnp.transpose(rim[:, :, band:].reshape(comps, levels, 2, rows), (0, 1, 3, 2))
        up = jnp.where(on_top, rim_lat, up)
        down = jnp.where(on_bottom, rim_lat, down)
        left = jnp.where(on_left, rim_lon, left)
        right = jnp.where(on_right, rim_lon, right)
        return rate(up, field, down, left, right)

    field = state[0]
    section_one = field + time_step * section(field)
    second = section(section_one)
    new_field = 0.5 * field + 0.5 * (section_one + time_step * second)
    return new_field[None]


def solution(mesh):
    in_specs = (
        P("panel", None, None, "lat", "lon"),
        P("panel", "lat", "lon", None),
        P("panel", "lat", "lon", None),
        P("panel", "lat", "lon", None, None),
        P("panel", "lat", "lon", None),
    )
    out_specs = P("panel", None, None, "lat", "lon")
    return jax.shard_map(
        per_device, mesh=mesh, in_specs=in_specs, out_specs=out_specs, check_vma=False
    )
```

```python
import jax
import jax.numpy as jnp
from jax import lax
from jax.sharding import PartitionSpec as P

viscosity = 0.05
resistivity = 0.05
diffusivity = 0.05
buoyancy = 0.5
time_step = 0.25

HIGHEST = lax.Precision.HIGHEST


def rate(up, mid, down, left, right):
    vert = jnp.concatenate([up, mid, down], axis=2)
    horz = jnp.concatenate([left, mid, right], axis=3)
    height = mid.shape[2]
    width = mid.shape[3]

    def lat_at(k):
        return vert[:, :, 2 + k : 2 + k + height, :]

    def lon_at(k):
        return horz[:, :, :, 2 + k : 2 + k + width]

    middle = mid
    d_lat = (8.0 * (lat_at(1) - lat_at(-1)) - (lat_at(2) - lat_at(-2))) / 12.0
    d_lon = (8.0 * (lon_at(1) - lon_at(-1)) - (lon_at(2) - lon_at(-2))) / 12.0
    padded = jnp.pad(middle, ((0, 0), (1, 1), (0, 0), (0, 0)))
    lap = lat_at(1) + lat_at(-1) + lon_at(1) + lon_at(-1) - 4.0 * middle
    lap = lap + padded[:, 2:] + padded[:, :-2] - 2.0 * middle
    adv_u = middle[1:2] * d_lat + middle[2:3] * d_lon
    adv_b = middle[4:5] * d_lat + middle[5:6] * d_lon
    moment = -adv_u[0:3] + adv_b[3:6] + viscosity * lap[0:3]
    induct = adv_b[0:3] - adv_u[3:6] + resistivity * lap[3:6]
    heat = -adv_u[6:7] + diffusivity * lap[6:7]
    first = moment[0:1] + buoyancy * middle[6:7]
    return jnp.concatenate([first, moment[1:3], induct, heat], axis=0)


def rotate(values, turn):
    cosine = jnp.cos(turn)
    sine = jnp.sin(turn)
    parts = [
        values[0],
        cosine * values[1] - sine * values[2],
        sine * values[1] + cosine * values[2],
        values[3],
        cosine * values[4] - sine * values[5],
        sine * values[4] + cosine * values[5],
        values[6],
    ]
    return jnp.stack(parts)


def per_device(state, source_slot, donor_cell, donor_frac, donor_turn):
    comps = state.shape[1]
    levels = state.shape[2]
    rows = state.shape[3]
    cols = state.shape[4]
    cells = donor_cell[0, 0, 0]
    frac_t = donor_frac[0, 0, 0, 0]
    frac_p = donor_frac[0, 0, 0, 1]
    turn = donor_turn[0, 0, 0]
    slots = source_slot[0, 0, 0]
    lat_pos = lax.axis_index("lat")
    lon_pos = lax.axis_index("lon")
    lat_count = lax.axis_size("lat")
    lon_count = lax.axis_size("lon")
    on_top = lat_pos == 0
    on_bottom = lat_pos == lat_count - 1
    on_left = lon_pos == 0
    on_right = lon_pos == lon_count - 1

    row = cells // (cols - 1)
    col = cells % (cols - 1)
    col_ids = jnp.arange(cols, dtype=jnp.int32)[None, :]
    row_ids = jnp.arange(rows, dtype=jnp.int32)[None, :]
    weight_lon = jnp.where(col_ids == col[:, None], (1.0 - frac_p)[:, None], 0.0) + jnp.where(
        col_ids == col[:, None] + 1, frac_p[:, None], 0.0
    )
    weight_lat = jnp.where(row_ids == row[:, None], (1.0 - frac_t)[:, None], 0.0) + jnp.where(
        row_ids == row[:, None] + 1, frac_t[:, None], 0.0
    )

    band = 2 * cols
    side = 2 * rows
    lat_slots = jnp.where(on_top, slots[0:band], slots[band : 2 * band])
    lon_slots = jnp.where(on_left, slots[2 * band : 2 * band + side], slots[2 * band + side :])
    wanted = jnp.concatenate([lat_slots, lon_slots])
    dons = cells.shape[0]
    lane = 256
    donor = wanted // dons
    held_lat = donor // lon_count ^ lat_pos
    held_lon = donor % lon_count ^ lon_pos
    place = (held_lat * lon_count + held_lon) * lane + wanted % dons
    total = lat_count * lon_count * lane
    pick = (jnp.arange(total, dtype=jnp.int32)[:, None] == place[None, :]).astype(jnp.bfloat16)

    def select(values):
        high = lax.reduce_precision(values, exponent_bits=8, mantissa_bits=7)
        rest = values - high
        middle = lax.reduce_precision(rest, exponent_bits=8, mantissa_bits=7)
        low = rest - middle
        parts = [part.astype(jnp.bfloat16) for part in (high, middle, low)]
        out = [jnp.dot(part, pick, preferred_element_type=jnp.float32) for part in parts]
        return out[0] + (out[1] + out[2])

    def donate(field):
        flat = field.reshape(comps * levels, rows, cols)
        along = jnp.einsum("kij,sj->kis", flat, weight_lon, precision=HIGHEST)
        value = jnp.sum(along * weight_lat.T[None], axis=1)
        return rotate(value.reshape(comps, levels, -1), turn).reshape(comps * levels, -1)

    def gather(packet, axis):
        size = lax.axis_size(axis)
        held = packet
        k = 1
        while k < size:
            other = lax.ppermute(held, axis, [(i, i ^ k) for i in range(size)])
            held = jnp.concatenate([held, other])
            k *= 2
        return held

    def section(field):
        flat = field.reshape(comps * levels, rows, cols)
        given = lax.ppermute(donate(field), "panel", [(0, 1), (1, 0)])
        given = jnp.pad(given, ((0, 0), (0, lane - dons)))
        side_cols = jnp.concatenate([flat[:, :, :2], flat[:, :, cols - 2 :]], axis=2)
        side_cols = jnp.transpose(side_cols, (0, 2, 1)).reshape(comps * levels, -1)
        lon_all = gather(jnp.stack([given, side_cols]), "lon").reshape(lon_count, 2, comps * levels, lane)
        side_rows = jnp.concatenate([flat[:, :2, :], flat[:, rows - 2 :, :]], axis=1)
        side_rows = side_rows.reshape(comps * levels, 2, lane).transpose(1, 0, 2)
        lat_packet = jnp.concatenate([lon_all[:, 0], side_rows])
        lat_all = gather(lat_packet, "lat").reshape(lat_count, lon_count + 2, comps * levels, lane)
        partner = jnp.transpose(lat_all[:, :lon_count], (2, 0, 1, 3)).reshape(comps * levels, -1)
        side_rows = lat_all[:, lon_count:].transpose(0, 2, 1, 3).reshape(lat_count, comps, levels, 4, cols)
        side_cols = lon_all[:, 1].reshape(lon_count, comps, levels, 4, rows)
        up = lax.dynamic_index_in_dim(side_rows, lat_pos ^ jnp.maximum(lat_pos - 1, 0), keepdims=False)[:, :, 2:]
        down = lax.dynamic_index_in_dim(side_rows, lat_pos ^ jnp.minimum(lat_pos + 1, lat_count - 1), keepdims=False)[:, :, :2]
        left = lax.dynamic_index_in_dim(side_cols, lon_pos ^ jnp.maximum(lon_pos - 1, 0), keepdims=False)[:, :, 2:]
        right = lax.dynamic_index_in_dim(side_cols, lon_pos ^ jnp.minimum(lon_pos + 1, lon_count - 1), keepdims=False)[:, :, :2]
        left = jnp.transpose(left, (0, 1, 3, 2))
        right = jnp.transpose(right, (0, 1, 3, 2))
        rim = select(partner).reshape(comps, levels, -1)
        rim_lat = rim[:, :, :band].reshape(comps, levels, 2, cols)
        rim_lon = jnp.transpose(rim[:, :, band:].reshape(comps, levels, 2, rows), (0, 1, 3, 2))
        up = jnp.where(on_top, rim_lat, up)
        down = jnp.where(on_bottom, rim_lat, down)
        left = jnp.where(on_left, rim_lon, left)
        right = jnp.where(on_right, rim_lon, right)
        return rate(up, field, down, left, right)

    field = state[0]
    section_one = field + time_step * section(field)
    second = section(section_one)
    new_field = 0.5 * field + 0.5 * (section_one + time_step * second)
    return new_field[None]


def solution(mesh):
    in_specs = (
        P("panel", None, None, "lat", "lon"),
        P("panel", "lat", "lon", None),
        P("panel", "lat", "lon", None),
        P("panel", "lat", "lon", None, None),
        P("panel", "lat", "lon", None),
    )
    out_specs = P("panel", None, None, "lat", "lon")
    return jax.shard_map(
        per_device, mesh=mesh, in_specs=in_specs, out_specs=out_specs, check_vma=False
    )
```

```python
import jax
import jax.numpy as jnp
from jax import lax
from jax.sharding import PartitionSpec as P
from jax.experimental import pallas as pl
from jax.experimental.pallas import tpu as pltpu
import functools

INTERPRET = False

viscosity = 0.05
resistivity = 0.05
diffusivity = 0.05
buoyancy = 0.5
time_step = 0.25

HIGHEST = lax.Precision.HIGHEST


def stencil_kernel(f_ref, up_ref, down_ref, left_ref, right_ref, base_ref, o_ref, *, first):
    planes, height, width = f_ref.shape
    comps = planes // 2
    row = lax.broadcasted_iota(jnp.int32, (height, width), 0)
    col = lax.broadcasted_iota(jnp.int32, (height, width), 1)

    def terms(k):
        x = f_ref[k]
        up = up_ref[k]
        down = down_ref[k]
        left = left_ref[k]
        right = right_ref[k]
        lat_m1 = jnp.where(row == 0, up[1:2, :], pltpu.roll(x, 1, 0))
        lat_m2 = jnp.where(row == 0, up[0:1, :], jnp.where(row == 1, up[1:2, :], pltpu.roll(x, 2, 0)))
        lat_p1 = jnp.where(row == height - 1, down[0:1, :], pltpu.roll(x, height - 1, 0))
        lat_p2 = jnp.where(
            row == height - 1, down[1:2, :], jnp.where(row == height - 2, down[0:1, :], pltpu.roll(x, height - 2, 0))
        )
        lon_m1 = jnp.where(col == 0, left[:, 1:2], pltpu.roll(x, 1, 1))
        lon_m2 = jnp.where(col == 0, left[:, 0:1], jnp.where(col == 1, left[:, 1:2], pltpu.roll(x, 2, 1)))
        lon_p1 = jnp.where(col == width - 1, right[:, 0:1], pltpu.roll(x, width - 1, 1))
        lon_p2 = jnp.where(
            col == width - 1, right[:, 1:2], jnp.where(col == width - 2, right[:, 0:1], pltpu.roll(x, width - 2, 1))
        )
        d_lat = (8.0 * (lat_p1 - lat_m1) - (lat_p2 - lat_m2)) / 12.0
        d_lon = (8.0 * (lon_p1 - lon_m1) - (lon_p2 - lon_m2)) / 12.0
        lap = lat_p1 + lat_m1 + lon_p1 + lon_m1 - 4.0 * x
        return x, d_lat, d_lon, lap

    for level in range(2):
        def plane(c):
            return c * 2 + level

        def value(c):
            return f_ref[plane(c)]

        def lap_of(c, x, lap):
            above = f_ref[c * 2 + 1] if level == 0 else 0.0
            below = f_ref[c * 2] if level == 1 else 0.0
            return lap + above + below - 2.0 * x

        def store(c, x, rate):
            section = x + time_step * rate
            if first:
                o_ref[plane(c)] = section
            else:
                o_ref[plane(c)] = 0.5 * base_ref[plane(c)] + 0.5 * section

        u1, u2, u4, u5, u6 = value(1), value(2), value(4), value(5), value(6)
        for c in range(3):
            xa, lat_a, lon_a, lap_a = terms(plane(c))
            xb, lat_b, lon_b, lap_b = terms(plane(c + 3))
            adv_u_a = u1 * lat_a + u2 * lon_a
            adv_b_a = u4 * lat_a + u5 * lon_a
            adv_u_b = u1 * lat_b + u2 * lon_b
            adv_b_b = u4 * lat_b + u5 * lon_b
            rate_a = -adv_u_a + adv_b_b + viscosity * lap_of(c, xa, lap_a)
            if c == 0:
                rate_a = rate_a + buoyancy * u6
            rate_b = adv_b_a - adv_u_b + resistivity * lap_of(c + 3, xb, lap_b)
            store(c, xa, rate_a)
            store(c + 3, xb, rate_b)
        x6, lat_6, lon_6, lap_6 = terms(plane(6))
        adv_u_6 = u1 * lat_6 + u2 * lon_6
        store(6, x6, -adv_u_6 + diffusivity * lap_of(6, x6, lap_6))


def advance(field, up, down, left, right, base, first):
    return pl.pallas_call(
        functools.partial(stencil_kernel, first=first),
        out_shape=jax.ShapeDtypeStruct(field.shape, field.dtype),
        interpret=INTERPRET,
    )(field, up, down, left, right, base)


def rotate(values, turn):
    cosine = jnp.cos(turn)
    sine = jnp.sin(turn)
    parts = [
        values[0],
        cosine * values[1] - sine * values[2],
        sine * values[1] + cosine * values[2],
        values[3],
        cosine * values[4] - sine * values[5],
        sine * values[4] + cosine * values[5],
        values[6],
    ]
    return jnp.stack(parts)


def per_device(state, source_slot, donor_cell, donor_frac, donor_turn):
    comps = state.shape[1]
    levels = state.shape[2]
    rows = state.shape[3]
    cols = state.shape[4]
    cells = donor_cell[0, 0, 0]
    frac_t = donor_frac[0, 0, 0, 0]
    frac_p = donor_frac[0, 0, 0, 1]
    turn = donor_turn[0, 0, 0]
    slots = source_slot[0, 0, 0]
    lat_pos = lax.axis_index("lat")
    lon_pos = lax.axis_index("lon")
    lat_count = lax.axis_size("lat")
    lon_count = lax.axis_size("lon")
    on_top = lat_pos == 0
    on_bottom = lat_pos == lat_count - 1
    on_left = lon_pos == 0
    on_right = lon_pos == lon_count - 1

    row = cells // (cols - 1)
    col = cells % (cols - 1)
    col_ids = jnp.arange(cols, dtype=jnp.int32)[None, :]
    row_ids = jnp.arange(rows, dtype=jnp.int32)[None, :]
    weight_lon = jnp.where(col_ids == col[:, None], (1.0 - frac_p)[:, None], 0.0) + jnp.where(
        col_ids == col[:, None] + 1, frac_p[:, None], 0.0
    )
    weight_lat = jnp.where(row_ids == row[:, None], (1.0 - frac_t)[:, None], 0.0) + jnp.where(
        row_ids == row[:, None] + 1, frac_t[:, None], 0.0
    )

    band = 2 * cols
    side = 2 * rows
    lat_slots = jnp.where(on_top, slots[0:band], slots[band : 2 * band])
    lon_slots = jnp.where(on_left, slots[2 * band : 2 * band + side], slots[2 * band + side :])
    wanted = jnp.concatenate([lat_slots, lon_slots])
    total = lax.axis_size("lat") * lax.axis_size("lon") * cells.shape[0]
    pick = (jnp.arange(total, dtype=jnp.int32)[:, None] == wanted[None, :]).astype(jnp.float32)

    def donate(field):
        flat = field.reshape(comps * levels, rows, cols)
        along = jnp.einsum("kij,sj->kis", flat, weight_lon, precision=HIGHEST)
        value = jnp.sum(along * weight_lat.T[None], axis=1)
        return rotate(value.reshape(comps, levels, -1), turn).reshape(comps * levels, -1)

    def gather(packet, axis):
        size = lax.axis_size(axis)
        pos = lax.axis_index(axis)
        held = packet[None]
        k = 1
        while k < size:
            other = lax.ppermute(held, axis, [(i, i ^ k) for i in range(size)])
            low = (pos // k) % 2 == 0
            held = jnp.where(low, jnp.concatenate([held, other]), jnp.concatenate([other, held]))
            k *= 2
        return held

    def section(field):
        flat = field.reshape(comps * levels, rows, cols)
        given = lax.ppermute(donate(field), "panel", [(0, 1), (1, 0)])
        dons = given.shape[1]
        side_cols = jnp.concatenate([flat[:, :, :2], flat[:, :, cols - 2 :]], axis=2)
        lon_packet = jnp.concatenate([given, side_cols.reshape(comps * levels, -1)], axis=1)
        lon_all = gather(lon_packet, "lon")
        row_given = jnp.transpose(lon_all[:, :, :dons], (1, 0, 2)).reshape(comps * levels, -1)
        side_cols = lon_all[:, :, dons:].reshape(lon_count, comps, levels, rows, 4)
        side_rows = jnp.concatenate([flat[:, :2, :], flat[:, rows - 2 :, :]], axis=1)
        lat_packet = jnp.concatenate([row_given, side_rows.reshape(comps * levels, -1)], axis=1)
        lat_all = gather(lat_packet, "lat")
        width = row_given.shape[1]
        partner = jnp.transpose(lat_all[:, :, :width], (1, 0, 2)).reshape(comps * levels, -1)
        side_rows = lat_all[:, :, width:].reshape(lat_count, comps, levels, 4, cols)
        up = lax.dynamic_index_in_dim(side_rows, jnp.maximum(lat_pos - 1, 0), keepdims=False)[:, :, 2:]
        down = lax.dynamic_index_in_dim(side_rows, jnp.minimum(lat_pos + 1, lat_count - 1), keepdims=False)[:, :, :2]
        left = lax.dynamic_index_in_dim(side_cols, jnp.maximum(lon_pos - 1, 0), keepdims=False)[..., 2:]
        right = lax.dynamic_index_in_dim(side_cols, jnp.minimum(lon_pos + 1, lon_count - 1), keepdims=False)[..., :2]
        rim = jnp.dot(partner, pick, precision=HIGHEST).reshape(comps, levels, -1)
        rim_lat = rim[:, :, :band].reshape(comps, levels, 2, cols)
        rim_lon = jnp.transpose(rim[:, :, band:].reshape(comps, levels, 2, rows), (0, 1, 3, 2))
        up = jnp.where(on_top, rim_lat, up).reshape(comps * levels, 2, cols)
        down = jnp.where(on_bottom, rim_lat, down).reshape(comps * levels, 2, cols)
        left = jnp.where(on_left, rim_lon, left).reshape(comps * levels, rows, 2)
        right = jnp.where(on_right, rim_lon, right).reshape(comps * levels, rows, 2)
        return up, down, left, right

    field = state[0].reshape(comps * levels, rows, cols)
    section_one = advance(field, *section(field), field, True)
    new_field = advance(section_one, *section(section_one), field, False)
    return new_field.reshape(1, comps, levels, rows, cols)


def solution(mesh):
    in_specs = (
        P("panel", None, None, "lat", "lon"),
        P("panel", "lat", "lon", None),
        P("panel", "lat", "lon", None),
        P("panel", "lat", "lon", None, None),
        P("panel", "lat", "lon", None),
    )
    out_specs = P("panel", None, None, "lat", "lon")
    return jax.shard_map(
        per_device, mesh=mesh, in_specs=in_specs, out_specs=out_specs, check_vma=False
    )
```

```python
import jax
import jax.numpy as jnp
from jax import lax
from jax.sharding import PartitionSpec as P
from jax.experimental import pallas as pl
from jax.experimental.pallas import tpu as pltpu
import functools

INTERPRET = False

viscosity = 0.05
resistivity = 0.05
diffusivity = 0.05
buoyancy = 0.5
time_step = 0.25

HIGHEST = lax.Precision.HIGHEST


def stencil_kernel(f_ref, up_ref, down_ref, left_ref, right_ref, base_ref, lon_ref, lat_ref, turn_ref, o_ref, *rest, first):
    planes, height, width = f_ref.shape
    comps = planes // 2
    row = lax.broadcasted_iota(jnp.int32, (height, width), 0)
    col = lax.broadcasted_iota(jnp.int32, (height, width), 1)

    def terms(k):
        x = f_ref[k]
        up = up_ref[k]
        down = down_ref[k]
        left = left_ref[k]
        right = right_ref[k]
        lat_m1 = jnp.where(row == 0, up[1:2, :], pltpu.roll(x, 1, 0))
        lat_m2 = jnp.where(row == 0, up[0:1, :], jnp.where(row == 1, up[1:2, :], pltpu.roll(x, 2, 0)))
        lat_p1 = jnp.where(row == height - 1, down[0:1, :], pltpu.roll(x, height - 1, 0))
        lat_p2 = jnp.where(
            row == height - 1, down[1:2, :], jnp.where(row == height - 2, down[0:1, :], pltpu.roll(x, height - 2, 0))
        )
        lon_m1 = jnp.where(col == 0, left[:, 1:2], pltpu.roll(x, 1, 1))
        lon_m2 = jnp.where(col == 0, left[:, 0:1], jnp.where(col == 1, left[:, 1:2], pltpu.roll(x, 2, 1)))
        lon_p1 = jnp.where(col == width - 1, right[:, 0:1], pltpu.roll(x, width - 1, 1))
        lon_p2 = jnp.where(
            col == width - 1, right[:, 1:2], jnp.where(col == width - 2, right[:, 0:1], pltpu.roll(x, width - 2, 1))
        )
        d_lat = (8.0 * (lat_p1 - lat_m1) - (lat_p2 - lat_m2)) / 12.0
        d_lon = (8.0 * (lon_p1 - lon_m1) - (lon_p2 - lon_m2)) / 12.0
        lap = lat_p1 + lat_m1 + lon_p1 + lon_m1 - 4.0 * x
        return x, d_lat, d_lon, lap

    for level in range(2):
        def plane(c):
            return c * 2 + level

        def value(c):
            return f_ref[plane(c)]

        def lap_of(c, x, lap):
            above = f_ref[c * 2 + 1] if level == 0 else 0.0
            below = f_ref[c * 2] if level == 1 else 0.0
            return lap + above + below - 2.0 * x

        def store(c, x, rate):
            section = x + time_step * rate
            if first:
                o_ref[plane(c)] = section
            else:
                o_ref[plane(c)] = 0.5 * base_ref[plane(c)] + 0.5 * section

        u1, u2, u4, u5, u6 = value(1), value(2), value(4), value(5), value(6)
        for c in range(3):
            xa, lat_a, lon_a, lap_a = terms(plane(c))
            xb, lat_b, lon_b, lap_b = terms(plane(c + 3))
            adv_u_a = u1 * lat_a + u2 * lon_a
            adv_b_a = u4 * lat_a + u5 * lon_a
            adv_u_b = u1 * lat_b + u2 * lon_b
            adv_b_b = u4 * lat_b + u5 * lon_b
            rate_a = -adv_u_a + adv_b_b + viscosity * lap_of(c, xa, lap_a)
            if c == 0:
                rate_a = rate_a + buoyancy * u6
            rate_b = adv_b_a - adv_u_b + resistivity * lap_of(c + 3, xb, lap_b)
            store(c, xa, rate_a)
            store(c + 3, xb, rate_b)
        x6, lat_6, lon_6, lap_6 = terms(plane(6))
        adv_u_6 = u1 * lat_6 + u2 * lon_6
        store(6, x6, -adv_u_6 + diffusivity * lap_of(6, x6, lap_6))

    if first:
        donate_planes(lambda k: o_ref[k], planes, lon_ref[...], lat_ref[...], turn_ref, rest[0])


def advance(field, up, down, left, right, base, lon, lat, turn, first):
    shape = jax.ShapeDtypeStruct(field.shape, field.dtype)
    if first:
        shape = (shape, jax.ShapeDtypeStruct((field.shape[0], lon.shape[1]), jnp.float32))
    return pl.pallas_call(
        functools.partial(stencil_kernel, first=first),
        out_shape=shape,
        interpret=INTERPRET,
    )(field, up, down, left, right, base, lon, lat, turn)


def donation_weights(cells_ref, frac_ref, rows, cols):
    dons = cells_ref.shape[1]
    cell = cells_ref[...].astype(jnp.float32)
    row = jnp.floor((cell + 0.5) * (1.0 / (cols - 1)))
    col = cell - row * (cols - 1)
    row = row.astype(jnp.int32)
    col = col.astype(jnp.int32)
    frac_t = frac_ref[0:1, :]
    frac_p = frac_ref[1:2, :]
    col_ids = lax.broadcasted_iota(jnp.int32, (cols, dons), 0)
    row_ids = lax.broadcasted_iota(jnp.int32, (rows, dons), 0)
    weight_lon = jnp.where(col_ids == col, 1.0 - frac_p, 0.0) + jnp.where(col_ids == col + 1, frac_p, 0.0)
    weight_lat = jnp.where(row_ids == row, 1.0 - frac_t, 0.0) + jnp.where(row_ids == row + 1, frac_t, 0.0)
    return weight_lon, weight_lat


def donate_planes(plane_of, planes, weight_lon, weight_lat, turn_ref, out_ref):
    cosine = turn_ref[0:1, :]
    sine = turn_ref[1:2, :]
    values = []
    for k in range(planes):
        along = jnp.dot(plane_of(k), weight_lon, precision=HIGHEST, preferred_element_type=jnp.float32)
        values.append(jnp.sum(along * weight_lat, axis=0, keepdims=True))
    for k in range(planes):
        comp, level = divmod(k, 2)
        if comp in (1, 4):
            value = cosine * values[k] - sine * values[k + 2]
        elif comp in (2, 5):
            value = sine * values[k - 2] + cosine * values[k]
        else:
            value = values[k]
        out_ref[k : k + 1, :] = value


def donation_kernel(f_ref, cells_ref, frac_ref, turn_ref, out_ref, lon_ref, lat_ref):
    planes, rows, cols = f_ref.shape
    weight_lon, weight_lat = donation_weights(cells_ref, frac_ref, rows, cols)
    lon_ref[...] = weight_lon
    lat_ref[...] = weight_lat
    donate_planes(lambda k: f_ref[k], planes, weight_lon, weight_lat, turn_ref, out_ref)


def first_donation(field, cells, frac, turn):
    planes, rows, cols = field.shape
    dons = cells.shape[1]
    return pl.pallas_call(
        donation_kernel,
        out_shape=(
            jax.ShapeDtypeStruct((planes, dons), jnp.float32),
            jax.ShapeDtypeStruct((cols, dons), jnp.float32),
            jax.ShapeDtypeStruct((rows, dons), jnp.float32),
        ),
        interpret=INTERPRET,
    )(field, cells, frac, turn)


def rotate(values, turn):
    cosine = jnp.cos(turn)
    sine = jnp.sin(turn)
    parts = [
        values[0],
        cosine * values[1] - sine * values[2],
        sine * values[1] + cosine * values[2],
        values[3],
        cosine * values[4] - sine * values[5],
        sine * values[4] + cosine * values[5],
        values[6],
    ]
    return jnp.stack(parts)


def per_device(state, source_slot, donor_cell, donor_frac, donor_turn):
    comps = state.shape[1]
    levels = state.shape[2]
    rows = state.shape[3]
    cols = state.shape[4]
    cells = donor_cell[0, 0, 0]
    frac_t = donor_frac[0, 0, 0, 0]
    frac_p = donor_frac[0, 0, 0, 1]
    turn = donor_turn[0, 0, 0]
    slots = source_slot[0, 0, 0]
    lat_pos = lax.axis_index("lat")
    lon_pos = lax.axis_index("lon")
    lat_count = lax.axis_size("lat")
    lon_count = lax.axis_size("lon")
    on_top = lat_pos == 0
    on_bottom = lat_pos == lat_count - 1
    on_left = lon_pos == 0
    on_right = lon_pos == lon_count - 1

    band = 2 * cols
    side = 2 * rows
    lat_slots = jnp.where(on_top, slots[0:band], slots[band : 2 * band])
    lon_slots = jnp.where(on_left, slots[2 * band : 2 * band + side], slots[2 * band + side :])
    wanted = jnp.concatenate([lat_slots, lon_slots])
    total = lat_count * lon_count * cells.shape[0]
    pick = (jnp.arange(total, dtype=jnp.int32)[:, None] == wanted[None, :]).astype(jnp.float32)

    def gather(packet, axis):
        size = lax.axis_size(axis)
        pos = lax.axis_index(axis)
        held = packet[None]
        k = 1
        while k < size:
            other = lax.ppermute(held, axis, [(i, i ^ k) for i in range(size)])
            low = (pos // k) % 2 == 0
            held = jnp.where(low, jnp.concatenate([held, other]), jnp.concatenate([other, held]))
            k *= 2
        return held

    def section(field, donation):
        flat = field
        given = lax.ppermute(donation, "panel", [(0, 1), (1, 0)])
        dons = given.shape[1]
        side_cols = jnp.concatenate([flat[:, :, :2], flat[:, :, cols - 2 :]], axis=2)
        lon_packet = jnp.concatenate([given, side_cols.reshape(comps * levels, -1)], axis=1)
        lon_all = gather(lon_packet, "lon")
        row_given = jnp.transpose(lon_all[:, :, :dons], (1, 0, 2)).reshape(comps * levels, -1)
        side_cols = lon_all[:, :, dons:].reshape(lon_count, comps, levels, rows, 4)
        side_rows = jnp.concatenate([flat[:, :2, :], flat[:, rows - 2 :, :]], axis=1)
        lat_packet = jnp.concatenate([row_given, side_rows.reshape(comps * levels, -1)], axis=1)
        lat_all = gather(lat_packet, "lat")
        width = row_given.shape[1]
        partner = jnp.transpose(lat_all[:, :, :width], (1, 0, 2)).reshape(comps * levels, -1)
        side_rows = lat_all[:, :, width:].reshape(lat_count, comps, levels, 4, cols)
        up = lax.dynamic_index_in_dim(side_rows, jnp.maximum(lat_pos - 1, 0), keepdims=False)[:, :, 2:]
        down = lax.dynamic_index_in_dim(side_rows, jnp.minimum(lat_pos + 1, lat_count - 1), keepdims=False)[:, :, :2]
        left = lax.dynamic_index_in_dim(side_cols, jnp.maximum(lon_pos - 1, 0), keepdims=False)[..., 2:]
        right = lax.dynamic_index_in_dim(side_cols, jnp.minimum(lon_pos + 1, lon_count - 1), keepdims=False)[..., :2]
        rim = jnp.dot(partner, pick, precision=HIGHEST).reshape(comps, levels, -1)
        rim_lat = rim[:, :, :band].reshape(comps, levels, 2, cols)
        rim_lon = jnp.transpose(rim[:, :, band:].reshape(comps, levels, 2, rows), (0, 1, 3, 2))
        up = jnp.where(on_top, rim_lat, up).reshape(comps * levels, 2, cols)
        down = jnp.where(on_bottom, rim_lat, down).reshape(comps * levels, 2, cols)
        left = jnp.where(on_left, rim_lon, left).reshape(comps * levels, rows, 2)
        right = jnp.where(on_right, rim_lon, right).reshape(comps * levels, rows, 2)
        return up, down, left, right

    field = state[0].reshape(comps * levels, rows, cols)
    turn_parts = jnp.concatenate([jnp.cos(donor_turn[0, 0]), jnp.sin(donor_turn[0, 0])])
    donation, lon_w, lat_w = first_donation(field, donor_cell[0, 0], donor_frac[0, 0, 0], turn_parts)
    section_one, donation = advance(field, *section(field, donation), field, lon_w, lat_w, turn_parts, True)
    new_field = advance(section_one, *section(section_one, donation), field, lon_w, lat_w, turn_parts, False)
    return new_field.reshape(1, comps, levels, rows, cols)


def solution(mesh):
    in_specs = (
        P("panel", None, None, "lat", "lon"),
        P("panel", "lat", "lon", None),
        P("panel", "lat", "lon", None),
        P("panel", "lat", "lon", None, None),
        P("panel", "lat", "lon", None),
    )
    out_specs = P("panel", None, None, "lat", "lon")
    return jax.shard_map(
        per_device, mesh=mesh, in_specs=in_specs, out_specs=out_specs, check_vma=False
    )
```

```python
import jax
import jax.numpy as jnp
from jax import lax
from jax.sharding import PartitionSpec as P
from jax.experimental import pallas as pl
from jax.experimental.pallas import tpu as pltpu
import functools

INTERPRET = False

viscosity = 0.05
resistivity = 0.05
diffusivity = 0.05
buoyancy = 0.5
time_step = 0.25

HIGHEST = lax.Precision.HIGHEST


def stencil_kernel(f_ref, up_ref, down_ref, left_ref, right_ref, base_ref, lon_ref, lat_ref, turn_ref, o_ref, *rest, first):
    planes, height, width = f_ref.shape
    comps = planes // 2
    row = lax.broadcasted_iota(jnp.int32, (height, width), 0)
    col = lax.broadcasted_iota(jnp.int32, (height, width), 1)

    eye = jnp.where(
        lax.broadcasted_iota(jnp.int32, (height, height), 0) == lax.broadcasted_iota(jnp.int32, (height, height), 1),
        1.0,
        0.0,
    )
    pick_row = lax.broadcasted_iota(jnp.int32, (width, height), 0)

    def columns(k):
        left = left_ref[k]
        right = right_ref[k]
        rows_of = jnp.where(
            pick_row == 0,
            left[0:1, :],
            jnp.where(pick_row == 1, left[1:2, :], jnp.where(pick_row == 2, right[0:1, :], jnp.where(pick_row == 3, right[1:2, :], 0.0))),
        )
        return lax.dot_general(
            eye, rows_of, (((1,), (1,)), ((), ())), precision=HIGHEST, preferred_element_type=jnp.float32
        )

    def terms(k):
        x = f_ref[k]
        up = up_ref[k]
        down = down_ref[k]
        sides = columns(k)
        left = sides[:, 0:2]
        right = sides[:, 2:4]
        lat_m1 = jnp.where(row == 0, up[1:2, :], pltpu.roll(x, 1, 0))
        lat_m2 = jnp.where(row == 0, up[0:1, :], jnp.where(row == 1, up[1:2, :], pltpu.roll(x, 2, 0)))
        lat_p1 = jnp.where(row == height - 1, down[0:1, :], pltpu.roll(x, height - 1, 0))
        lat_p2 = jnp.where(
            row == height - 1, down[1:2, :], jnp.where(row == height - 2, down[0:1, :], pltpu.roll(x, height - 2, 0))
        )
        lon_m1 = jnp.where(col == 0, left[:, 1:2], pltpu.roll(x, 1, 1))
        lon_m2 = jnp.where(col == 0, left[:, 0:1], jnp.where(col == 1, left[:, 1:2], pltpu.roll(x, 2, 1)))
        lon_p1 = jnp.where(col == width - 1, right[:, 0:1], pltpu.roll(x, width - 1, 1))
        lon_p2 = jnp.where(
            col == width - 1, right[:, 1:2], jnp.where(col == width - 2, right[:, 0:1], pltpu.roll(x, width - 2, 1))
        )
        d_lat = (8.0 * (lat_p1 - lat_m1) - (lat_p2 - lat_m2)) / 12.0
        d_lon = (8.0 * (lon_p1 - lon_m1) - (lon_p2 - lon_m2)) / 12.0
        lap = lat_p1 + lat_m1 + lon_p1 + lon_m1 - 4.0 * x
        return x, d_lat, d_lon, lap

    for level in range(2):
        def plane(c):
            return c * 2 + level

        def value(c):
            return f_ref[plane(c)]

        def lap_of(c, x, lap):
            above = f_ref[c * 2 + 1] if level == 0 else 0.0
            below = f_ref[c * 2] if level == 1 else 0.0
            return lap + above + below - 2.0 * x

        def store(c, x, rate):
            section = x + time_step * rate
            if first:
                o_ref[plane(c)] = section
            else:
                o_ref[plane(c)] = 0.5 * base_ref[plane(c)] + 0.5 * section

        u1, u2, u4, u5, u6 = value(1), value(2), value(4), value(5), value(6)
        for c in range(3):
            xa, lat_a, lon_a, lap_a = terms(plane(c))
            xb, lat_b, lon_b, lap_b = terms(plane(c + 3))
            adv_u_a = u1 * lat_a + u2 * lon_a
            adv_b_a = u4 * lat_a + u5 * lon_a
            adv_u_b = u1 * lat_b + u2 * lon_b
            adv_b_b = u4 * lat_b + u5 * lon_b
            rate_a = -adv_u_a + adv_b_b + viscosity * lap_of(c, xa, lap_a)
            if c == 0:
                rate_a = rate_a + buoyancy * u6
            rate_b = adv_b_a - adv_u_b + resistivity * lap_of(c + 3, xb, lap_b)
            store(c, xa, rate_a)
            store(c + 3, xb, rate_b)
        x6, lat_6, lon_6, lap_6 = terms(plane(6))
        adv_u_6 = u1 * lat_6 + u2 * lon_6
        store(6, x6, -adv_u_6 + diffusivity * lap_of(6, x6, lap_6))

    if first:
        donate_planes(lambda k: o_ref[k], planes, lon_ref[...], lat_ref[...], turn_ref, rest[0])


def advance(field, up, down, left, right, base, lon, lat, turn, first):
    shape = jax.ShapeDtypeStruct(field.shape, field.dtype)
    if first:
        shape = (shape, jax.ShapeDtypeStruct((field.shape[0], lon.shape[1]), jnp.float32))
    return pl.pallas_call(
        functools.partial(stencil_kernel, first=first),
        out_shape=shape,
        interpret=INTERPRET,
    )(field, up, down, left, right, base, lon, lat, turn)


def donation_weights(cells_ref, frac_ref, rows, cols):
    dons = cells_ref.shape[1]
    cell = cells_ref[...].astype(jnp.float32)
    row = jnp.floor((cell + 0.5) * (1.0 / (cols - 1)))
    col = cell - row * (cols - 1)
    row = row.astype(jnp.int32)
    col = col.astype(jnp.int32)
    frac_t = frac_ref[0:1, :]
    frac_p = frac_ref[1:2, :]
    col_ids = lax.broadcasted_iota(jnp.int32, (cols, dons), 0)
    row_ids = lax.broadcasted_iota(jnp.int32, (rows, dons), 0)
    weight_lon = jnp.where(col_ids == col, 1.0 - frac_p, 0.0) + jnp.where(col_ids == col + 1, frac_p, 0.0)
    weight_lat = jnp.where(row_ids == row, 1.0 - frac_t, 0.0) + jnp.where(row_ids == row + 1, frac_t, 0.0)
    return weight_lon, weight_lat


def donate_planes(plane_of, planes, weight_lon, weight_lat, turn_ref, out_ref):
    cosine = turn_ref[0:1, :]
    sine = turn_ref[1:2, :]
    values = []
    for k in range(planes):
        along = jnp.dot(plane_of(k), weight_lon, precision=HIGHEST, preferred_element_type=jnp.float32)
        values.append(jnp.sum(along * weight_lat, axis=0, keepdims=True))
    for k in range(planes):
        comp, level = divmod(k, 2)
        if comp in (1, 4):
            value = cosine * values[k] - sine * values[k + 2]
        elif comp in (2, 5):
            value = sine * values[k - 2] + cosine * values[k]
        else:
            value = values[k]
        out_ref[k : k + 1, :] = value


def donation_kernel(f_ref, cells_ref, frac_ref, turn_ref, out_ref, lon_ref, lat_ref):
    planes, rows, cols = f_ref.shape
    weight_lon, weight_lat = donation_weights(cells_ref, frac_ref, rows, cols)
    lon_ref[...] = weight_lon
    lat_ref[...] = weight_lat
    donate_planes(lambda k: f_ref[k], planes, weight_lon, weight_lat, turn_ref, out_ref)


def first_donation(field, cells, frac, turn):
    planes, rows, cols = field.shape
    dons = cells.shape[1]
    return pl.pallas_call(
        donation_kernel,
        out_shape=(
            jax.ShapeDtypeStruct((planes, dons), jnp.float32),
            jax.ShapeDtypeStruct((cols, dons), jnp.float32),
            jax.ShapeDtypeStruct((rows, dons), jnp.float32),
        ),
        interpret=INTERPRET,
    )(field, cells, frac, turn)


def rotate(values, turn):
    cosine = jnp.cos(turn)
    sine = jnp.sin(turn)
    parts = [
        values[0],
        cosine * values[1] - sine * values[2],
        sine * values[1] + cosine * values[2],
        values[3],
        cosine * values[4] - sine * values[5],
        sine * values[4] + cosine * values[5],
        values[6],
    ]
    return jnp.stack(parts)


def per_device(state, source_slot, donor_cell, donor_frac, donor_turn):
    comps = state.shape[1]
    levels = state.shape[2]
    rows = state.shape[3]
    cols = state.shape[4]
    cells = donor_cell[0, 0, 0]
    frac_t = donor_frac[0, 0, 0, 0]
    frac_p = donor_frac[0, 0, 0, 1]
    turn = donor_turn[0, 0, 0]
    slots = source_slot[0, 0, 0]
    lat_pos = lax.axis_index("lat")
    lon_pos = lax.axis_index("lon")
    lat_count = lax.axis_size("lat")
    lon_count = lax.axis_size("lon")
    on_top = lat_pos == 0
    on_bottom = lat_pos == lat_count - 1
    on_left = lon_pos == 0
    on_right = lon_pos == lon_count - 1

    band = 2 * cols
    side = 2 * rows
    lat_slots = jnp.where(on_top, slots[0:band], slots[band : 2 * band])
    lon_slots = jnp.where(on_left, slots[2 * band : 2 * band + side], slots[2 * band + side :])
    wanted = jnp.concatenate([lat_slots, lon_slots])
    total = lat_count * lon_count * cells.shape[0]
    pick = (jnp.arange(total, dtype=jnp.int32)[:, None] == wanted[None, :]).astype(jnp.float32)

    def gather(packet, axis):
        size = lax.axis_size(axis)
        pos = lax.axis_index(axis)
        held = packet[None]
        k = 1
        while k < size:
            other = lax.ppermute(held, axis, [(i, i ^ k) for i in range(size)])
            low = (pos // k) % 2 == 0
            held = jnp.where(low, jnp.concatenate([held, other]), jnp.concatenate([other, held]))
            k *= 2
        return held

    def section(field, donation):
        flat = field
        given = lax.ppermute(donation, "panel", [(0, 1), (1, 0)])
        dons = given.shape[1]
        side_cols = jnp.concatenate([flat[:, :, :2], flat[:, :, cols - 2 :]], axis=2)
        lon_packet = jnp.concatenate([given, side_cols.reshape(comps * levels, -1)], axis=1)
        lon_all = gather(lon_packet, "lon")
        row_given = jnp.transpose(lon_all[:, :, :dons], (1, 0, 2)).reshape(comps * levels, -1)
        side_cols = lon_all[:, :, dons:].reshape(lon_count, comps, levels, rows, 4)
        side_rows = jnp.concatenate([flat[:, :2, :], flat[:, rows - 2 :, :]], axis=1)
        lat_packet = jnp.concatenate([row_given, side_rows.reshape(comps * levels, -1)], axis=1)
        lat_all = gather(lat_packet, "lat")
        width = row_given.shape[1]
        partner = jnp.transpose(lat_all[:, :, :width], (1, 0, 2)).reshape(comps * levels, -1)
        side_rows = lat_all[:, :, width:].reshape(lat_count, comps, levels, 4, cols)
        up = lax.dynamic_index_in_dim(side_rows, jnp.maximum(lat_pos - 1, 0), keepdims=False)[:, :, 2:]
        down = lax.dynamic_index_in_dim(side_rows, jnp.minimum(lat_pos + 1, lat_count - 1), keepdims=False)[:, :, :2]
        left = lax.dynamic_index_in_dim(side_cols, jnp.maximum(lon_pos - 1, 0), keepdims=False)[..., 2:]
        right = lax.dynamic_index_in_dim(side_cols, jnp.minimum(lon_pos + 1, lon_count - 1), keepdims=False)[..., :2]
        rim = jnp.dot(partner, pick, precision=HIGHEST).reshape(comps, levels, -1)
        rim_lat = rim[:, :, :band].reshape(comps, levels, 2, cols)
        rim_lon = jnp.transpose(rim[:, :, band:].reshape(comps, levels, 2, rows), (0, 1, 3, 2))
        up = jnp.where(on_top, rim_lat, up).reshape(comps * levels, 2, cols)
        down = jnp.where(on_bottom, rim_lat, down).reshape(comps * levels, 2, cols)
        left = jnp.swapaxes(jnp.where(on_left, rim_lon, left).reshape(comps * levels, rows, 2), 1, 2)
        right = jnp.swapaxes(jnp.where(on_right, rim_lon, right).reshape(comps * levels, rows, 2), 1, 2)
        return up, down, left, right

    field = state[0].reshape(comps * levels, rows, cols)
    turn_parts = jnp.concatenate([jnp.cos(donor_turn[0, 0]), jnp.sin(donor_turn[0, 0])])
    donation, lon_w, lat_w = first_donation(field, donor_cell[0, 0], donor_frac[0, 0, 0], turn_parts)
    section_one, donation = advance(field, *section(field, donation), field, lon_w, lat_w, turn_parts, True)
    new_field = advance(section_one, *section(section_one, donation), field, lon_w, lat_w, turn_parts, False)
    return new_field.reshape(1, comps, levels, rows, cols)


def solution(mesh):
    in_specs = (
        P("panel", None, None, "lat", "lon"),
        P("panel", "lat", "lon", None),
        P("panel", "lat", "lon", None),
        P("panel", "lat", "lon", None, None),
        P("panel", "lat", "lon", None),
    )
    out_specs = P("panel", None, None, "lat", "lon")
    return jax.shard_map(
        per_device, mesh=mesh, in_specs=in_specs, out_specs=out_specs, check_vma=False
    )
```

```python
import jax
import jax.numpy as jnp
from jax import lax
from jax.sharding import PartitionSpec as P
from jax.experimental import pallas as pl
from jax.experimental.pallas import tpu as pltpu
import functools

INTERPRET = False

viscosity = 0.05
resistivity = 0.05
diffusivity = 0.05
buoyancy = 0.5
time_step = 0.25

HIGHEST = lax.Precision.HIGHEST


def stencil_kernel(
    flags_ref, f_ref, rim_ref, up_ref, down_ref, left_ref, right_ref, base_ref, lon_ref, lat_ref, turn_ref, o_ref, *rest, first
):
    planes, height, width = f_ref.shape
    comps = planes // 2
    row = lax.broadcasted_iota(jnp.int32, (height, width), 0)
    col = lax.broadcasted_iota(jnp.int32, (height, width), 1)

    eye = jnp.where(
        lax.broadcasted_iota(jnp.int32, (height, height), 0) == lax.broadcasted_iota(jnp.int32, (height, height), 1),
        1.0,
        0.0,
    )
    pick_row = lax.broadcasted_iota(jnp.int32, (width, height), 0)

    on_top = flags_ref[0] == 1
    on_bottom = flags_ref[1] == 1
    on_left = flags_ref[2] == 1
    on_right = flags_ref[3] == 1
    band = 2 * width
    group = rim_ref.shape[1] - band

    def edge(flag, rim, halo):
        return jnp.where(jnp.broadcast_to(flag, halo.shape), rim, halo)

    def halo_rows(k):
        rim = jnp.concatenate([rim_ref[k : k + 1, 0:width], rim_ref[k : k + 1, width:band]], axis=0)
        return edge(on_top, rim, up_ref[k]), edge(on_bottom, rim, down_ref[k])

    def columns(k):
        start = band
        rim = jnp.concatenate(
            [rim_ref[k : k + 1, start : start + height], rim_ref[k : k + 1, start + group // 2 : start + group // 2 + height]],
            axis=0,
        )
        left = edge(on_left, rim, left_ref[k])
        right = edge(on_right, rim, right_ref[k])
        rows_of = jnp.where(
            pick_row == 0,
            left[0:1, :],
            jnp.where(pick_row == 1, left[1:2, :], jnp.where(pick_row == 2, right[0:1, :], jnp.where(pick_row == 3, right[1:2, :], 0.0))),
        )
        return lax.dot_general(
            eye, rows_of, (((1,), (1,)), ((), ())), precision=HIGHEST, preferred_element_type=jnp.float32
        )

    def terms(k):
        x = f_ref[k]
        up, down = halo_rows(k)
        sides = columns(k)
        left = sides[:, 0:2]
        right = sides[:, 2:4]
        lat_m1 = jnp.where(row == 0, up[1:2, :], pltpu.roll(x, 1, 0))
        lat_m2 = jnp.where(row == 0, up[0:1, :], jnp.where(row == 1, up[1:2, :], pltpu.roll(x, 2, 0)))
        lat_p1 = jnp.where(row == height - 1, down[0:1, :], pltpu.roll(x, height - 1, 0))
        lat_p2 = jnp.where(
            row == height - 1, down[1:2, :], jnp.where(row == height - 2, down[0:1, :], pltpu.roll(x, height - 2, 0))
        )
        lon_m1 = jnp.where(col == 0, left[:, 1:2], pltpu.roll(x, 1, 1))
        lon_m2 = jnp.where(col == 0, left[:, 0:1], jnp.where(col == 1, left[:, 1:2], pltpu.roll(x, 2, 1)))
        lon_p1 = jnp.where(col == width - 1, right[:, 0:1], pltpu.roll(x, width - 1, 1))
        lon_p2 = jnp.where(
            col == width - 1, right[:, 1:2], jnp.where(col == width - 2, right[:, 0:1], pltpu.roll(x, width - 2, 1))
        )
        d_lat = (8.0 * (lat_p1 - lat_m1) - (lat_p2 - lat_m2)) / 12.0
        d_lon = (8.0 * (lon_p1 - lon_m1) - (lon_p2 - lon_m2)) / 12.0
        lap = lat_p1 + lat_m1 + lon_p1 + lon_m1 - 4.0 * x
        return x, d_lat, d_lon, lap

    for level in range(2):
        def plane(c):
            return c * 2 + level

        def value(c):
            return f_ref[plane(c)]

        def lap_of(c, x, lap):
            above = f_ref[c * 2 + 1] if level == 0 else 0.0
            below = f_ref[c * 2] if level == 1 else 0.0
            return lap + above + below - 2.0 * x

        def store(c, x, rate):
            section = x + time_step * rate
            if first:
                o_ref[plane(c)] = section
            else:
                o_ref[plane(c)] = 0.5 * base_ref[plane(c)] + 0.5 * section

        u1, u2, u4, u5, u6 = value(1), value(2), value(4), value(5), value(6)
        for c in range(3):
            xa, lat_a, lon_a, lap_a = terms(plane(c))
            xb, lat_b, lon_b, lap_b = terms(plane(c + 3))
            adv_u_a = u1 * lat_a + u2 * lon_a
            adv_b_a = u4 * lat_a + u5 * lon_a
            adv_u_b = u1 * lat_b + u2 * lon_b
            adv_b_b = u4 * lat_b + u5 * lon_b
            rate_a = -adv_u_a + adv_b_b + viscosity * lap_of(c, xa, lap_a)
            if c == 0:
                rate_a = rate_a + buoyancy * u6
            rate_b = adv_b_a - adv_u_b + resistivity * lap_of(c + 3, xb, lap_b)
            store(c, xa, rate_a)
            store(c + 3, xb, rate_b)
        x6, lat_6, lon_6, lap_6 = terms(plane(6))
        adv_u_6 = u1 * lat_6 + u2 * lon_6
        store(6, x6, -adv_u_6 + diffusivity * lap_of(6, x6, lap_6))

    if first:
        donate_planes(lambda k: o_ref[k], planes, lon_ref[...], lat_ref[...], turn_ref, rest[0])


def advance(field, flags, rim, up, down, left, right, base, lon, lat, turn, first):
    shape = jax.ShapeDtypeStruct(field.shape, field.dtype)
    if first:
        shape = (shape, jax.ShapeDtypeStruct((field.shape[0], lon.shape[1]), jnp.float32))
    vmem = pl.BlockSpec(memory_space=pltpu.VMEM)
    return pl.pallas_call(
        functools.partial(stencil_kernel, first=first),
        out_shape=shape,
        in_specs=[pl.BlockSpec(memory_space=pltpu.SMEM)] + [vmem] * 10,
        out_specs=(vmem, vmem) if first else vmem,
        interpret=INTERPRET,
    )(flags, field, rim, up, down, left, right, base, lon, lat, turn)


def donation_weights(cells_ref, frac_ref, rows, cols):
    dons = cells_ref.shape[1]
    cell = cells_ref[...].astype(jnp.float32)
    row = jnp.floor((cell + 0.5) * (1.0 / (cols - 1)))
    col = cell - row * (cols - 1)
    row = row.astype(jnp.int32)
    col = col.astype(jnp.int32)
    frac_t = frac_ref[0:1, :]
    frac_p = frac_ref[1:2, :]
    col_ids = lax.broadcasted_iota(jnp.int32, (cols, dons), 0)
    row_ids = lax.broadcasted_iota(jnp.int32, (rows, dons), 0)
    weight_lon = jnp.where(col_ids == col, 1.0 - frac_p, 0.0) + jnp.where(col_ids == col + 1, frac_p, 0.0)
    weight_lat = jnp.where(row_ids == row, 1.0 - frac_t, 0.0) + jnp.where(row_ids == row + 1, frac_t, 0.0)
    return weight_lon, weight_lat


def donate_planes(plane_of, planes, weight_lon, weight_lat, turn_ref, out_ref):
    cosine = turn_ref[0:1, :]
    sine = turn_ref[1:2, :]
    values = []
    for k in range(planes):
        along = jnp.dot(plane_of(k), weight_lon, precision=HIGHEST, preferred_element_type=jnp.float32)
        values.append(jnp.sum(along * weight_lat, axis=0, keepdims=True))
    for k in range(planes):
        comp, level = divmod(k, 2)
        if comp in (1, 4):
            value = cosine * values[k] - sine * values[k + 2]
        elif comp in (2, 5):
            value = sine * values[k - 2] + cosine * values[k]
        else:
            value = values[k]
        out_ref[k : k + 1, :] = value


def donation_kernel(f_ref, cells_ref, frac_ref, turn_ref, out_ref, lon_ref, lat_ref):
    planes, rows, cols = f_ref.shape
    weight_lon, weight_lat = donation_weights(cells_ref, frac_ref, rows, cols)
    lon_ref[...] = weight_lon
    lat_ref[...] = weight_lat
    donate_planes(lambda k: f_ref[k], planes, weight_lon, weight_lat, turn_ref, out_ref)


def first_donation(field, cells, frac, turn):
    planes, rows, cols = field.shape
    dons = cells.shape[1]
    return pl.pallas_call(
        donation_kernel,
        out_shape=(
            jax.ShapeDtypeStruct((planes, dons), jnp.float32),
            jax.ShapeDtypeStruct((cols, dons), jnp.float32),
            jax.ShapeDtypeStruct((rows, dons), jnp.float32),
        ),
        interpret=INTERPRET,
    )(field, cells, frac, turn)


def rotate(values, turn):
    cosine = jnp.cos(turn)
    sine = jnp.sin(turn)
    parts = [
        values[0],
        cosine * values[1] - sine * values[2],
        sine * values[1] + cosine * values[2],
        values[3],
        cosine * values[4] - sine * values[5],
        sine * values[4] + cosine * values[5],
        values[6],
    ]
    return jnp.stack(parts)


def per_device(state, source_slot, donor_cell, donor_frac, donor_turn):
    comps = state.shape[1]
    levels = state.shape[2]
    rows = state.shape[3]
    cols = state.shape[4]
    cells = donor_cell[0, 0, 0]
    frac_t = donor_frac[0, 0, 0, 0]
    frac_p = donor_frac[0, 0, 0, 1]
    turn = donor_turn[0, 0, 0]
    slots = source_slot[0, 0, 0]
    lat_pos = lax.axis_index("lat")
    lon_pos = lax.axis_index("lon")
    lat_count = lax.axis_size("lat")
    lon_count = lax.axis_size("lon")
    on_top = lat_pos == 0
    on_bottom = lat_pos == lat_count - 1
    on_left = lon_pos == 0
    on_right = lon_pos == lon_count - 1

    band = 2 * cols
    side = 2 * rows
    lat_slots = jnp.where(on_top, slots[0:band], slots[band : 2 * band])
    lon_slots = jnp.where(on_left, slots[2 * band : 2 * band + side], slots[2 * band + side :])
    group = -(-rows // 128) * 128
    filler = jnp.zeros((group - rows,), jnp.int32)
    wanted = jnp.concatenate([lat_slots, lon_slots[:rows], filler, lon_slots[rows:], filler])
    flags = jnp.stack([on_top, on_bottom, on_left, on_right]).astype(jnp.int32)
    total = lat_count * lon_count * cells.shape[0]
    pick = (jnp.arange(total, dtype=jnp.int32)[:, None] == wanted[None, :]).astype(jnp.float32)

    def gather(packet, axis):
        size = lax.axis_size(axis)
        pos = lax.axis_index(axis)
        held = packet[None]
        k = 1
        while k < size:
            other = lax.ppermute(held, axis, [(i, i ^ k) for i in range(size)])
            low = (pos // k) % 2 == 0
            held = jnp.where(low, jnp.concatenate([held, other]), jnp.concatenate([other, held]))
            k *= 2
        return held

    def section(field, donation):
        flat = field
        given = lax.ppermute(donation, "panel", [(0, 1), (1, 0)])
        dons = given.shape[1]
        side_cols = jnp.concatenate([flat[:, :, :2], flat[:, :, cols - 2 :]], axis=2)
        lon_packet = jnp.concatenate([given, side_cols.reshape(comps * levels, -1)], axis=1)
        lon_all = gather(lon_packet, "lon")
        row_given = jnp.transpose(lon_all[:, :, :dons], (1, 0, 2)).reshape(comps * levels, -1)
        side_cols = lon_all[:, :, dons:].reshape(lon_count, comps, levels, rows, 4)
        side_rows = jnp.concatenate([flat[:, :2, :], flat[:, rows - 2 :, :]], axis=1)
        lat_packet = jnp.concatenate([row_given, side_rows.reshape(comps * levels, -1)], axis=1)
        lat_all = gather(lat_packet, "lat")
        width = row_given.shape[1]
        partner = jnp.transpose(lat_all[:, :, :width], (1, 0, 2)).reshape(comps * levels, -1)
        side_rows = lat_all[:, :, width:].reshape(lat_count, comps, levels, 4, cols)
        up = lax.dynamic_index_in_dim(side_rows, jnp.maximum(lat_pos - 1, 0), keepdims=False)[:, :, 2:]
        down = lax.dynamic_index_in_dim(side_rows, jnp.minimum(lat_pos + 1, lat_count - 1), keepdims=False)[:, :, :2]
        left = lax.dynamic_index_in_dim(side_cols, jnp.maximum(lon_pos - 1, 0), keepdims=False)[..., 2:]
        right = lax.dynamic_index_in_dim(side_cols, jnp.minimum(lon_pos + 1, lon_count - 1), keepdims=False)[..., :2]
        rim = jnp.dot(partner, pick, precision=HIGHEST)
        up = up.reshape(comps * levels, 2, cols)
        down = down.reshape(comps * levels, 2, cols)
        left = jnp.swapaxes(left.reshape(comps * levels, rows, 2), 1, 2)
        right = jnp.swapaxes(right.reshape(comps * levels, rows, 2), 1, 2)
        return flags, rim, up, down, left, right

    field = state[0].reshape(comps * levels, rows, cols)
    turn_parts = jnp.concatenate([jnp.cos(donor_turn[0, 0]), jnp.sin(donor_turn[0, 0])])
    donation, lon_w, lat_w = first_donation(field, donor_cell[0, 0], donor_frac[0, 0, 0], turn_parts)
    section_one, donation = advance(field, *section(field, donation), field, lon_w, lat_w, turn_parts, True)
    new_field = advance(section_one, *section(section_one, donation), field, lon_w, lat_w, turn_parts, False)
    return new_field.reshape(1, comps, levels, rows, cols)


def solution(mesh):
    in_specs = (
        P("panel", None, None, "lat", "lon"),
        P("panel", "lat", "lon", None),
        P("panel", "lat", "lon", None),
        P("panel", "lat", "lon", None, None),
        P("panel", "lat", "lon", None),
    )
    out_specs = P("panel", None, None, "lat", "lon")
    return jax.shard_map(
        per_device, mesh=mesh, in_specs=in_specs, out_specs=out_specs, check_vma=False
    )
```

```python
import jax
import jax.numpy as jnp
from jax import lax
from jax.sharding import PartitionSpec as P
from jax.experimental import pallas as pl
from jax.experimental.pallas import tpu as pltpu
import functools

INTERPRET = False

viscosity = 0.05
resistivity = 0.05
diffusivity = 0.05
buoyancy = 0.5
time_step = 0.25

HIGHEST = lax.Precision.HIGHEST


def stencil_kernel(f_ref, up_ref, down_ref, left_ref, right_ref, base_ref, lon_ref, lat_ref, turn_ref, o_ref, *rest, first):
    planes, height, width = f_ref.shape
    comps = planes // 2
    row = lax.broadcasted_iota(jnp.int32, (height, width), 0)
    col = lax.broadcasted_iota(jnp.int32, (height, width), 1)

    eye = jnp.where(
        lax.broadcasted_iota(jnp.int32, (height, height), 0) == lax.broadcasted_iota(jnp.int32, (height, height), 1),
        1.0,
        0.0,
    )
    pick_row = lax.broadcasted_iota(jnp.int32, (width, height), 0)

    def columns(k):
        left = left_ref[k]
        right = right_ref[k]
        rows_of = jnp.where(
            pick_row == 0,
            left[0:1, :],
            jnp.where(pick_row == 1, left[1:2, :], jnp.where(pick_row == 2, right[0:1, :], jnp.where(pick_row == 3, right[1:2, :], 0.0))),
        )
        return lax.dot_general(
            eye, rows_of, (((1,), (1,)), ((), ())), precision=HIGHEST, preferred_element_type=jnp.float32
        )

    def terms(k):
        x = f_ref[k]
        up = up_ref[k]
        down = down_ref[k]
        sides = columns(k)
        left = sides[:, 0:2]
        right = sides[:, 2:4]
        lat_m1 = jnp.where(row == 0, up[1:2, :], pltpu.roll(x, 1, 0))
        lat_m2 = jnp.where(row == 0, up[0:1, :], jnp.where(row == 1, up[1:2, :], pltpu.roll(x, 2, 0)))
        lat_p1 = jnp.where(row == height - 1, down[0:1, :], pltpu.roll(x, height - 1, 0))
        lat_p2 = jnp.where(
            row == height - 1, down[1:2, :], jnp.where(row == height - 2, down[0:1, :], pltpu.roll(x, height - 2, 0))
        )
        lon_m1 = jnp.where(col == 0, left[:, 1:2], pltpu.roll(x, 1, 1))
        lon_m2 = jnp.where(col == 0, left[:, 0:1], jnp.where(col == 1, left[:, 1:2], pltpu.roll(x, 2, 1)))
        lon_p1 = jnp.where(col == width - 1, right[:, 0:1], pltpu.roll(x, width - 1, 1))
        lon_p2 = jnp.where(
            col == width - 1, right[:, 1:2], jnp.where(col == width - 2, right[:, 0:1], pltpu.roll(x, width - 2, 1))
        )
        d_lat = (8.0 * (lat_p1 - lat_m1) - (lat_p2 - lat_m2)) / 12.0
        d_lon = (8.0 * (lon_p1 - lon_m1) - (lon_p2 - lon_m2)) / 12.0
        lap = lat_p1 + lat_m1 + lon_p1 + lon_m1 - 4.0 * x
        return x, d_lat, d_lon, lap

    for level in range(2):
        def plane(c):
            return c * 2 + level

        def value(c):
            return f_ref[plane(c)]

        def lap_of(c, x, lap):
            above = f_ref[c * 2 + 1] if level == 0 else 0.0
            below = f_ref[c * 2] if level == 1 else 0.0
            return lap + above + below - 2.0 * x

        def store(c, x, rate):
            section = x + time_step * rate
            if first:
                o_ref[plane(c)] = section
            else:
                o_ref[plane(c)] = 0.5 * base_ref[plane(c)] + 0.5 * section

        u1, u2, u4, u5, u6 = value(1), value(2), value(4), value(5), value(6)
        for c in range(3):
            xa, lat_a, lon_a, lap_a = terms(plane(c))
            xb, lat_b, lon_b, lap_b = terms(plane(c + 3))
            adv_u_a = u1 * lat_a + u2 * lon_a
            adv_b_a = u4 * lat_a + u5 * lon_a
            adv_u_b = u1 * lat_b + u2 * lon_b
            adv_b_b = u4 * lat_b + u5 * lon_b
            rate_a = -adv_u_a + adv_b_b + viscosity * lap_of(c, xa, lap_a)
            if c == 0:
                rate_a = rate_a + buoyancy * u6
            rate_b = adv_b_a - adv_u_b + resistivity * lap_of(c + 3, xb, lap_b)
            store(c, xa, rate_a)
            store(c + 3, xb, rate_b)
        x6, lat_6, lon_6, lap_6 = terms(plane(6))
        adv_u_6 = u1 * lat_6 + u2 * lon_6
        store(6, x6, -adv_u_6 + diffusivity * lap_of(6, x6, lap_6))

    if first:
        donate_planes(lambda k: o_ref[k], planes, lon_ref[...], lat_ref[...], turn_ref, rest[0])


def advance(field, up, down, left, right, base, lon, lat, turn, first):
    shape = jax.ShapeDtypeStruct(field.shape, field.dtype)
    if first:
        shape = (shape, jax.ShapeDtypeStruct((field.shape[0], lon.shape[1]), jnp.float32))
    return pl.pallas_call(
        functools.partial(stencil_kernel, first=first),
        out_shape=shape,
        interpret=INTERPRET,
    )(field, up, down, left, right, base, lon, lat, turn)


def donation_weights(cells_ref, frac_ref, rows, cols):
    dons = cells_ref.shape[1]
    cell = cells_ref[...].astype(jnp.float32)
    row = jnp.floor((cell + 0.5) * (1.0 / (cols - 1)))
    col = cell - row * (cols - 1)
    row = row.astype(jnp.int32)
    col = col.astype(jnp.int32)
    frac_t = frac_ref[0:1, :]
    frac_p = frac_ref[1:2, :]
    col_ids = lax.broadcasted_iota(jnp.int32, (cols, dons), 0)
    row_ids = lax.broadcasted_iota(jnp.int32, (rows, dons), 0)
    weight_lon = jnp.where(col_ids == col, 1.0 - frac_p, 0.0) + jnp.where(col_ids == col + 1, frac_p, 0.0)
    weight_lat = jnp.where(row_ids == row, 1.0 - frac_t, 0.0) + jnp.where(row_ids == row + 1, frac_t, 0.0)
    return weight_lon, weight_lat


def donate_planes(plane_of, planes, weight_lon, weight_lat, turn_ref, out_ref):
    cosine = turn_ref[0:1, :]
    sine = turn_ref[1:2, :]
    values = []
    for k in range(planes):
        along = jnp.dot(plane_of(k), weight_lon, precision=HIGHEST, preferred_element_type=jnp.float32)
        values.append(jnp.sum(along * weight_lat, axis=0, keepdims=True))
    for k in range(planes):
        comp, level = divmod(k, 2)
        if comp in (1, 4):
            value = cosine * values[k] - sine * values[k + 2]
        elif comp in (2, 5):
            value = sine * values[k - 2] + cosine * values[k]
        else:
            value = values[k]
        out_ref[k : k + 1, :] = value


def donation_kernel(f_ref, cells_ref, frac_ref, turn_ref, out_ref, lon_ref, lat_ref):
    planes, rows, cols = f_ref.shape
    weight_lon, weight_lat = donation_weights(cells_ref, frac_ref, rows, cols)
    lon_ref[...] = weight_lon
    lat_ref[...] = weight_lat
    donate_planes(lambda k: f_ref[k], planes, weight_lon, weight_lat, turn_ref, out_ref)


def first_donation(field, cells, frac, turn):
    planes, rows, cols = field.shape
    dons = cells.shape[1]
    return pl.pallas_call(
        donation_kernel,
        out_shape=(
            jax.ShapeDtypeStruct((planes, dons), jnp.float32),
            jax.ShapeDtypeStruct((cols, dons), jnp.float32),
            jax.ShapeDtypeStruct((rows, dons), jnp.float32),
        ),
        interpret=INTERPRET,
    )(field, cells, frac, turn)


def rotate(values, turn):
    cosine = jnp.cos(turn)
    sine = jnp.sin(turn)
    parts = [
        values[0],
        cosine * values[1] - sine * values[2],
        sine * values[1] + cosine * values[2],
        values[3],
        cosine * values[4] - sine * values[5],
        sine * values[4] + cosine * values[5],
        values[6],
    ]
    return jnp.stack(parts)


def per_device(state, source_slot, donor_cell, donor_frac, donor_turn):
    comps = state.shape[1]
    levels = state.shape[2]
    rows = state.shape[3]
    cols = state.shape[4]
    cells = donor_cell[0, 0, 0]
    frac_t = donor_frac[0, 0, 0, 0]
    frac_p = donor_frac[0, 0, 0, 1]
    turn = donor_turn[0, 0, 0]
    slots = source_slot[0, 0, 0]
    lat_pos = lax.axis_index("lat")
    lon_pos = lax.axis_index("lon")
    lat_count = lax.axis_size("lat")
    lon_count = lax.axis_size("lon")
    on_top = lat_pos == 0
    on_bottom = lat_pos == lat_count - 1
    on_left = lon_pos == 0
    on_right = lon_pos == lon_count - 1

    band = 2 * cols
    side = 2 * rows
    lat_slots = jnp.where(on_top, slots[0:band], slots[band : 2 * band])
    lon_slots = jnp.where(on_left, slots[2 * band : 2 * band + side], slots[2 * band + side :])
    wanted = jnp.concatenate([lat_slots, lon_slots])
    total = lat_count * lon_count * cells.shape[0]
    pick = (jnp.arange(total, dtype=jnp.int32)[:, None] == wanted[None, :]).astype(jnp.float32)

    def gather(packet, axis):
        size = lax.axis_size(axis)
        pos = lax.axis_index(axis)
        held = packet[None]
        k = 1
        while k < size:
            other = lax.ppermute(held, axis, [(i, i ^ k) for i in range(size)])
            low = (pos // k) % 2 == 0
            held = jnp.where(low, jnp.concatenate([held, other]), jnp.concatenate([other, held]))
            k *= 2
        return held

    def section(field, donation):
        flat = field
        given = lax.ppermute(donation, "panel", [(0, 1), (1, 0)])
        dons = given.shape[1]
        side_rows = jnp.concatenate([flat[:, :2, :], flat[:, rows - 2 :, :]], axis=1)
        lat_packet = jnp.concatenate([given, side_rows.reshape(comps * levels, -1)], axis=1)
        lat_all = gather(lat_packet, "lat")
        col_given = jnp.transpose(lat_all[:, :, :dons], (1, 0, 2)).reshape(comps * levels, -1)
        side_rows = lat_all[:, :, dons:].reshape(lat_count, comps, levels, 4, cols)
        side_cols = jnp.concatenate([flat[:, :, :2], flat[:, :, cols - 2 :]], axis=2)
        lon_packet = jnp.concatenate([col_given, side_cols.reshape(comps * levels, -1)], axis=1)
        lon_all = gather(lon_packet, "lon")
        width = col_given.shape[1]
        partner = lon_all[:, :, :width].reshape(lon_count, comps * levels, lat_count, dons)
        partner = jnp.transpose(partner, (1, 2, 0, 3)).reshape(comps * levels, -1)
        side_cols = lon_all[:, :, width:].reshape(lon_count, comps, levels, rows, 4)
        up = lax.dynamic_index_in_dim(side_rows, jnp.maximum(lat_pos - 1, 0), keepdims=False)[:, :, 2:]
        down = lax.dynamic_index_in_dim(side_rows, jnp.minimum(lat_pos + 1, lat_count - 1), keepdims=False)[:, :, :2]
        left = lax.dynamic_index_in_dim(side_cols, jnp.maximum(lon_pos - 1, 0), keepdims=False)[..., 2:]
        right = lax.dynamic_index_in_dim(side_cols, jnp.minimum(lon_pos + 1, lon_count - 1), keepdims=False)[..., :2]
        rim = jnp.dot(partner, pick, precision=HIGHEST).reshape(comps, levels, -1)
        rim_lat = rim[:, :, :band].reshape(comps, levels, 2, cols)
        rim_lon = jnp.transpose(rim[:, :, band:].reshape(comps, levels, 2, rows), (0, 1, 3, 2))
        up = jnp.where(on_top, rim_lat, up).reshape(comps * levels, 2, cols)
        down = jnp.where(on_bottom, rim_lat, down).reshape(comps * levels, 2, cols)
        left = jnp.swapaxes(jnp.where(on_left, rim_lon, left).reshape(comps * levels, rows, 2), 1, 2)
        right = jnp.swapaxes(jnp.where(on_right, rim_lon, right).reshape(comps * levels, rows, 2), 1, 2)
        return up, down, left, right

    field = state[0].reshape(comps * levels, rows, cols)
    turn_parts = jnp.concatenate([jnp.cos(donor_turn[0, 0]), jnp.sin(donor_turn[0, 0])])
    donation, lon_w, lat_w = first_donation(field, donor_cell[0, 0], donor_frac[0, 0, 0], turn_parts)
    section_one, donation = advance(field, *section(field, donation), field, lon_w, lat_w, turn_parts, True)
    new_field = advance(section_one, *section(section_one, donation), field, lon_w, lat_w, turn_parts, False)
    return new_field.reshape(1, comps, levels, rows, cols)


def solution(mesh):
    in_specs = (
        P("panel", None, None, "lat", "lon"),
        P("panel", "lat", "lon", None),
        P("panel", "lat", "lon", None),
        P("panel", "lat", "lon", None, None),
        P("panel", "lat", "lon", None),
    )
    out_specs = P("panel", None, None, "lat", "lon")
    return jax.shard_map(
        per_device, mesh=mesh, in_specs=in_specs, out_specs=out_specs, check_vma=False
    )
```

```python
import jax
import jax.numpy as jnp
from jax import lax
from jax.sharding import PartitionSpec as P
from jax.experimental import pallas as pl
from jax.experimental.pallas import tpu as pltpu
import functools

INTERPRET = False

viscosity = 0.05
resistivity = 0.05
diffusivity = 0.05
buoyancy = 0.5
time_step = 0.25

HIGHEST = lax.Precision.HIGHEST


def stencil_kernel(f_ref, up_ref, down_ref, left_ref, right_ref, base_ref, lon_ref, lat_ref, turn_ref, o_ref, *rest, first):
    planes, height, width = f_ref.shape
    comps = planes // 2
    row = lax.broadcasted_iota(jnp.int32, (height, width), 0)
    col = lax.broadcasted_iota(jnp.int32, (height, width), 1)

    eye = jnp.where(
        lax.broadcasted_iota(jnp.int32, (height, height), 0) == lax.broadcasted_iota(jnp.int32, (height, height), 1),
        1.0,
        0.0,
    )
    pick_row = lax.broadcasted_iota(jnp.int32, (width, height), 0)

    def columns(k):
        left = left_ref[k]
        right = right_ref[k]
        rows_of = jnp.where(
            pick_row == 0,
            left[0:1, :],
            jnp.where(pick_row == 1, left[1:2, :], jnp.where(pick_row == 2, right[0:1, :], jnp.where(pick_row == 3, right[1:2, :], 0.0))),
        )
        return lax.dot_general(
            eye, rows_of, (((1,), (1,)), ((), ())), precision=HIGHEST, preferred_element_type=jnp.float32
        )

    def terms(k):
        x = f_ref[k]
        up = up_ref[k]
        down = down_ref[k]
        sides = columns(k)
        left = sides[:, 0:2]
        right = sides[:, 2:4]
        lat_m1 = jnp.where(row == 0, up[1:2, :], pltpu.roll(x, 1, 0))
        lat_m2 = jnp.where(row == 0, up[0:1, :], jnp.where(row == 1, up[1:2, :], pltpu.roll(x, 2, 0)))
        lat_p1 = jnp.where(row == height - 1, down[0:1, :], pltpu.roll(x, height - 1, 0))
        lat_p2 = jnp.where(
            row == height - 1, down[1:2, :], jnp.where(row == height - 2, down[0:1, :], pltpu.roll(x, height - 2, 0))
        )
        lon_m1 = jnp.where(col == 0, left[:, 1:2], pltpu.roll(x, 1, 1))
        lon_m2 = jnp.where(col == 0, left[:, 0:1], jnp.where(col == 1, left[:, 1:2], pltpu.roll(x, 2, 1)))
        lon_p1 = jnp.where(col == width - 1, right[:, 0:1], pltpu.roll(x, width - 1, 1))
        lon_p2 = jnp.where(
            col == width - 1, right[:, 1:2], jnp.where(col == width - 2, right[:, 0:1], pltpu.roll(x, width - 2, 1))
        )
        d_lat = (8.0 * (lat_p1 - lat_m1) - (lat_p2 - lat_m2)) / 12.0
        d_lon = (8.0 * (lon_p1 - lon_m1) - (lon_p2 - lon_m2)) / 12.0
        lap = lat_p1 + lat_m1 + lon_p1 + lon_m1 - 4.0 * x
        return x, d_lat, d_lon, lap

    for level in range(2):
        def plane(c):
            return c * 2 + level

        def value(c):
            return f_ref[plane(c)]

        def lap_of(c, x, lap):
            above = f_ref[c * 2 + 1] if level == 0 else 0.0
            below = f_ref[c * 2] if level == 1 else 0.0
            return lap + above + below - 2.0 * x

        def store(c, x, rate):
            section = x + time_step * rate
            if first:
                o_ref[plane(c)] = section
            else:
                o_ref[plane(c)] = 0.5 * base_ref[plane(c)] + 0.5 * section

        u1, u2, u4, u5, u6 = value(1), value(2), value(4), value(5), value(6)
        for c in range(3):
            xa, lat_a, lon_a, lap_a = terms(plane(c))
            xb, lat_b, lon_b, lap_b = terms(plane(c + 3))
            adv_u_a = u1 * lat_a + u2 * lon_a
            adv_b_a = u4 * lat_a + u5 * lon_a
            adv_u_b = u1 * lat_b + u2 * lon_b
            adv_b_b = u4 * lat_b + u5 * lon_b
            rate_a = -adv_u_a + adv_b_b + viscosity * lap_of(c, xa, lap_a)
            if c == 0:
                rate_a = rate_a + buoyancy * u6
            rate_b = adv_b_a - adv_u_b + resistivity * lap_of(c + 3, xb, lap_b)
            store(c, xa, rate_a)
            store(c + 3, xb, rate_b)
        x6, lat_6, lon_6, lap_6 = terms(plane(6))
        adv_u_6 = u1 * lat_6 + u2 * lon_6
        store(6, x6, -adv_u_6 + diffusivity * lap_of(6, x6, lap_6))

    if first:
        donate_planes(lambda k: o_ref[k], planes, lon_ref[...], lat_ref[...], turn_ref, rest[0])


def advance(field, up, down, left, right, base, lon, lat, turn, first):
    shape = jax.ShapeDtypeStruct(field.shape, field.dtype)
    if first:
        shape = (shape, jax.ShapeDtypeStruct((field.shape[0], lon.shape[1]), jnp.float32))
    return pl.pallas_call(
        functools.partial(stencil_kernel, first=first),
        out_shape=shape,
        interpret=INTERPRET,
    )(field, up, down, left, right, base, lon, lat, turn)


def donation_weights(cells_ref, frac_ref, rows, cols):
    dons = cells_ref.shape[1]
    cell = cells_ref[...].astype(jnp.float32)
    row = jnp.floor((cell + 0.5) * (1.0 / (cols - 1)))
    col = cell - row * (cols - 1)
    row = row.astype(jnp.int32)
    col = col.astype(jnp.int32)
    frac_t = frac_ref[0:1, :]
    frac_p = frac_ref[1:2, :]
    col_ids = lax.broadcasted_iota(jnp.int32, (cols, dons), 0)
    row_ids = lax.broadcasted_iota(jnp.int32, (rows, dons), 0)
    weight_lon = jnp.where(col_ids == col, 1.0 - frac_p, 0.0) + jnp.where(col_ids == col + 1, frac_p, 0.0)
    weight_lat = jnp.where(row_ids == row, 1.0 - frac_t, 0.0) + jnp.where(row_ids == row + 1, frac_t, 0.0)
    return weight_lon, weight_lat


def donate_planes(plane_of, planes, weight_lon, weight_lat, turn_ref, out_ref):
    cosine = turn_ref[0:1, :]
    sine = turn_ref[1:2, :]
    values = []
    for k in range(planes):
        along = jnp.dot(plane_of(k), weight_lon, precision=HIGHEST, preferred_element_type=jnp.float32)
        values.append(jnp.sum(along * weight_lat, axis=0, keepdims=True))
    for k in range(planes):
        comp, level = divmod(k, 2)
        if comp in (1, 4):
            value = cosine * values[k] - sine * values[k + 2]
        elif comp in (2, 5):
            value = sine * values[k - 2] + cosine * values[k]
        else:
            value = values[k]
        out_ref[k : k + 1, :] = value


def donation_kernel(f_ref, cells_ref, frac_ref, turn_ref, out_ref, lon_ref, lat_ref):
    planes, rows, cols = f_ref.shape
    weight_lon, weight_lat = donation_weights(cells_ref, frac_ref, rows, cols)
    lon_ref[...] = weight_lon
    lat_ref[...] = weight_lat
    donate_planes(lambda k: f_ref[k], planes, weight_lon, weight_lat, turn_ref, out_ref)


def first_donation(field, cells, frac, turn):
    planes, rows, cols = field.shape
    dons = cells.shape[1]
    return pl.pallas_call(
        donation_kernel,
        out_shape=(
            jax.ShapeDtypeStruct((planes, dons), jnp.float32),
            jax.ShapeDtypeStruct((cols, dons), jnp.float32),
            jax.ShapeDtypeStruct((rows, dons), jnp.float32),
        ),
        interpret=INTERPRET,
    )(field, cells, frac, turn)


def rotate(values, turn):
    cosine = jnp.cos(turn)
    sine = jnp.sin(turn)
    parts = [
        values[0],
        cosine * values[1] - sine * values[2],
        sine * values[1] + cosine * values[2],
        values[3],
        cosine * values[4] - sine * values[5],
        sine * values[4] + cosine * values[5],
        values[6],
    ]
    return jnp.stack(parts)


def per_device(state, source_slot, donor_cell, donor_frac, donor_turn):
    comps = state.shape[1]
    levels = state.shape[2]
    rows = state.shape[3]
    cols = state.shape[4]
    cells = donor_cell[0, 0, 0]
    frac_t = donor_frac[0, 0, 0, 0]
    frac_p = donor_frac[0, 0, 0, 1]
    turn = donor_turn[0, 0, 0]
    slots = source_slot[0, 0, 0]
    lat_pos = lax.axis_index("lat")
    lon_pos = lax.axis_index("lon")
    lat_count = lax.axis_size("lat")
    lon_count = lax.axis_size("lon")
    on_top = lat_pos == 0
    on_bottom = lat_pos == lat_count - 1
    on_left = lon_pos == 0
    on_right = lon_pos == lon_count - 1

    band = 2 * cols
    side = 2 * rows
    lat_slots = jnp.where(on_top, slots[0:band], slots[band : 2 * band])
    lon_slots = jnp.where(on_left, slots[2 * band : 2 * band + side], slots[2 * band + side :])
    wanted = jnp.concatenate([lat_slots, lon_slots])
    total = lat_count * lon_count * cells.shape[0]
    pick = (jnp.arange(total, dtype=jnp.int32)[:, None] == wanted[None, :]).astype(jnp.float32)

    def gather(packet, axis):
        size = lax.axis_size(axis)
        pos = lax.axis_index(axis)
        held = packet[None]
        k = 1
        while k < size:
            other = lax.ppermute(held, axis, [(i, i ^ k) for i in range(size)])
            low = (pos // k) % 2 == 0
            held = jnp.where(low, jnp.concatenate([held, other]), jnp.concatenate([other, held]))
            k *= 2
        return held

    def section(field, donation):
        flat = field
        given = lax.ppermute(donation, "panel", [(0, 1), (1, 0)])
        dons = given.shape[1]
        side_rows = jnp.concatenate([flat[:, :2, :], flat[:, rows - 2 :, :]], axis=1)
        lat_packet = jnp.concatenate([given, side_rows.reshape(comps * levels, -1)], axis=1)
        lat_all = gather(lat_packet, "lat")
        col_given = jnp.transpose(lat_all[:, :, :dons], (1, 0, 2)).reshape(comps * levels, -1)
        side_rows = lat_all[:, :, dons:].reshape(lat_count, comps, levels, 4, cols)
        side_cols = jnp.concatenate([flat[:, :, :2], flat[:, :, cols - 2 :]], axis=2)
        side_cols = jnp.swapaxes(side_cols, 1, 2)
        lon_packet = jnp.concatenate([col_given, side_cols.reshape(comps * levels, -1)], axis=1)
        lon_all = gather(lon_packet, "lon")
        width = col_given.shape[1]
        partner = lon_all[:, :, :width].reshape(lon_count, comps * levels, lat_count, dons)
        partner = jnp.transpose(partner, (1, 2, 0, 3)).reshape(comps * levels, -1)
        side_cols = lon_all[:, :, width:].reshape(lon_count, comps, levels, 4, rows)
        up = lax.dynamic_index_in_dim(side_rows, jnp.maximum(lat_pos - 1, 0), keepdims=False)[:, :, 2:]
        down = lax.dynamic_index_in_dim(side_rows, jnp.minimum(lat_pos + 1, lat_count - 1), keepdims=False)[:, :, :2]
        left = lax.dynamic_index_in_dim(side_cols, jnp.maximum(lon_pos - 1, 0), keepdims=False)[:, :, 2:]
        right = lax.dynamic_index_in_dim(side_cols, jnp.minimum(lon_pos + 1, lon_count - 1), keepdims=False)[:, :, :2]
        rim = jnp.dot(partner, pick, precision=HIGHEST).reshape(comps, levels, -1)
        rim_lat = rim[:, :, :band].reshape(comps, levels, 2, cols)
        rim_lon = rim[:, :, band:].reshape(comps, levels, 2, rows)
        up = jnp.where(on_top, rim_lat, up).reshape(comps * levels, 2, cols)
        down = jnp.where(on_bottom, rim_lat, down).reshape(comps * levels, 2, cols)
        left = jnp.where(on_left, rim_lon, left).reshape(comps * levels, 2, rows)
        right = jnp.where(on_right, rim_lon, right).reshape(comps * levels, 2, rows)
        return up, down, left, right

    field = state[0].reshape(comps * levels, rows, cols)
    turn_parts = jnp.concatenate([jnp.cos(donor_turn[0, 0]), jnp.sin(donor_turn[0, 0])])
    donation, lon_w, lat_w = first_donation(field, donor_cell[0, 0], donor_frac[0, 0, 0], turn_parts)
    section_one, donation = advance(field, *section(field, donation), field, lon_w, lat_w, turn_parts, True)
    new_field = advance(section_one, *section(section_one, donation), field, lon_w, lat_w, turn_parts, False)
    return new_field.reshape(1, comps, levels, rows, cols)


def solution(mesh):
    in_specs = (
        P("panel", None, None, "lat", "lon"),
        P("panel", "lat", "lon", None),
        P("panel", "lat", "lon", None),
        P("panel", "lat", "lon", None, None),
        P("panel", "lat", "lon", None),
    )
    out_specs = P("panel", None, None, "lat", "lon")
    return jax.shard_map(
        per_device, mesh=mesh, in_specs=in_specs, out_specs=out_specs, check_vma=False
    )
```

```python
import jax
import jax.numpy as jnp
from jax import lax
from jax.sharding import PartitionSpec as P
from jax.experimental import pallas as pl
from jax.experimental.pallas import tpu as pltpu
import functools

INTERPRET = False

viscosity = 0.05
resistivity = 0.05
diffusivity = 0.05
buoyancy = 0.5
time_step = 0.25

HIGHEST = lax.Precision.HIGHEST


def stencil_kernel(*refs, first):
    if first:
        f_ref, other_ref, up_ref, down_ref, left_ref, right_ref, lon_ref, lat_ref, turn_ref, o_ref, don_ref = refs
    else:
        f_ref, other_ref, up_ref, down_ref, left_ref, right_ref, base_ref, lon_ref, lat_ref, turn_ref, o_ref = refs
    comps, _, height, width = f_ref.shape
    level = pl.program_id(0)
    row = lax.broadcasted_iota(jnp.int32, (height, width), 0)
    col = lax.broadcasted_iota(jnp.int32, (height, width), 1)
    eye = jnp.where(
        lax.broadcasted_iota(jnp.int32, (height, height), 0) == lax.broadcasted_iota(jnp.int32, (height, height), 1),
        1.0,
        0.0,
    )
    pick_row = lax.broadcasted_iota(jnp.int32, (width, height), 0)

    def columns(c):
        left = left_ref[c, 0]
        right = right_ref[c, 0]
        rows_of = jnp.where(
            pick_row == 0,
            left[0:1, :],
            jnp.where(pick_row == 1, left[1:2, :], jnp.where(pick_row == 2, right[0:1, :], jnp.where(pick_row == 3, right[1:2, :], 0.0))),
        )
        return lax.dot_general(
            eye, rows_of, (((1,), (1,)), ((), ())), precision=HIGHEST, preferred_element_type=jnp.float32
        )

    def terms(c):
        x = f_ref[c, 0]
        up = up_ref[c, 0]
        down = down_ref[c, 0]
        sides = columns(c)
        left = sides[:, 0:2]
        right = sides[:, 2:4]
        lat_m1 = jnp.where(row == 0, up[1:2, :], pltpu.roll(x, 1, 0))
        lat_m2 = jnp.where(row == 0, up[0:1, :], jnp.where(row == 1, up[1:2, :], pltpu.roll(x, 2, 0)))
        lat_p1 = jnp.where(row == height - 1, down[0:1, :], pltpu.roll(x, height - 1, 0))
        lat_p2 = jnp.where(
            row == height - 1, down[1:2, :], jnp.where(row == height - 2, down[0:1, :], pltpu.roll(x, height - 2, 0))
        )
        lon_m1 = jnp.where(col == 0, left[:, 1:2], pltpu.roll(x, 1, 1))
        lon_m2 = jnp.where(col == 0, left[:, 0:1], jnp.where(col == 1, left[:, 1:2], pltpu.roll(x, 2, 1)))
        lon_p1 = jnp.where(col == width - 1, right[:, 0:1], pltpu.roll(x, width - 1, 1))
        lon_p2 = jnp.where(
            col == width - 1, right[:, 1:2], jnp.where(col == width - 2, right[:, 0:1], pltpu.roll(x, width - 2, 1))
        )
        d_lat = (8.0 * (lat_p1 - lat_m1) - (lat_p2 - lat_m2)) / 12.0
        d_lon = (8.0 * (lon_p1 - lon_m1) - (lon_p2 - lon_m2)) / 12.0
        lap = lat_p1 + lat_m1 + lon_p1 + lon_m1 - 4.0 * x
        return x, d_lat, d_lon, lap

    def lap_of(c, x, lap):
        return lap + other_ref[c, 0] - 2.0 * x

    def store(c, x, rate):
        section = x + time_step * rate
        if first:
            o_ref[c, 0] = section
        else:
            o_ref[c, 0] = 0.5 * base_ref[c, 0] + 0.5 * section

    u1, u2, u4, u5, u6 = (f_ref[c, 0] for c in (1, 2, 4, 5, 6))
    for c in range(3):
        xa, lat_a, lon_a, lap_a = terms(c)
        xb, lat_b, lon_b, lap_b = terms(c + 3)
        adv_u_a = u1 * lat_a + u2 * lon_a
        adv_b_a = u4 * lat_a + u5 * lon_a
        adv_u_b = u1 * lat_b + u2 * lon_b
        adv_b_b = u4 * lat_b + u5 * lon_b
        rate_a = -adv_u_a + adv_b_b + viscosity * lap_of(c, xa, lap_a)
        if c == 0:
            rate_a = rate_a + buoyancy * u6
        rate_b = adv_b_a - adv_u_b + resistivity * lap_of(c + 3, xb, lap_b)
        store(c, xa, rate_a)
        store(c + 3, xb, rate_b)
    x6, lat_6, lon_6, lap_6 = terms(6)
    adv_u_6 = u1 * lat_6 + u2 * lon_6
    store(6, x6, -adv_u_6 + diffusivity * lap_of(6, x6, lap_6))

    if first:
        weight_lon = lon_ref[...]
        weight_lat = lat_ref[...]
        cosine = turn_ref[0:1, :]
        sine = turn_ref[1:2, :]
        values = []
        for c in range(comps):
            along = jnp.dot(o_ref[c, 0], weight_lon, precision=HIGHEST, preferred_element_type=jnp.float32)
            values.append(jnp.sum(along * weight_lat, axis=0, keepdims=True))
        for c in range(comps):
            if c in (1, 4):
                value = cosine * values[c] - sine * values[c + 1]
            elif c in (2, 5):
                value = sine * values[c - 1] + cosine * values[c]
            else:
                value = values[c]
            don_ref[pl.ds(2 * c + level, 1), :] = value


def advance(field, up, down, left, right, base, lon, lat, turn, first):
    planes, height, width = field.shape
    comps = planes // 2
    field = field.reshape(comps, 2, height, width)

    def by_level(shape, other=False):
        if other:
            return pl.BlockSpec((comps, 1) + shape, lambda r: (0, 1 - r, 0, 0))
        return pl.BlockSpec((comps, 1) + shape, lambda r: (0, r, 0, 0))

    def whole(shape):
        return pl.BlockSpec(shape, lambda r: (0,) * len(shape))

    args = [field, field, up.reshape(comps, 2, 2, width), down.reshape(comps, 2, 2, width)]
    args += [left.reshape(comps, 2, 2, height), right.reshape(comps, 2, 2, height)]
    specs = [by_level((height, width)), by_level((height, width), True), by_level((2, width)), by_level((2, width))]
    specs += [by_level((2, height)), by_level((2, height))]
    if not first:
        args.append(base.reshape(comps, 2, height, width))
        specs.append(by_level((height, width)))
    args += [lon, lat, turn]
    specs += [whole(lon.shape), whole(lat.shape), whole(turn.shape)]
    shape = jax.ShapeDtypeStruct(field.shape, field.dtype)
    out_specs = by_level((height, width))
    if first:
        shape = (shape, jax.ShapeDtypeStruct((planes, lon.shape[1]), jnp.float32))
        out_specs = (out_specs, whole((planes, lon.shape[1])))
    out = pl.pallas_call(
        functools.partial(stencil_kernel, first=first),
        grid=(2,),
        in_specs=specs,
        out_specs=out_specs,
        out_shape=shape,
        interpret=INTERPRET,
    )(*args)
    if first:
        return out[0].reshape(planes, height, width), out[1]
    return out.reshape(planes, height, width)


def donation_weights(cells_ref, frac_ref, rows, cols):
    dons = cells_ref.shape[1]
    cell = cells_ref[...].astype(jnp.float32)
    row = jnp.floor((cell + 0.5) * (1.0 / (cols - 1)))
    col = cell - row * (cols - 1)
    row = row.astype(jnp.int32)
    col = col.astype(jnp.int32)
    frac_t = frac_ref[0:1, :]
    frac_p = frac_ref[1:2, :]
    col_ids = lax.broadcasted_iota(jnp.int32, (cols, dons), 0)
    row_ids = lax.broadcasted_iota(jnp.int32, (rows, dons), 0)
    weight_lon = jnp.where(col_ids == col, 1.0 - frac_p, 0.0) + jnp.where(col_ids == col + 1, frac_p, 0.0)
    weight_lat = jnp.where(row_ids == row, 1.0 - frac_t, 0.0) + jnp.where(row_ids == row + 1, frac_t, 0.0)
    return weight_lon, weight_lat


def donate_planes(plane_of, planes, weight_lon, weight_lat, turn_ref, out_ref):
    cosine = turn_ref[0:1, :]
    sine = turn_ref[1:2, :]
    values = []
    for k in range(planes):
        along = jnp.dot(plane_of(k), weight_lon, precision=HIGHEST, preferred_element_type=jnp.float32)
        values.append(jnp.sum(along * weight_lat, axis=0, keepdims=True))
    for k in range(planes):
        comp, level = divmod(k, 2)
        if comp in (1, 4):
            value = cosine * values[k] - sine * values[k + 2]
        elif comp in (2, 5):
            value = sine * values[k - 2] + cosine * values[k]
        else:
            value = values[k]
        out_ref[k : k + 1, :] = value


def donation_kernel(f_ref, cells_ref, frac_ref, turn_ref, out_ref, lon_ref, lat_ref):
    planes, rows, cols = f_ref.shape
    weight_lon, weight_lat = donation_weights(cells_ref, frac_ref, rows, cols)
    lon_ref[...] = weight_lon
    lat_ref[...] = weight_lat
    donate_planes(lambda k: f_ref[k], planes, weight_lon, weight_lat, turn_ref, out_ref)


def first_donation(field, cells, frac, turn):
    planes, rows, cols = field.shape
    dons = cells.shape[1]
    return pl.pallas_call(
        donation_kernel,
        out_shape=(
            jax.ShapeDtypeStruct((planes, dons), jnp.float32),
            jax.ShapeDtypeStruct((cols, dons), jnp.float32),
            jax.ShapeDtypeStruct((rows, dons), jnp.float32),
        ),
        interpret=INTERPRET,
    )(field, cells, frac, turn)


def rotate(values, turn):
    cosine = jnp.cos(turn)
    sine = jnp.sin(turn)
    parts = [
        values[0],
        cosine * values[1] - sine * values[2],
        sine * values[1] + cosine * values[2],
        values[3],
        cosine * values[4] - sine * values[5],
        sine * values[4] + cosine * values[5],
        values[6],
    ]
    return jnp.stack(parts)


def per_device(state, source_slot, donor_cell, donor_frac, donor_turn):
    comps = state.shape[1]
    levels = state.shape[2]
    rows = state.shape[3]
    cols = state.shape[4]
    cells = donor_cell[0, 0, 0]
    frac_t = donor_frac[0, 0, 0, 0]
    frac_p = donor_frac[0, 0, 0, 1]
    turn = donor_turn[0, 0, 0]
    slots = source_slot[0, 0, 0]
    lat_pos = lax.axis_index("lat")
    lon_pos = lax.axis_index("lon")
    lat_count = lax.axis_size("lat")
    lon_count = lax.axis_size("lon")
    on_top = lat_pos == 0
    on_bottom = lat_pos == lat_count - 1
    on_left = lon_pos == 0
    on_right = lon_pos == lon_count - 1

    band = 2 * cols
    side = 2 * rows
    lat_slots = jnp.where(on_top, slots[0:band], slots[band : 2 * band])
    lon_slots = jnp.where(on_left, slots[2 * band : 2 * band + side], slots[2 * band + side :])
    wanted = jnp.concatenate([lat_slots, lon_slots])
    total = lat_count * lon_count * cells.shape[0]
    pick = (jnp.arange(total, dtype=jnp.int32)[:, None] == wanted[None, :]).astype(jnp.float32)

    def gather(packet, axis):
        size = lax.axis_size(axis)
        pos = lax.axis_index(axis)
        held = packet[None]
        k = 1
        while k < size:
            other = lax.ppermute(held, axis, [(i, i ^ k) for i in range(size)])
            low = (pos // k) % 2 == 0
            held = jnp.where(low, jnp.concatenate([held, other]), jnp.concatenate([other, held]))
            k *= 2
        return held

    def section(field, donation):
        flat = field
        given = lax.ppermute(donation, "panel", [(0, 1), (1, 0)])
        dons = given.shape[1]
        side_rows = jnp.concatenate([flat[:, :2, :], flat[:, rows - 2 :, :]], axis=1)
        lat_packet = jnp.concatenate([given, side_rows.reshape(comps * levels, -1)], axis=1)
        lat_all = gather(lat_packet, "lat")
        col_given = jnp.transpose(lat_all[:, :, :dons], (1, 0, 2)).reshape(comps * levels, -1)
        side_rows = lat_all[:, :, dons:].reshape(lat_count, comps, levels, 4, cols)
        side_cols = jnp.concatenate([flat[:, :, :2], flat[:, :, cols - 2 :]], axis=2)
        side_cols = jnp.swapaxes(side_cols, 1, 2)
        lon_packet = jnp.concatenate([col_given, side_cols.reshape(comps * levels, -1)], axis=1)
        lon_all = gather(lon_packet, "lon")
        width = col_given.shape[1]
        partner = lon_all[:, :, :width].reshape(lon_count, comps * levels, lat_count, dons)
        partner = jnp.transpose(partner, (1, 2, 0, 3)).reshape(comps * levels, -1)
        side_cols = lon_all[:, :, width:].reshape(lon_count, comps, levels, 4, rows)
        up = lax.dynamic_index_in_dim(side_rows, jnp.maximum(lat_pos - 1, 0), keepdims=False)[:, :, 2:]
        down = lax.dynamic_index_in_dim(side_rows, jnp.minimum(lat_pos + 1, lat_count - 1), keepdims=False)[:, :, :2]
        left = lax.dynamic_index_in_dim(side_cols, jnp.maximum(lon_pos - 1, 0), keepdims=False)[:, :, 2:]
        right = lax.dynamic_index_in_dim(side_cols, jnp.minimum(lon_pos + 1, lon_count - 1), keepdims=False)[:, :, :2]
        rim = jnp.dot(partner, pick, precision=HIGHEST).reshape(comps, levels, -1)
        rim_lat = rim[:, :, :band].reshape(comps, levels, 2, cols)
        rim_lon = rim[:, :, band:].reshape(comps, levels, 2, rows)
        up = jnp.where(on_top, rim_lat, up).reshape(comps * levels, 2, cols)
        down = jnp.where(on_bottom, rim_lat, down).reshape(comps * levels, 2, cols)
        left = jnp.where(on_left, rim_lon, left).reshape(comps * levels, 2, rows)
        right = jnp.where(on_right, rim_lon, right).reshape(comps * levels, 2, rows)
        return up, down, left, right

    field = state[0].reshape(comps * levels, rows, cols)
    turn_parts = jnp.concatenate([jnp.cos(donor_turn[0, 0]), jnp.sin(donor_turn[0, 0])])
    donation, lon_w, lat_w = first_donation(field, donor_cell[0, 0], donor_frac[0, 0, 0], turn_parts)
    section_one, donation = advance(field, *section(field, donation), field, lon_w, lat_w, turn_parts, True)
    new_field = advance(section_one, *section(section_one, donation), field, lon_w, lat_w, turn_parts, False)
    return new_field.reshape(1, comps, levels, rows, cols)


def solution(mesh):
    in_specs = (
        P("panel", None, None, "lat", "lon"),
        P("panel", "lat", "lon", None),
        P("panel", "lat", "lon", None),
        P("panel", "lat", "lon", None, None),
        P("panel", "lat", "lon", None),
    )
    out_specs = P("panel", None, None, "lat", "lon")
    return jax.shard_map(
        per_device, mesh=mesh, in_specs=in_specs, out_specs=out_specs, check_vma=False
    )
```

```python
import jax
import jax.numpy as jnp
from jax import lax
from jax.sharding import PartitionSpec as P
from jax.experimental import pallas as pl
from jax.experimental.pallas import tpu as pltpu
import functools

INTERPRET = False

viscosity = 0.05
resistivity = 0.05
diffusivity = 0.05
buoyancy = 0.5
time_step = 0.25

HIGHEST = lax.Precision.HIGHEST


def stencil_kernel(f_ref, up_ref, down_ref, left_ref, right_ref, base_ref, lon_ref, lat_ref, turn_ref, o_ref, *rest, first):
    planes, height, width = f_ref.shape
    comps = planes // 2
    row = lax.broadcasted_iota(jnp.int32, (height, width), 0)
    col = lax.broadcasted_iota(jnp.int32, (height, width), 1)

    eye = jnp.where(
        lax.broadcasted_iota(jnp.int32, (height, height), 0) == lax.broadcasted_iota(jnp.int32, (height, height), 1),
        1.0,
        0.0,
    )
    pick_row = lax.broadcasted_iota(jnp.int32, (width, height), 0)

    def columns(k):
        left = left_ref[k]
        right = right_ref[k]
        rows_of = jnp.where(
            pick_row == 0,
            left[0:1, :],
            jnp.where(pick_row == 1, left[1:2, :], jnp.where(pick_row == 2, right[0:1, :], jnp.where(pick_row == 3, right[1:2, :], 0.0))),
        )
        return lax.dot_general(
            eye, rows_of, (((1,), (1,)), ((), ())), precision=HIGHEST, preferred_element_type=jnp.float32
        )

    def terms(k):
        x = f_ref[k]
        up = up_ref[k]
        down = down_ref[k]
        sides = columns(k)
        left = sides[:, 0:2]
        right = sides[:, 2:4]
        lat_m1 = jnp.where(row == 0, up[1:2, :], pltpu.roll(x, 1, 0))
        lat_m2 = jnp.where(row == 0, up[0:1, :], jnp.where(row == 1, up[1:2, :], pltpu.roll(x, 2, 0)))
        lat_p1 = jnp.where(row == height - 1, down[0:1, :], pltpu.roll(x, height - 1, 0))
        lat_p2 = jnp.where(
            row == height - 1, down[1:2, :], jnp.where(row == height - 2, down[0:1, :], pltpu.roll(x, height - 2, 0))
        )
        lon_m1 = jnp.where(col == 0, left[:, 1:2], pltpu.roll(x, 1, 1))
        lon_m2 = jnp.where(col == 0, left[:, 0:1], jnp.where(col == 1, left[:, 1:2], pltpu.roll(x, 2, 1)))
        lon_p1 = jnp.where(col == width - 1, right[:, 0:1], pltpu.roll(x, width - 1, 1))
        lon_p2 = jnp.where(
            col == width - 1, right[:, 1:2], jnp.where(col == width - 2, right[:, 0:1], pltpu.roll(x, width - 2, 1))
        )
        d_lat = (8.0 * (lat_p1 - lat_m1) - (lat_p2 - lat_m2)) * (1.0 / 12.0)
        d_lon = (8.0 * (lon_p1 - lon_m1) - (lon_p2 - lon_m2)) * (1.0 / 12.0)
        lap = lat_p1 + lat_m1 + lon_p1 + lon_m1 - 4.0 * x
        return x, d_lat, d_lon, lap

    for level in range(2):
        def plane(c):
            return c * 2 + level

        def value(c):
            return f_ref[plane(c)]

        def lap_of(c, x, lap):
            above = f_ref[c * 2 + 1] if level == 0 else 0.0
            below = f_ref[c * 2] if level == 1 else 0.0
            return lap + above + below - 2.0 * x

        def store(c, x, rate):
            section = x + time_step * rate
            if first:
                o_ref[plane(c)] = section
            else:
                o_ref[plane(c)] = 0.5 * base_ref[plane(c)] + 0.5 * section

        u1, u2, u4, u5, u6 = value(1), value(2), value(4), value(5), value(6)
        for c in range(3):
            xa, lat_a, lon_a, lap_a = terms(plane(c))
            xb, lat_b, lon_b, lap_b = terms(plane(c + 3))
            adv_u_a = u1 * lat_a + u2 * lon_a
            adv_b_a = u4 * lat_a + u5 * lon_a
            adv_u_b = u1 * lat_b + u2 * lon_b
            adv_b_b = u4 * lat_b + u5 * lon_b
            rate_a = -adv_u_a + adv_b_b + viscosity * lap_of(c, xa, lap_a)
            if c == 0:
                rate_a = rate_a + buoyancy * u6
            rate_b = adv_b_a - adv_u_b + resistivity * lap_of(c + 3, xb, lap_b)
            store(c, xa, rate_a)
            store(c + 3, xb, rate_b)
        x6, lat_6, lon_6, lap_6 = terms(plane(6))
        adv_u_6 = u1 * lat_6 + u2 * lon_6
        store(6, x6, -adv_u_6 + diffusivity * lap_of(6, x6, lap_6))

    if first:
        donate_planes(lambda k: o_ref[k], planes, lon_ref[...], lat_ref[...], turn_ref, rest[0])


def advance(field, up, down, left, right, base, lon, lat, turn, first):
    shape = jax.ShapeDtypeStruct(field.shape, field.dtype)
    if first:
        shape = (shape, jax.ShapeDtypeStruct((field.shape[0], lon.shape[1]), jnp.float32))
    return pl.pallas_call(
        functools.partial(stencil_kernel, first=first),
        out_shape=shape,
        interpret=INTERPRET,
    )(field, up, down, left, right, base, lon, lat, turn)


def donation_weights(cells_ref, frac_ref, rows, cols):
    dons = cells_ref.shape[1]
    cell = cells_ref[...].astype(jnp.float32)
    row = jnp.floor((cell + 0.5) * (1.0 / (cols - 1)))
    col = cell - row * (cols - 1)
    row = row.astype(jnp.int32)
    col = col.astype(jnp.int32)
    frac_t = frac_ref[0:1, :]
    frac_p = frac_ref[1:2, :]
    col_ids = lax.broadcasted_iota(jnp.int32, (cols, dons), 0)
    row_ids = lax.broadcasted_iota(jnp.int32, (rows, dons), 0)
    weight_lon = jnp.where(col_ids == col, 1.0 - frac_p, 0.0) + jnp.where(col_ids == col + 1, frac_p, 0.0)
    weight_lat = jnp.where(row_ids == row, 1.0 - frac_t, 0.0) + jnp.where(row_ids == row + 1, frac_t, 0.0)
    return weight_lon, weight_lat


def donate_planes(plane_of, planes, weight_lon, weight_lat, turn_ref, out_ref):
    cosine = turn_ref[0:1, :]
    sine = turn_ref[1:2, :]
    values = []
    for k in range(planes):
        along = jnp.dot(plane_of(k), weight_lon, precision=HIGHEST, preferred_element_type=jnp.float32)
        values.append(jnp.sum(along * weight_lat, axis=0, keepdims=True))
    for k in range(planes):
        comp, level = divmod(k, 2)
        if comp in (1, 4):
            value = cosine * values[k] - sine * values[k + 2]
        elif comp in (2, 5):
            value = sine * values[k - 2] + cosine * values[k]
        else:
            value = values[k]
        out_ref[k : k + 1, :] = value


def donation_kernel(f_ref, cells_ref, frac_ref, turn_ref, out_ref, lon_ref, lat_ref):
    planes, rows, cols = f_ref.shape
    weight_lon, weight_lat = donation_weights(cells_ref, frac_ref, rows, cols)
    lon_ref[...] = weight_lon
    lat_ref[...] = weight_lat
    donate_planes(lambda k: f_ref[k], planes, weight_lon, weight_lat, turn_ref, out_ref)


def first_donation(field, cells, frac, turn):
    planes, rows, cols = field.shape
    dons = cells.shape[1]
    return pl.pallas_call(
        donation_kernel,
        out_shape=(
            jax.ShapeDtypeStruct((planes, dons), jnp.float32),
            jax.ShapeDtypeStruct((cols, dons), jnp.float32),
            jax.ShapeDtypeStruct((rows, dons), jnp.float32),
        ),
        interpret=INTERPRET,
    )(field, cells, frac, turn)


def rotate(values, turn):
    cosine = jnp.cos(turn)
    sine = jnp.sin(turn)
    parts = [
        values[0],
        cosine * values[1] - sine * values[2],
        sine * values[1] + cosine * values[2],
        values[3],
        cosine * values[4] - sine * values[5],
        sine * values[4] + cosine * values[5],
        values[6],
    ]
    return jnp.stack(parts)


def per_device(state, source_slot, donor_cell, donor_frac, donor_turn):
    comps = state.shape[1]
    levels = state.shape[2]
    rows = state.shape[3]
    cols = state.shape[4]
    cells = donor_cell[0, 0, 0]
    frac_t = donor_frac[0, 0, 0, 0]
    frac_p = donor_frac[0, 0, 0, 1]
    turn = donor_turn[0, 0, 0]
    slots = source_slot[0, 0, 0]
    lat_pos = lax.axis_index("lat")
    lon_pos = lax.axis_index("lon")
    lat_count = lax.axis_size("lat")
    lon_count = lax.axis_size("lon")
    on_top = lat_pos == 0
    on_bottom = lat_pos == lat_count - 1
    on_left = lon_pos == 0
    on_right = lon_pos == lon_count - 1

    band = 2 * cols
    side = 2 * rows
    lat_slots = jnp.where(on_top, slots[0:band], slots[band : 2 * band])
    lon_slots = jnp.where(on_left, slots[2 * band : 2 * band + side], slots[2 * band + side :])
    wanted = jnp.concatenate([lat_slots, lon_slots])
    total = lat_count * lon_count * cells.shape[0]
    pick = (jnp.arange(total, dtype=jnp.int32)[:, None] == wanted[None, :]).astype(jnp.float32)

    def gather(packet, axis):
        size = lax.axis_size(axis)
        pos = lax.axis_index(axis)
        held = packet[None]
        k = 1
        while k < size:
            other = lax.ppermute(held, axis, [(i, i ^ k) for i in range(size)])
            low = (pos // k) % 2 == 0
            held = jnp.where(low, jnp.concatenate([held, other]), jnp.concatenate([other, held]))
            k *= 2
        return held

    def section(field, donation):
        flat = field
        given = lax.ppermute(donation, "panel", [(0, 1), (1, 0)])
        dons = given.shape[1]
        side_rows = jnp.concatenate([flat[:, :2, :], flat[:, rows - 2 :, :]], axis=1)
        lat_packet = jnp.concatenate([given, side_rows.reshape(comps * levels, -1)], axis=1)
        lat_all = gather(lat_packet, "lat")
        col_given = jnp.transpose(lat_all[:, :, :dons], (1, 0, 2)).reshape(comps * levels, -1)
        side_rows = lat_all[:, :, dons:].reshape(lat_count, comps, levels, 4, cols)
        side_cols = jnp.concatenate([flat[:, :, :2], flat[:, :, cols - 2 :]], axis=2)
        side_cols = jnp.swapaxes(side_cols, 1, 2)
        lon_packet = jnp.concatenate([col_given, side_cols.reshape(comps * levels, -1)], axis=1)
        lon_all = gather(lon_packet, "lon")
        width = col_given.shape[1]
        partner = lon_all[:, :, :width].reshape(lon_count, comps * levels, lat_count, dons)
        partner = jnp.transpose(partner, (1, 2, 0, 3)).reshape(comps * levels, -1)
        side_cols = lon_all[:, :, width:].reshape(lon_count, comps, levels, 4, rows)
        up = lax.dynamic_index_in_dim(side_rows, jnp.maximum(lat_pos - 1, 0), keepdims=False)[:, :, 2:]
        down = lax.dynamic_index_in_dim(side_rows, jnp.minimum(lat_pos + 1, lat_count - 1), keepdims=False)[:, :, :2]
        left = lax.dynamic_index_in_dim(side_cols, jnp.maximum(lon_pos - 1, 0), keepdims=False)[:, :, 2:]
        right = lax.dynamic_index_in_dim(side_cols, jnp.minimum(lon_pos + 1, lon_count - 1), keepdims=False)[:, :, :2]
        rim = jnp.dot(partner, pick, precision=HIGHEST).reshape(comps, levels, -1)
        rim_lat = rim[:, :, :band].reshape(comps, levels, 2, cols)
        rim_lon = rim[:, :, band:].reshape(comps, levels, 2, rows)
        up = jnp.where(on_top, rim_lat, up).reshape(comps * levels, 2, cols)
        down = jnp.where(on_bottom, rim_lat, down).reshape(comps * levels, 2, cols)
        left = jnp.where(on_left, rim_lon, left).reshape(comps * levels, 2, rows)
        right = jnp.where(on_right, rim_lon, right).reshape(comps * levels, 2, rows)
        return up, down, left, right

    field = state[0].reshape(comps * levels, rows, cols)
    turn_parts = jnp.concatenate([jnp.cos(donor_turn[0, 0]), jnp.sin(donor_turn[0, 0])])
    donation, lon_w, lat_w = first_donation(field, donor_cell[0, 0], donor_frac[0, 0, 0], turn_parts)
    section_one, donation = advance(field, *section(field, donation), field, lon_w, lat_w, turn_parts, True)
    new_field = advance(section_one, *section(section_one, donation), field, lon_w, lat_w, turn_parts, False)
    return new_field.reshape(1, comps, levels, rows, cols)


def solution(mesh):
    in_specs = (
        P("panel", None, None, "lat", "lon"),
        P("panel", "lat", "lon", None),
        P("panel", "lat", "lon", None),
        P("panel", "lat", "lon", None, None),
        P("panel", "lat", "lon", None),
    )
    out_specs = P("panel", None, None, "lat", "lon")
    return jax.shard_map(
        per_device, mesh=mesh, in_specs=in_specs, out_specs=out_specs, check_vma=False
    )
```

```python
import jax
import jax.numpy as jnp
from jax import lax
from jax.sharding import PartitionSpec as P
from jax.experimental import pallas as pl
from jax.experimental.pallas import tpu as pltpu
import functools

INTERPRET = False

viscosity = 0.05
resistivity = 0.05
diffusivity = 0.05
buoyancy = 0.5
time_step = 0.25

HIGHEST = lax.Precision.HIGHEST


def stencil_kernel(f_ref, up_ref, down_ref, left_ref, right_ref, base_ref, lon_ref, lat_ref, turn_ref, o_ref, *rest, first):
    planes, height, width = f_ref.shape
    comps = planes // 2
    row = lax.broadcasted_iota(jnp.int32, (height, width), 0)
    col = lax.broadcasted_iota(jnp.int32, (height, width), 1)

    eye = jnp.where(
        lax.broadcasted_iota(jnp.int32, (height, height), 0) == lax.broadcasted_iota(jnp.int32, (height, height), 1),
        1.0,
        0.0,
    )
    pick_row = lax.broadcasted_iota(jnp.int32, (width, height), 0)

    def columns(k):
        left = left_ref[k]
        right = right_ref[k]
        rows_of = jnp.where(
            pick_row == 0,
            left[0:1, :],
            jnp.where(pick_row == 1, left[1:2, :], jnp.where(pick_row == 2, right[0:1, :], jnp.where(pick_row == 3, right[1:2, :], 0.0))),
        )
        return lax.dot_general(
            eye, rows_of, (((1,), (1,)), ((), ())), precision=HIGHEST, preferred_element_type=jnp.float32
        )

    def terms(k):
        x = f_ref[k]
        up = up_ref[k]
        down = down_ref[k]
        sides = columns(k)
        left = sides[:, 0:2]
        right = sides[:, 2:4]
        lat_m1 = jnp.where(row == 0, up[1:2, :], pltpu.roll(x, 1, 0))
        lat_m2 = jnp.where(row == 0, up[0:1, :], jnp.where(row == 1, up[1:2, :], pltpu.roll(x, 2, 0)))
        lat_p1 = jnp.where(row == height - 1, down[0:1, :], pltpu.roll(x, height - 1, 0))
        lat_p2 = jnp.where(
            row == height - 1, down[1:2, :], jnp.where(row == height - 2, down[0:1, :], pltpu.roll(x, height - 2, 0))
        )
        lon_m1 = jnp.where(col == 0, left[:, 1:2], pltpu.roll(x, 1, 1))
        lon_m2 = jnp.where(col == 0, left[:, 0:1], jnp.where(col == 1, left[:, 1:2], pltpu.roll(x, 2, 1)))
        lon_p1 = jnp.where(col == width - 1, right[:, 0:1], pltpu.roll(x, width - 1, 1))
        lon_p2 = jnp.where(
            col == width - 1, right[:, 1:2], jnp.where(col == width - 2, right[:, 0:1], pltpu.roll(x, width - 2, 1))
        )
        d_lat = (8.0 * (lat_p1 - lat_m1) - (lat_p2 - lat_m2)) * (1.0 / 12.0)
        d_lon = (8.0 * (lon_p1 - lon_m1) - (lon_p2 - lon_m2)) * (1.0 / 12.0)
        lap = lat_p1 + lat_m1 + lon_p1 + lon_m1 - 4.0 * x
        return x, d_lat, d_lon, lap

    for level in range(2):
        def plane(c):
            return c * 2 + level

        def value(c):
            return f_ref[plane(c)]

        def lap_of(c, x, lap):
            above = f_ref[c * 2 + 1] if level == 0 else 0.0
            below = f_ref[c * 2] if level == 1 else 0.0
            return lap + above + below - 2.0 * x

        def store(c, x, rate):
            section = x + time_step * rate
            if first:
                o_ref[plane(c)] = section
            else:
                o_ref[plane(c)] = 0.5 * base_ref[plane(c)] + 0.5 * section

        u1, u2, u4, u5, u6 = value(1), value(2), value(4), value(5), value(6)
        for c in range(3):
            xa, lat_a, lon_a, lap_a = terms(plane(c))
            xb, lat_b, lon_b, lap_b = terms(plane(c + 3))
            adv_u_a = u1 * lat_a + u2 * lon_a
            adv_b_a = u4 * lat_a + u5 * lon_a
            adv_u_b = u1 * lat_b + u2 * lon_b
            adv_b_b = u4 * lat_b + u5 * lon_b
            rate_a = -adv_u_a + adv_b_b + viscosity * lap_of(c, xa, lap_a)
            if c == 0:
                rate_a = rate_a + buoyancy * u6
            rate_b = adv_b_a - adv_u_b + resistivity * lap_of(c + 3, xb, lap_b)
            store(c, xa, rate_a)
            store(c + 3, xb, rate_b)
        x6, lat_6, lon_6, lap_6 = terms(plane(6))
        adv_u_6 = u1 * lat_6 + u2 * lon_6
        store(6, x6, -adv_u_6 + diffusivity * lap_of(6, x6, lap_6))

    if first:
        donate_planes(lambda k: o_ref[k], planes, lon_ref[...], lat_ref[...], turn_ref, rest[0])


def advance(field, up, down, left, right, base, lon, lat, turn, first):
    shape = jax.ShapeDtypeStruct(field.shape, field.dtype)
    if first:
        shape = (shape, jax.ShapeDtypeStruct((field.shape[0], lon.shape[1]), jnp.float32))
    return pl.pallas_call(
        functools.partial(stencil_kernel, first=first),
        out_shape=shape,
        interpret=INTERPRET,
    )(field, up, down, left, right, base, lon, lat, turn)


def donation_weights(cells_ref, frac_ref, rows, cols):
    dons = cells_ref.shape[1]
    cell = cells_ref[...].astype(jnp.float32)
    row = jnp.floor((cell + 0.5) * (1.0 / (cols - 1)))
    col = cell - row * (cols - 1)
    row = row.astype(jnp.int32)
    col = col.astype(jnp.int32)
    frac_t = frac_ref[0:1, :]
    frac_p = frac_ref[1:2, :]
    col_ids = lax.broadcasted_iota(jnp.int32, (cols, dons), 0)
    row_ids = lax.broadcasted_iota(jnp.int32, (rows, dons), 0)
    weight_lon = jnp.where(col_ids == col, 1.0 - frac_p, 0.0) + jnp.where(col_ids == col + 1, frac_p, 0.0)
    weight_lat = jnp.where(row_ids == row, 1.0 - frac_t, 0.0) + jnp.where(row_ids == row + 1, frac_t, 0.0)
    return weight_lon, weight_lat


def donate_planes(plane_of, planes, weight_lon, weight_lat, turn_ref, out_ref):
    cosine = turn_ref[0:1, :]
    sine = turn_ref[1:2, :]
    values = []
    for k in range(planes):
        along = jnp.dot(plane_of(k), weight_lon, precision=HIGHEST, preferred_element_type=jnp.float32)
        values.append(jnp.sum(along * weight_lat, axis=0, keepdims=True))
    for k in range(planes):
        comp, level = divmod(k, 2)
        if comp in (1, 4):
            value = cosine * values[k] - sine * values[k + 2]
        elif comp in (2, 5):
            value = sine * values[k - 2] + cosine * values[k]
        else:
            value = values[k]
        out_ref[k : k + 1, :] = value


def donation_kernel(f_ref, cells_ref, frac_ref, turn_ref, out_ref, lon_ref, lat_ref):
    planes, rows, cols = f_ref.shape
    weight_lon, weight_lat = donation_weights(cells_ref, frac_ref, rows, cols)
    lon_ref[...] = weight_lon
    lat_ref[...] = weight_lat
    donate_planes(lambda k: f_ref[k], planes, weight_lon, weight_lat, turn_ref, out_ref)


def first_donation(field, cells, frac, turn):
    planes, rows, cols = field.shape
    dons = cells.shape[1]
    return pl.pallas_call(
        donation_kernel,
        out_shape=(
            jax.ShapeDtypeStruct((planes, dons), jnp.float32),
            jax.ShapeDtypeStruct((cols, dons), jnp.float32),
            jax.ShapeDtypeStruct((rows, dons), jnp.float32),
        ),
        interpret=INTERPRET,
    )(field, cells, frac, turn)


def rotate(values, turn):
    cosine = jnp.cos(turn)
    sine = jnp.sin(turn)
    parts = [
        values[0],
        cosine * values[1] - sine * values[2],
        sine * values[1] + cosine * values[2],
        values[3],
        cosine * values[4] - sine * values[5],
        sine * values[4] + cosine * values[5],
        values[6],
    ]
    return jnp.stack(parts)


def per_device(state, source_slot, donor_cell, donor_frac, donor_turn):
    comps = state.shape[1]
    levels = state.shape[2]
    rows = state.shape[3]
    cols = state.shape[4]
    cells = donor_cell[0, 0, 0]
    frac_t = donor_frac[0, 0, 0, 0]
    frac_p = donor_frac[0, 0, 0, 1]
    turn = donor_turn[0, 0, 0]
    slots = source_slot[0, 0, 0]
    lat_pos = lax.axis_index("lat")
    lon_pos = lax.axis_index("lon")
    lat_count = lax.axis_size("lat")
    lon_count = lax.axis_size("lon")
    on_top = lat_pos == 0
    on_bottom = lat_pos == lat_count - 1
    on_left = lon_pos == 0
    on_right = lon_pos == lon_count - 1

    band = 2 * cols
    side = 2 * rows
    lat_slots = jnp.where(on_top, slots[0:band], slots[band : 2 * band])
    lon_slots = jnp.where(on_left, slots[2 * band : 2 * band + side], slots[2 * band + side :])
    wanted = jnp.concatenate([lat_slots, lon_slots])
    total = lat_count * lon_count * cells.shape[0]
    pick = (jnp.arange(total, dtype=jnp.int32)[:, None] == wanted[None, :]).astype(jnp.bfloat16)

    def select(values):
        high = lax.reduce_precision(values, exponent_bits=8, mantissa_bits=7)
        rest = values - high
        middle = lax.reduce_precision(rest, exponent_bits=8, mantissa_bits=7)
        low = rest - middle
        parts = jnp.concatenate([high, middle, low]).astype(jnp.bfloat16)
        picked = jnp.dot(parts, pick, preferred_element_type=jnp.float32)
        count = values.shape[0]
        return picked[:count] + (picked[count : 2 * count] + picked[2 * count :])

    def gather(packet, axis):
        size = lax.axis_size(axis)
        pos = lax.axis_index(axis)
        held = packet[None]
        k = 1
        while k < size:
            other = lax.ppermute(held, axis, [(i, i ^ k) for i in range(size)])
            low = (pos // k) % 2 == 0
            held = jnp.where(low, jnp.concatenate([held, other]), jnp.concatenate([other, held]))
            k *= 2
        return held

    def section(field, donation):
        flat = field
        given = lax.ppermute(donation, "panel", [(0, 1), (1, 0)])
        dons = given.shape[1]
        side_rows = jnp.concatenate([flat[:, :2, :], flat[:, rows - 2 :, :]], axis=1)
        lat_packet = jnp.concatenate([given, side_rows.reshape(comps * levels, -1)], axis=1)
        lat_all = gather(lat_packet, "lat")
        col_given = jnp.transpose(lat_all[:, :, :dons], (1, 0, 2)).reshape(comps * levels, -1)
        side_rows = lat_all[:, :, dons:].reshape(lat_count, comps, levels, 4, cols)
        side_cols = jnp.concatenate([flat[:, :, :2], flat[:, :, cols - 2 :]], axis=2)
        side_cols = jnp.swapaxes(side_cols, 1, 2)
        lon_packet = jnp.concatenate([col_given, side_cols.reshape(comps * levels, -1)], axis=1)
        lon_all = gather(lon_packet, "lon")
        width = col_given.shape[1]
        partner = lon_all[:, :, :width].reshape(lon_count, comps * levels, lat_count, dons)
        partner = jnp.transpose(partner, (1, 2, 0, 3)).reshape(comps * levels, -1)
        side_cols = lon_all[:, :, width:].reshape(lon_count, comps, levels, 4, rows)
        up = lax.dynamic_index_in_dim(side_rows, jnp.maximum(lat_pos - 1, 0), keepdims=False)[:, :, 2:]
        down = lax.dynamic_index_in_dim(side_rows, jnp.minimum(lat_pos + 1, lat_count - 1), keepdims=False)[:, :, :2]
        left = lax.dynamic_index_in_dim(side_cols, jnp.maximum(lon_pos - 1, 0), keepdims=False)[:, :, 2:]
        right = lax.dynamic_index_in_dim(side_cols, jnp.minimum(lon_pos + 1, lon_count - 1), keepdims=False)[:, :, :2]
        rim = select(partner).reshape(comps, levels, -1)
        rim_lat = rim[:, :, :band].reshape(comps, levels, 2, cols)
        rim_lon = rim[:, :, band:].reshape(comps, levels, 2, rows)
        up = jnp.where(on_top, rim_lat, up).reshape(comps * levels, 2, cols)
        down = jnp.where(on_bottom, rim_lat, down).reshape(comps * levels, 2, cols)
        left = jnp.where(on_left, rim_lon, left).reshape(comps * levels, 2, rows)
        right = jnp.where(on_right, rim_lon, right).reshape(comps * levels, 2, rows)
        return up, down, left, right

    field = state[0].reshape(comps * levels, rows, cols)
    turn_parts = jnp.concatenate([jnp.cos(donor_turn[0, 0]), jnp.sin(donor_turn[0, 0])])
    donation, lon_w, lat_w = first_donation(field, donor_cell[0, 0], donor_frac[0, 0, 0], turn_parts)
    section_one, donation = advance(field, *section(field, donation), field, lon_w, lat_w, turn_parts, True)
    new_field = advance(section_one, *section(section_one, donation), field, lon_w, lat_w, turn_parts, False)
    return new_field.reshape(1, comps, levels, rows, cols)


def solution(mesh):
    in_specs = (
        P("panel", None, None, "lat", "lon"),
        P("panel", "lat", "lon", None),
        P("panel", "lat", "lon", None),
        P("panel", "lat", "lon", None, None),
        P("panel", "lat", "lon", None),
    )
    out_specs = P("panel", None, None, "lat", "lon")
    return jax.shard_map(
        per_device, mesh=mesh, in_specs=in_specs, out_specs=out_specs, check_vma=False
    )
```

```python
import jax
import jax.numpy as jnp
from jax import lax
from jax.sharding import PartitionSpec as P
from jax.experimental import pallas as pl
from jax.experimental.pallas import tpu as pltpu
import functools

INTERPRET = False

viscosity = 0.05
resistivity = 0.05
diffusivity = 0.05
buoyancy = 0.5
time_step = 0.25

HIGHEST = lax.Precision.HIGHEST


def stencil_kernel(f_ref, halo_ref, base_ref, lon_ref, lat_ref, turn_ref, o_ref, *rest, first):
    planes, height, width = f_ref.shape
    comps = planes // 2
    row = lax.broadcasted_iota(jnp.int32, (height, width), 0)
    col = lax.broadcasted_iota(jnp.int32, (height, width), 1)

    eye = jnp.where(
        lax.broadcasted_iota(jnp.int32, (height, height), 0) == lax.broadcasted_iota(jnp.int32, (height, height), 1),
        1.0,
        0.0,
    )
    pick_row = lax.broadcasted_iota(jnp.int32, (width, height), 0)

    def columns(k):
        left = halo_ref[k, 4:6, 0:height]
        right = halo_ref[k, 6:8, 0:height]
        rows_of = jnp.where(
            pick_row == 0,
            left[0:1, :],
            jnp.where(pick_row == 1, left[1:2, :], jnp.where(pick_row == 2, right[0:1, :], jnp.where(pick_row == 3, right[1:2, :], 0.0))),
        )
        return lax.dot_general(
            eye, rows_of, (((1,), (1,)), ((), ())), precision=HIGHEST, preferred_element_type=jnp.float32
        )

    def terms(k):
        x = f_ref[k]
        up = halo_ref[k, 0:2, :]
        down = halo_ref[k, 2:4, :]
        sides = columns(k)
        left = sides[:, 0:2]
        right = sides[:, 2:4]
        lat_m1 = jnp.where(row == 0, up[1:2, :], pltpu.roll(x, 1, 0))
        lat_m2 = jnp.where(row == 0, up[0:1, :], jnp.where(row == 1, up[1:2, :], pltpu.roll(x, 2, 0)))
        lat_p1 = jnp.where(row == height - 1, down[0:1, :], pltpu.roll(x, height - 1, 0))
        lat_p2 = jnp.where(
            row == height - 1, down[1:2, :], jnp.where(row == height - 2, down[0:1, :], pltpu.roll(x, height - 2, 0))
        )
        lon_m1 = jnp.where(col == 0, left[:, 1:2], pltpu.roll(x, 1, 1))
        lon_m2 = jnp.where(col == 0, left[:, 0:1], jnp.where(col == 1, left[:, 1:2], pltpu.roll(x, 2, 1)))
        lon_p1 = jnp.where(col == width - 1, right[:, 0:1], pltpu.roll(x, width - 1, 1))
        lon_p2 = jnp.where(
            col == width - 1, right[:, 1:2], jnp.where(col == width - 2, right[:, 0:1], pltpu.roll(x, width - 2, 1))
        )
        d_lat = (8.0 * (lat_p1 - lat_m1) - (lat_p2 - lat_m2)) * (1.0 / 12.0)
        d_lon = (8.0 * (lon_p1 - lon_m1) - (lon_p2 - lon_m2)) * (1.0 / 12.0)
        lap = lat_p1 + lat_m1 + lon_p1 + lon_m1 - 4.0 * x
        return x, d_lat, d_lon, lap

    for level in range(2):
        def plane(c):
            return c * 2 + level

        def value(c):
            return f_ref[plane(c)]

        def lap_of(c, x, lap):
            above = f_ref[c * 2 + 1] if level == 0 else 0.0
            below = f_ref[c * 2] if level == 1 else 0.0
            return lap + above + below - 2.0 * x

        def store(c, x, rate):
            section = x + time_step * rate
            if first:
                o_ref[plane(c)] = section
            else:
                o_ref[plane(c)] = 0.5 * base_ref[plane(c)] + 0.5 * section

        u1, u2, u4, u5, u6 = value(1), value(2), value(4), value(5), value(6)
        for c in range(3):
            xa, lat_a, lon_a, lap_a = terms(plane(c))
            xb, lat_b, lon_b, lap_b = terms(plane(c + 3))
            adv_u_a = u1 * lat_a + u2 * lon_a
            adv_b_a = u4 * lat_a + u5 * lon_a
            adv_u_b = u1 * lat_b + u2 * lon_b
            adv_b_b = u4 * lat_b + u5 * lon_b
            rate_a = -adv_u_a + adv_b_b + viscosity * lap_of(c, xa, lap_a)
            if c == 0:
                rate_a = rate_a + buoyancy * u6
            rate_b = adv_b_a - adv_u_b + resistivity * lap_of(c + 3, xb, lap_b)
            store(c, xa, rate_a)
            store(c + 3, xb, rate_b)
        x6, lat_6, lon_6, lap_6 = terms(plane(6))
        adv_u_6 = u1 * lat_6 + u2 * lon_6
        store(6, x6, -adv_u_6 + diffusivity * lap_of(6, x6, lap_6))

    if first:
        donate_planes(lambda k: o_ref[k], planes, lon_ref[...], lat_ref[...], turn_ref, rest[0])


def advance(field, halo, base, lon, lat, turn, first):
    shape = jax.ShapeDtypeStruct(field.shape, field.dtype)
    if first:
        shape = (shape, jax.ShapeDtypeStruct((field.shape[0], lon.shape[1]), jnp.float32))
    return pl.pallas_call(
        functools.partial(stencil_kernel, first=first),
        out_shape=shape,
        interpret=INTERPRET,
    )(field, halo, base, lon, lat, turn)


def donation_weights(cells_ref, frac_ref, rows, cols):
    dons = cells_ref.shape[1]
    cell = cells_ref[...].astype(jnp.float32)
    row = jnp.floor((cell + 0.5) * (1.0 / (cols - 1)))
    col = cell - row * (cols - 1)
    row = row.astype(jnp.int32)
    col = col.astype(jnp.int32)
    frac_t = frac_ref[0:1, :]
    frac_p = frac_ref[1:2, :]
    col_ids = lax.broadcasted_iota(jnp.int32, (cols, dons), 0)
    row_ids = lax.broadcasted_iota(jnp.int32, (rows, dons), 0)
    weight_lon = jnp.where(col_ids == col, 1.0 - frac_p, 0.0) + jnp.where(col_ids == col + 1, frac_p, 0.0)
    weight_lat = jnp.where(row_ids == row, 1.0 - frac_t, 0.0) + jnp.where(row_ids == row + 1, frac_t, 0.0)
    return weight_lon, weight_lat


def donate_planes(plane_of, planes, weight_lon, weight_lat, turn_ref, out_ref):
    cosine = turn_ref[0:1, :]
    sine = turn_ref[1:2, :]
    values = []
    for k in range(planes):
        along = jnp.dot(plane_of(k), weight_lon, precision=HIGHEST, preferred_element_type=jnp.float32)
        values.append(jnp.sum(along * weight_lat, axis=0, keepdims=True))
    for k in range(planes):
        comp, level = divmod(k, 2)
        if comp in (1, 4):
            value = cosine * values[k] - sine * values[k + 2]
        elif comp in (2, 5):
            value = sine * values[k - 2] + cosine * values[k]
        else:
            value = values[k]
        out_ref[k : k + 1, :] = value


def donation_kernel(f_ref, cells_ref, frac_ref, turn_ref, out_ref, lon_ref, lat_ref):
    planes, rows, cols = f_ref.shape
    weight_lon, weight_lat = donation_weights(cells_ref, frac_ref, rows, cols)
    lon_ref[...] = weight_lon
    lat_ref[...] = weight_lat
    donate_planes(lambda k: f_ref[k], planes, weight_lon, weight_lat, turn_ref, out_ref)


def first_donation(field, cells, frac, turn):
    planes, rows, cols = field.shape
    dons = cells.shape[1]
    return pl.pallas_call(
        donation_kernel,
        out_shape=(
            jax.ShapeDtypeStruct((planes, dons), jnp.float32),
            jax.ShapeDtypeStruct((cols, dons), jnp.float32),
            jax.ShapeDtypeStruct((rows, dons), jnp.float32),
        ),
        interpret=INTERPRET,
    )(field, cells, frac, turn)


def rotate(values, turn):
    cosine = jnp.cos(turn)
    sine = jnp.sin(turn)
    parts = [
        values[0],
        cosine * values[1] - sine * values[2],
        sine * values[1] + cosine * values[2],
        values[3],
        cosine * values[4] - sine * values[5],
        sine * values[4] + cosine * values[5],
        values[6],
    ]
    return jnp.stack(parts)


def per_device(state, source_slot, donor_cell, donor_frac, donor_turn):
    comps = state.shape[1]
    levels = state.shape[2]
    rows = state.shape[3]
    cols = state.shape[4]
    cells = donor_cell[0, 0, 0]
    frac_t = donor_frac[0, 0, 0, 0]
    frac_p = donor_frac[0, 0, 0, 1]
    turn = donor_turn[0, 0, 0]
    slots = source_slot[0, 0, 0]
    lat_pos = lax.axis_index("lat")
    lon_pos = lax.axis_index("lon")
    lat_count = lax.axis_size("lat")
    lon_count = lax.axis_size("lon")
    on_top = lat_pos == 0
    on_bottom = lat_pos == lat_count - 1
    on_left = lon_pos == 0
    on_right = lon_pos == lon_count - 1

    band = 2 * cols
    side = 2 * rows
    lat_slots = jnp.where(on_top, slots[0:band], slots[band : 2 * band])
    lon_slots = jnp.where(on_left, slots[2 * band : 2 * band + side], slots[2 * band + side :])
    wanted = jnp.concatenate([lat_slots, lon_slots])
    total = lat_count * lon_count * cells.shape[0]
    pick = (jnp.arange(total, dtype=jnp.int32)[:, None] == wanted[None, :]).astype(jnp.bfloat16)

    def select(values):
        high = lax.reduce_precision(values, exponent_bits=8, mantissa_bits=7)
        rest = values - high
        middle = lax.reduce_precision(rest, exponent_bits=8, mantissa_bits=7)
        low = rest - middle
        parts = jnp.concatenate([high, middle, low]).astype(jnp.bfloat16)
        picked = jnp.dot(parts, pick, preferred_element_type=jnp.float32)
        count = values.shape[0]
        return picked[:count] + (picked[count : 2 * count] + picked[2 * count :])

    def gather(packet, axis):
        size = lax.axis_size(axis)
        pos = lax.axis_index(axis)
        held = packet[None]
        k = 1
        while k < size:
            other = lax.ppermute(held, axis, [(i, i ^ k) for i in range(size)])
            low = (pos // k) % 2 == 0
            held = jnp.where(low, jnp.concatenate([held, other]), jnp.concatenate([other, held]))
            k *= 2
        return held

    def section(field, donation):
        flat = field
        given = lax.ppermute(donation, "panel", [(0, 1), (1, 0)])
        dons = given.shape[1]
        side_rows = jnp.concatenate([flat[:, :2, :], flat[:, rows - 2 :, :]], axis=1)
        lat_packet = jnp.concatenate([given, side_rows.reshape(comps * levels, -1)], axis=1)
        lat_all = gather(lat_packet, "lat")
        col_given = jnp.transpose(lat_all[:, :, :dons], (1, 0, 2)).reshape(comps * levels, -1)
        side_rows = lat_all[:, :, dons:].reshape(lat_count, comps, levels, 4, cols)
        side_cols = jnp.concatenate([flat[:, :, :2], flat[:, :, cols - 2 :]], axis=2)
        side_cols = jnp.swapaxes(side_cols, 1, 2)
        lon_packet = jnp.concatenate([col_given, side_cols.reshape(comps * levels, -1)], axis=1)
        lon_all = gather(lon_packet, "lon")
        width = col_given.shape[1]
        partner = lon_all[:, :, :width].reshape(lon_count, comps * levels, lat_count, dons)
        partner = jnp.transpose(partner, (1, 2, 0, 3)).reshape(comps * levels, -1)
        side_cols = lon_all[:, :, width:].reshape(lon_count, comps, levels, 4, rows)
        up = lax.dynamic_index_in_dim(side_rows, jnp.maximum(lat_pos - 1, 0), keepdims=False)[:, :, 2:]
        down = lax.dynamic_index_in_dim(side_rows, jnp.minimum(lat_pos + 1, lat_count - 1), keepdims=False)[:, :, :2]
        left = lax.dynamic_index_in_dim(side_cols, jnp.maximum(lon_pos - 1, 0), keepdims=False)[:, :, 2:]
        right = lax.dynamic_index_in_dim(side_cols, jnp.minimum(lon_pos + 1, lon_count - 1), keepdims=False)[:, :, :2]
        rim = select(partner).reshape(comps, levels, -1)
        rim_lat = rim[:, :, :band].reshape(comps, levels, 2, cols)
        rim_lon = rim[:, :, band:].reshape(comps, levels, 2, rows)
        up = jnp.where(on_top, rim_lat, up).reshape(comps * levels, 2, cols)
        down = jnp.where(on_bottom, rim_lat, down).reshape(comps * levels, 2, cols)
        left = jnp.where(on_left, rim_lon, left).reshape(comps * levels, 2, rows)
        right = jnp.where(on_right, rim_lon, right).reshape(comps * levels, 2, rows)
        sides = jnp.pad(jnp.concatenate([left, right], axis=1), ((0, 0), (0, 0), (0, cols - rows)))
        return (jnp.concatenate([up, down, sides], axis=1),)

    field = state[0].reshape(comps * levels, rows, cols)
    turn_parts = jnp.concatenate([jnp.cos(donor_turn[0, 0]), jnp.sin(donor_turn[0, 0])])
    donation, lon_w, lat_w = first_donation(field, donor_cell[0, 0], donor_frac[0, 0, 0], turn_parts)
    section_one, donation = advance(field, *section(field, donation), field, lon_w, lat_w, turn_parts, True)
    new_field = advance(section_one, *section(section_one, donation), field, lon_w, lat_w, turn_parts, False)
    return new_field.reshape(1, comps, levels, rows, cols)


def solution(mesh):
    in_specs = (
        P("panel", None, None, "lat", "lon"),
        P("panel", "lat", "lon", None),
        P("panel", "lat", "lon", None),
        P("panel", "lat", "lon", None, None),
        P("panel", "lat", "lon", None),
    )
    out_specs = P("panel", None, None, "lat", "lon")
    return jax.shard_map(
        per_device, mesh=mesh, in_specs=in_specs, out_specs=out_specs, check_vma=False
    )
```

```python
import jax
import jax.numpy as jnp
from jax import lax
from jax.sharding import PartitionSpec as P
from jax.experimental import pallas as pl
from jax.experimental.pallas import tpu as pltpu
import functools

INTERPRET = False

viscosity = 0.05
resistivity = 0.05
diffusivity = 0.05
buoyancy = 0.5
time_step = 0.25

HIGHEST = lax.Precision.HIGHEST


def stencil_kernel(f_ref, halo_ref, base_ref, lon_ref, lat_ref, turn_ref, o_ref, *rest, first):
    planes, height, width = f_ref.shape
    comps = planes // 2
    row = lax.broadcasted_iota(jnp.int32, (height, width), 0)
    col = lax.broadcasted_iota(jnp.int32, (height, width), 1)
    tile = lax.broadcasted_iota(jnp.int32, (8, width), 0)

    eye = jnp.where(
        lax.broadcasted_iota(jnp.int32, (height, height), 0) == lax.broadcasted_iota(jnp.int32, (height, height), 1),
        1.0,
        0.0,
    )
    pick_row = lax.broadcasted_iota(jnp.int32, (width, height), 0)

    def columns(k):
        left = halo_ref[k, 4:6, 0:height]
        right = halo_ref[k, 6:8, 0:height]
        rows_of = jnp.where(
            pick_row == 0,
            left[0:1, :],
            jnp.where(pick_row == 1, left[1:2, :], jnp.where(pick_row == 2, right[0:1, :], jnp.where(pick_row == 3, right[1:2, :], 0.0))),
        )
        return lax.dot_general(
            eye, rows_of, (((1,), (1,)), ((), ())), precision=HIGHEST, preferred_element_type=jnp.float32
        )

    def terms(k):
        x = f_ref[k]
        up = halo_ref[k, 0:2, :]
        down = halo_ref[k, 2:4, :]
        sides = columns(k)
        left = sides[:, 0:2]
        right = sides[:, 2:4]
        rolled = pltpu.roll(x, 1, 0)
        lat_m1 = jnp.concatenate([jnp.where(tile == 0, up[1:2, :], rolled[:8]), rolled[8:]], axis=0)
        rolled = pltpu.roll(x, 2, 0)
        top = jnp.where(tile == 0, up[0:1, :], jnp.where(tile == 1, up[1:2, :], rolled[:8]))
        lat_m2 = jnp.concatenate([top, rolled[8:]], axis=0)
        rolled = pltpu.roll(x, height - 1, 0)
        lat_p1 = jnp.concatenate([rolled[: height - 8], jnp.where(tile == 7, down[0:1, :], rolled[height - 8 :])], axis=0)
        rolled = pltpu.roll(x, height - 2, 0)
        bottom = jnp.where(tile == 7, down[1:2, :], jnp.where(tile == 6, down[0:1, :], rolled[height - 8 :]))
        lat_p2 = jnp.concatenate([rolled[: height - 8], bottom], axis=0)
        lon_m1 = jnp.where(col == 0, left[:, 1:2], pltpu.roll(x, 1, 1))
        lon_m2 = jnp.where(col == 0, left[:, 0:1], jnp.where(col == 1, left[:, 1:2], pltpu.roll(x, 2, 1)))
        lon_p1 = jnp.where(col == width - 1, right[:, 0:1], pltpu.roll(x, width - 1, 1))
        lon_p2 = jnp.where(
            col == width - 1, right[:, 1:2], jnp.where(col == width - 2, right[:, 0:1], pltpu.roll(x, width - 2, 1))
        )
        d_lat = (8.0 * (lat_p1 - lat_m1) - (lat_p2 - lat_m2)) * (1.0 / 12.0)
        d_lon = (8.0 * (lon_p1 - lon_m1) - (lon_p2 - lon_m2)) * (1.0 / 12.0)
        lap = lat_p1 + lat_m1 + lon_p1 + lon_m1 - 4.0 * x
        return x, d_lat, d_lon, lap

    for level in range(2):
        def plane(c):
            return c * 2 + level

        def value(c):
            return f_ref[plane(c)]

        def lap_of(c, x, lap):
            above = f_ref[c * 2 + 1] if level == 0 else 0.0
            below = f_ref[c * 2] if level == 1 else 0.0
            return lap + above + below - 2.0 * x

        def store(c, x, rate):
            section = x + time_step * rate
            if first:
                o_ref[plane(c)] = section
            else:
                o_ref[plane(c)] = 0.5 * base_ref[plane(c)] + 0.5 * section

        u1, u2, u4, u5, u6 = value(1), value(2), value(4), value(5), value(6)
        for c in range(3):
            xa, lat_a, lon_a, lap_a = terms(plane(c))
            xb, lat_b, lon_b, lap_b = terms(plane(c + 3))
            adv_u_a = u1 * lat_a + u2 * lon_a
            adv_b_a = u4 * lat_a + u5 * lon_a
            adv_u_b = u1 * lat_b + u2 * lon_b
            adv_b_b = u4 * lat_b + u5 * lon_b
            rate_a = -adv_u_a + adv_b_b + viscosity * lap_of(c, xa, lap_a)
            if c == 0:
                rate_a = rate_a + buoyancy * u6
            rate_b = adv_b_a - adv_u_b + resistivity * lap_of(c + 3, xb, lap_b)
            store(c, xa, rate_a)
            store(c + 3, xb, rate_b)
        x6, lat_6, lon_6, lap_6 = terms(plane(6))
        adv_u_6 = u1 * lat_6 + u2 * lon_6
        store(6, x6, -adv_u_6 + diffusivity * lap_of(6, x6, lap_6))

    if first:
        donate_planes(lambda k: o_ref[k], planes, lon_ref[...], lat_ref[...], turn_ref, rest[0])


def advance(field, halo, base, lon, lat, turn, first):
    shape = jax.ShapeDtypeStruct(field.shape, field.dtype)
    if first:
        shape = (shape, jax.ShapeDtypeStruct((field.shape[0], lon.shape[1]), jnp.float32))
    return pl.pallas_call(
        functools.partial(stencil_kernel, first=first),
        out_shape=shape,
        interpret=INTERPRET,
    )(field, halo, base, lon, lat, turn)


def donation_weights(cells_ref, frac_ref, rows, cols):
    dons = cells_ref.shape[1]
    cell = cells_ref[...].astype(jnp.float32)
    row = jnp.floor((cell + 0.5) * (1.0 / (cols - 1)))
    col = cell - row * (cols - 1)
    row = row.astype(jnp.int32)
    col = col.astype(jnp.int32)
    frac_t = frac_ref[0:1, :]
    frac_p = frac_ref[1:2, :]
    col_ids = lax.broadcasted_iota(jnp.int32, (cols, dons), 0)
    row_ids = lax.broadcasted_iota(jnp.int32, (rows, dons), 0)
    weight_lon = jnp.where(col_ids == col, 1.0 - frac_p, 0.0) + jnp.where(col_ids == col + 1, frac_p, 0.0)
    weight_lat = jnp.where(row_ids == row, 1.0 - frac_t, 0.0) + jnp.where(row_ids == row + 1, frac_t, 0.0)
    return weight_lon, weight_lat


def donate_planes(plane_of, planes, weight_lon, weight_lat, turn_ref, out_ref):
    cosine = turn_ref[0:1, :]
    sine = turn_ref[1:2, :]
    values = []
    for k in range(planes):
        along = jnp.dot(plane_of(k), weight_lon, precision=HIGHEST, preferred_element_type=jnp.float32)
        values.append(jnp.sum(along * weight_lat, axis=0, keepdims=True))
    for k in range(planes):
        comp, level = divmod(k, 2)
        if comp in (1, 4):
            value = cosine * values[k] - sine * values[k + 2]
        elif comp in (2, 5):
            value = sine * values[k - 2] + cosine * values[k]
        else:
            value = values[k]
        out_ref[k : k + 1, :] = value


def donation_kernel(f_ref, cells_ref, frac_ref, turn_ref, out_ref, lon_ref, lat_ref):
    planes, rows, cols = f_ref.shape
    weight_lon, weight_lat = donation_weights(cells_ref, frac_ref, rows, cols)
    lon_ref[...] = weight_lon
    lat_ref[...] = weight_lat
    donate_planes(lambda k: f_ref[k], planes, weight_lon, weight_lat, turn_ref, out_ref)


def first_donation(field, cells, frac, turn):
    planes, rows, cols = field.shape
    dons = cells.shape[1]
    return pl.pallas_call(
        donation_kernel,
        out_shape=(
            jax.ShapeDtypeStruct((planes, dons), jnp.float32),
            jax.ShapeDtypeStruct((cols, dons), jnp.float32),
            jax.ShapeDtypeStruct((rows, dons), jnp.float32),
        ),
        interpret=INTERPRET,
    )(field, cells, frac, turn)


def rotate(values, turn):
    cosine = jnp.cos(turn)
    sine = jnp.sin(turn)
    parts = [
        values[0],
        cosine * values[1] - sine * values[2],
        sine * values[1] + cosine * values[2],
        values[3],
        cosine * values[4] - sine * values[5],
        sine * values[4] + cosine * values[5],
        values[6],
    ]
    return jnp.stack(parts)


def per_device(state, source_slot, donor_cell, donor_frac, donor_turn):
    comps = state.shape[1]
    levels = state.shape[2]
    rows = state.shape[3]
    cols = state.shape[4]
    cells = donor_cell[0, 0, 0]
    frac_t = donor_frac[0, 0, 0, 0]
    frac_p = donor_frac[0, 0, 0, 1]
    turn = donor_turn[0, 0, 0]
    slots = source_slot[0, 0, 0]
    lat_pos = lax.axis_index("lat")
    lon_pos = lax.axis_index("lon")
    lat_count = lax.axis_size("lat")
    lon_count = lax.axis_size("lon")
    on_top = lat_pos == 0
    on_bottom = lat_pos == lat_count - 1
    on_left = lon_pos == 0
    on_right = lon_pos == lon_count - 1

    band = 2 * cols
    side = 2 * rows
    lat_slots = jnp.where(on_top, slots[0:band], slots[band : 2 * band])
    lon_slots = jnp.where(on_left, slots[2 * band : 2 * band + side], slots[2 * band + side :])
    wanted = jnp.concatenate([lat_slots, lon_slots])
    total = lat_count * lon_count * cells.shape[0]
    pick = (jnp.arange(total, dtype=jnp.int32)[:, None] == wanted[None, :]).astype(jnp.bfloat16)

    def select(values):
        high = lax.reduce_precision(values, exponent_bits=8, mantissa_bits=7)
        rest = values - high
        middle = lax.reduce_precision(rest, exponent_bits=8, mantissa_bits=7)
        low = rest - middle
        parts = jnp.concatenate([high, middle, low]).astype(jnp.bfloat16)
        picked = jnp.dot(parts, pick, preferred_element_type=jnp.float32)
        count = values.shape[0]
        return picked[:count] + (picked[count : 2 * count] + picked[2 * count :])

    def gather(packet, axis):
        size = lax.axis_size(axis)
        pos = lax.axis_index(axis)
        held = packet[None]
        k = 1
        while k < size:
            other = lax.ppermute(held, axis, [(i, i ^ k) for i in range(size)])
            low = (pos // k) % 2 == 0
            held = jnp.where(low, jnp.concatenate([held, other]), jnp.concatenate([other, held]))
            k *= 2
        return held

    def section(field, donation):
        flat = field
        given = lax.ppermute(donation, "panel", [(0, 1), (1, 0)])
        dons = given.shape[1]
        side_rows = jnp.concatenate([flat[:, :2, :], flat[:, rows - 2 :, :]], axis=1)
        lat_packet = jnp.concatenate([given, side_rows.reshape(comps * levels, -1)], axis=1)
        lat_all = gather(lat_packet, "lat")
        col_given = jnp.transpose(lat_all[:, :, :dons], (1, 0, 2)).reshape(comps * levels, -1)
        side_rows = lat_all[:, :, dons:].reshape(lat_count, comps, levels, 4, cols)
        side_cols = jnp.concatenate([flat[:, :, :2], flat[:, :, cols - 2 :]], axis=2)
        side_cols = jnp.swapaxes(side_cols, 1, 2)
        lon_packet = jnp.concatenate([col_given, side_cols.reshape(comps * levels, -1)], axis=1)
        lon_all = gather(lon_packet, "lon")
        width = col_given.shape[1]
        partner = lon_all[:, :, :width].reshape(lon_count, comps * levels, lat_count, dons)
        partner = jnp.transpose(partner, (1, 2, 0, 3)).reshape(comps * levels, -1)
        side_cols = lon_all[:, :, width:].reshape(lon_count, comps, levels, 4, rows)
        up = lax.dynamic_index_in_dim(side_rows, jnp.maximum(lat_pos - 1, 0), keepdims=False)[:, :, 2:]
        down = lax.dynamic_index_in_dim(side_rows, jnp.minimum(lat_pos + 1, lat_count - 1), keepdims=False)[:, :, :2]
        left = lax.dynamic_index_in_dim(side_cols, jnp.maximum(lon_pos - 1, 0), keepdims=False)[:, :, 2:]
        right = lax.dynamic_index_in_dim(side_cols, jnp.minimum(lon_pos + 1, lon_count - 1), keepdims=False)[:, :, :2]
        rim = select(partner).reshape(comps, levels, -1)
        rim_lat = rim[:, :, :band].reshape(comps, levels, 2, cols)
        rim_lon = rim[:, :, band:].reshape(comps, levels, 2, rows)
        up = jnp.where(on_top, rim_lat, up).reshape(comps * levels, 2, cols)
        down = jnp.where(on_bottom, rim_lat, down).reshape(comps * levels, 2, cols)
        left = jnp.where(on_left, rim_lon, left).reshape(comps * levels, 2, rows)
        right = jnp.where(on_right, rim_lon, right).reshape(comps * levels, 2, rows)
        sides = jnp.pad(jnp.concatenate([left, right], axis=1), ((0, 0), (0, 0), (0, cols - rows)))
        return (jnp.concatenate([up, down, sides], axis=1),)

    field = state[0].reshape(comps * levels, rows, cols)
    turn_parts = jnp.concatenate([jnp.cos(donor_turn[0, 0]), jnp.sin(donor_turn[0, 0])])
    donation, lon_w, lat_w = first_donation(field, donor_cell[0, 0], donor_frac[0, 0, 0], turn_parts)
    section_one, donation = advance(field, *section(field, donation), field, lon_w, lat_w, turn_parts, True)
    new_field = advance(section_one, *section(section_one, donation), field, lon_w, lat_w, turn_parts, False)
    return new_field.reshape(1, comps, levels, rows, cols)


def solution(mesh):
    in_specs = (
        P("panel", None, None, "lat", "lon"),
        P("panel", "lat", "lon", None),
        P("panel", "lat", "lon", None),
        P("panel", "lat", "lon", None, None),
        P("panel", "lat", "lon", None),
    )
    out_specs = P("panel", None, None, "lat", "lon")
    return jax.shard_map(
        per_device, mesh=mesh, in_specs=in_specs, out_specs=out_specs, check_vma=False
    )
```

```python
import jax
import jax.numpy as jnp
from jax import lax
from jax.sharding import PartitionSpec as P
from jax.experimental import pallas as pl
from jax.experimental.pallas import tpu as pltpu
import functools

INTERPRET = False

viscosity = 0.05
resistivity = 0.05
diffusivity = 0.05
buoyancy = 0.5
time_step = 0.25

HIGHEST = lax.Precision.HIGHEST


def stencil_kernel(*refs, first):
    if first:
        f_ref, halo_ref, lon_ref, lat_ref, turn_ref, o_ref, don_ref = refs
    else:
        f_ref, halo_ref, base_ref, o_ref = refs
    planes, height, width = f_ref.shape
    comps = planes // 2
    row = lax.broadcasted_iota(jnp.int32, (height, width), 0)
    col = lax.broadcasted_iota(jnp.int32, (height, width), 1)
    tile = lax.broadcasted_iota(jnp.int32, (8, width), 0)

    eye = jnp.where(
        lax.broadcasted_iota(jnp.int32, (height, height), 0) == lax.broadcasted_iota(jnp.int32, (height, height), 1),
        1.0,
        0.0,
    )
    pick_row = lax.broadcasted_iota(jnp.int32, (width, height), 0)

    def columns(k):
        left = halo_ref[k, 4:6, 0:height]
        right = halo_ref[k, 6:8, 0:height]
        rows_of = jnp.where(
            pick_row == 0,
            left[0:1, :],
            jnp.where(pick_row == 1, left[1:2, :], jnp.where(pick_row == 2, right[0:1, :], jnp.where(pick_row == 3, right[1:2, :], 0.0))),
        )
        return lax.dot_general(
            eye, rows_of, (((1,), (1,)), ((), ())), precision=HIGHEST, preferred_element_type=jnp.float32
        )

    def terms(k):
        x = f_ref[k]
        up = halo_ref[k, 0:2, :]
        down = halo_ref[k, 2:4, :]
        sides = columns(k)
        left = sides[:, 0:2]
        right = sides[:, 2:4]
        rolled = pltpu.roll(x, 1, 0)
        lat_m1 = jnp.concatenate([jnp.where(tile == 0, up[1:2, :], rolled[:8]), rolled[8:]], axis=0)
        rolled = pltpu.roll(x, 2, 0)
        top = jnp.where(tile == 0, up[0:1, :], jnp.where(tile == 1, up[1:2, :], rolled[:8]))
        lat_m2 = jnp.concatenate([top, rolled[8:]], axis=0)
        rolled = pltpu.roll(x, height - 1, 0)
        lat_p1 = jnp.concatenate([rolled[: height - 8], jnp.where(tile == 7, down[0:1, :], rolled[height - 8 :])], axis=0)
        rolled = pltpu.roll(x, height - 2, 0)
        bottom = jnp.where(tile == 7, down[1:2, :], jnp.where(tile == 6, down[0:1, :], rolled[height - 8 :]))
        lat_p2 = jnp.concatenate([rolled[: height - 8], bottom], axis=0)
        lon_m1 = jnp.where(col == 0, left[:, 1:2], pltpu.roll(x, 1, 1))
        lon_m2 = jnp.where(col == 0, left[:, 0:1], jnp.where(col == 1, left[:, 1:2], pltpu.roll(x, 2, 1)))
        lon_p1 = jnp.where(col == width - 1, right[:, 0:1], pltpu.roll(x, width - 1, 1))
        lon_p2 = jnp.where(
            col == width - 1, right[:, 1:2], jnp.where(col == width - 2, right[:, 0:1], pltpu.roll(x, width - 2, 1))
        )
        d_lat = (8.0 * (lat_p1 - lat_m1) - (lat_p2 - lat_m2)) * (1.0 / 12.0)
        d_lon = (8.0 * (lon_p1 - lon_m1) - (lon_p2 - lon_m2)) * (1.0 / 12.0)
        lap = lat_p1 + lat_m1 + lon_p1 + lon_m1 - 4.0 * x
        return x, d_lat, d_lon, lap

    for level in range(2):
        def plane(c):
            return c * 2 + level

        def value(c):
            return f_ref[plane(c)]

        def lap_of(c, x, lap):
            above = f_ref[c * 2 + 1] if level == 0 else 0.0
            below = f_ref[c * 2] if level == 1 else 0.0
            return lap + above + below - 2.0 * x

        def store(c, x, rate):
            section = x + time_step * rate
            if first:
                o_ref[plane(c)] = section
            else:
                o_ref[plane(c)] = 0.5 * base_ref[plane(c)] + 0.5 * section

        u1, u2, u4, u5, u6 = value(1), value(2), value(4), value(5), value(6)
        for c in range(3):
            xa, lat_a, lon_a, lap_a = terms(plane(c))
            xb, lat_b, lon_b, lap_b = terms(plane(c + 3))
            adv_u_a = u1 * lat_a + u2 * lon_a
            adv_b_a = u4 * lat_a + u5 * lon_a
            adv_u_b = u1 * lat_b + u2 * lon_b
            adv_b_b = u4 * lat_b + u5 * lon_b
            rate_a = -adv_u_a + adv_b_b + viscosity * lap_of(c, xa, lap_a)
            if c == 0:
                rate_a = rate_a + buoyancy * u6
            rate_b = adv_b_a - adv_u_b + resistivity * lap_of(c + 3, xb, lap_b)
            store(c, xa, rate_a)
            store(c + 3, xb, rate_b)
        x6, lat_6, lon_6, lap_6 = terms(plane(6))
        adv_u_6 = u1 * lat_6 + u2 * lon_6
        store(6, x6, -adv_u_6 + diffusivity * lap_of(6, x6, lap_6))

    if first:
        donate_planes(lambda k: o_ref[k], planes, lon_ref[...], lat_ref[...], turn_ref, don_ref)


def advance(field, halo, base, lon, lat, turn, first):
    shape = jax.ShapeDtypeStruct(field.shape, field.dtype)
    if first:
        shape = (shape, jax.ShapeDtypeStruct((field.shape[0], lon.shape[1]), jnp.float32))
    return pl.pallas_call(
        functools.partial(stencil_kernel, first=first),
        out_shape=shape,
        interpret=INTERPRET,
    )(*((field, halo, lon, lat, turn) if first else (field, halo, base)))


def donation_weights(cells_ref, frac_ref, rows, cols):
    dons = cells_ref.shape[1]
    cell = cells_ref[...].astype(jnp.float32)
    row = jnp.floor((cell + 0.5) * (1.0 / (cols - 1)))
    col = cell - row * (cols - 1)
    row = row.astype(jnp.int32)
    col = col.astype(jnp.int32)
    frac_t = frac_ref[0:1, :]
    frac_p = frac_ref[1:2, :]
    col_ids = lax.broadcasted_iota(jnp.int32, (cols, dons), 0)
    row_ids = lax.broadcasted_iota(jnp.int32, (rows, dons), 0)
    weight_lon = jnp.where(col_ids == col, 1.0 - frac_p, 0.0) + jnp.where(col_ids == col + 1, frac_p, 0.0)
    weight_lat = jnp.where(row_ids == row, 1.0 - frac_t, 0.0) + jnp.where(row_ids == row + 1, frac_t, 0.0)
    return weight_lon, weight_lat


def donate_planes(plane_of, planes, weight_lon, weight_lat, turn_ref, out_ref):
    cosine = turn_ref[0:1, :]
    sine = turn_ref[1:2, :]
    values = []
    for k in range(planes):
        along = jnp.dot(plane_of(k), weight_lon, precision=HIGHEST, preferred_element_type=jnp.float32)
        values.append(jnp.sum(along * weight_lat, axis=0, keepdims=True))
    for k in range(planes):
        comp, level = divmod(k, 2)
        if comp in (1, 4):
            value = cosine * values[k] - sine * values[k + 2]
        elif comp in (2, 5):
            value = sine * values[k - 2] + cosine * values[k]
        else:
            value = values[k]
        out_ref[k : k + 1, :] = value


def donation_kernel(f_ref, cells_ref, frac_ref, turn_ref, out_ref, lon_ref, lat_ref):
    planes, rows, cols = f_ref.shape
    weight_lon, weight_lat = donation_weights(cells_ref, frac_ref, rows, cols)
    lon_ref[...] = weight_lon
    lat_ref[...] = weight_lat
    donate_planes(lambda k: f_ref[k], planes, weight_lon, weight_lat, turn_ref, out_ref)


def first_donation(field, cells, frac, turn):
    planes, rows, cols = field.shape
    dons = cells.shape[1]
    return pl.pallas_call(
        donation_kernel,
        out_shape=(
            jax.ShapeDtypeStruct((planes, dons), jnp.float32),
            jax.ShapeDtypeStruct((cols, dons), jnp.float32),
            jax.ShapeDtypeStruct((rows, dons), jnp.float32),
        ),
        interpret=INTERPRET,
    )(field, cells, frac, turn)


def rotate(values, turn):
    cosine = jnp.cos(turn)
    sine = jnp.sin(turn)
    parts = [
        values[0],
        cosine * values[1] - sine * values[2],
        sine * values[1] + cosine * values[2],
        values[3],
        cosine * values[4] - sine * values[5],
        sine * values[4] + cosine * values[5],
        values[6],
    ]
    return jnp.stack(parts)


def per_device(state, source_slot, donor_cell, donor_frac, donor_turn):
    comps = state.shape[1]
    levels = state.shape[2]
    rows = state.shape[3]
    cols = state.shape[4]
    cells = donor_cell[0, 0, 0]
    frac_t = donor_frac[0, 0, 0, 0]
    frac_p = donor_frac[0, 0, 0, 1]
    turn = donor_turn[0, 0, 0]
    slots = source_slot[0, 0, 0]
    lat_pos = lax.axis_index("lat")
    lon_pos = lax.axis_index("lon")
    lat_count = lax.axis_size("lat")
    lon_count = lax.axis_size("lon")
    on_top = lat_pos == 0
    on_bottom = lat_pos == lat_count - 1
    on_left = lon_pos == 0
    on_right = lon_pos == lon_count - 1

    band = 2 * cols
    side = 2 * rows
    lat_slots = jnp.where(on_top, slots[0:band], slots[band : 2 * band])
    lon_slots = jnp.where(on_left, slots[2 * band : 2 * band + side], slots[2 * band + side :])
    wanted = jnp.concatenate([lat_slots, lon_slots])
    total = lat_count * lon_count * cells.shape[0]
    pick = (jnp.arange(total, dtype=jnp.int32)[:, None] == wanted[None, :]).astype(jnp.bfloat16)

    def select(values):
        high = lax.reduce_precision(values, exponent_bits=8, mantissa_bits=7)
        rest = values - high
        middle = lax.reduce_precision(rest, exponent_bits=8, mantissa_bits=7)
        low = rest - middle
        parts = jnp.concatenate([high, middle, low]).astype(jnp.bfloat16)
        picked = jnp.dot(parts, pick, preferred_element_type=jnp.float32)
        count = values.shape[0]
        return picked[:count] + (picked[count : 2 * count] + picked[2 * count :])

    def gather(packet, axis):
        size = lax.axis_size(axis)
        pos = lax.axis_index(axis)
        held = packet[None]
        k = 1
        while k < size:
            other = lax.ppermute(held, axis, [(i, i ^ k) for i in range(size)])
            low = (pos // k) % 2 == 0
            held = jnp.where(low, jnp.concatenate([held, other]), jnp.concatenate([other, held]))
            k *= 2
        return held

    def section(field, donation):
        flat = field
        given = lax.ppermute(donation, "panel", [(0, 1), (1, 0)])
        dons = given.shape[1]
        side_rows = jnp.concatenate([flat[:, :2, :], flat[:, rows - 2 :, :]], axis=1)
        lat_packet = jnp.concatenate([given, side_rows.reshape(comps * levels, -1)], axis=1)
        lat_all = gather(lat_packet, "lat")
        col_given = jnp.transpose(lat_all[:, :, :dons], (1, 0, 2)).reshape(comps * levels, -1)
        side_rows = lat_all[:, :, dons:].reshape(lat_count, comps, levels, 4, cols)
        side_cols = jnp.concatenate([flat[:, :, :2], flat[:, :, cols - 2 :]], axis=2)
        side_cols = jnp.swapaxes(side_cols, 1, 2)
        lon_packet = jnp.concatenate([col_given, side_cols.reshape(comps * levels, -1)], axis=1)
        lon_all = gather(lon_packet, "lon")
        width = col_given.shape[1]
        partner = lon_all[:, :, :width].reshape(lon_count, comps * levels, lat_count, dons)
        partner = jnp.transpose(partner, (1, 2, 0, 3)).reshape(comps * levels, -1)
        side_cols = lon_all[:, :, width:].reshape(lon_count, comps, levels, 4, rows)
        up = lax.dynamic_index_in_dim(side_rows, jnp.maximum(lat_pos - 1, 0), keepdims=False)[:, :, 2:]
        down = lax.dynamic_index_in_dim(side_rows, jnp.minimum(lat_pos + 1, lat_count - 1), keepdims=False)[:, :, :2]
        left = lax.dynamic_index_in_dim(side_cols, jnp.maximum(lon_pos - 1, 0), keepdims=False)[:, :, 2:]
        right = lax.dynamic_index_in_dim(side_cols, jnp.minimum(lon_pos + 1, lon_count - 1), keepdims=False)[:, :, :2]
        rim = select(partner).reshape(comps, levels, -1)
        rim_lat = rim[:, :, :band].reshape(comps, levels, 2, cols)
        rim_lon = rim[:, :, band:].reshape(comps, levels, 2, rows)
        up = jnp.where(on_top, rim_lat, up).reshape(comps * levels, 2, cols)
        down = jnp.where(on_bottom, rim_lat, down).reshape(comps * levels, 2, cols)
        left = jnp.where(on_left, rim_lon, left).reshape(comps * levels, 2, rows)
        right = jnp.where(on_right, rim_lon, right).reshape(comps * levels, 2, rows)
        sides = jnp.pad(jnp.concatenate([left, right], axis=1), ((0, 0), (0, 0), (0, cols - rows)))
        return (jnp.concatenate([up, down, sides], axis=1),)

    field = state[0].reshape(comps * levels, rows, cols)
    turn_parts = jnp.concatenate([jnp.cos(donor_turn[0, 0]), jnp.sin(donor_turn[0, 0])])
    donation, lon_w, lat_w = first_donation(field, donor_cell[0, 0], donor_frac[0, 0, 0], turn_parts)
    section_one, donation = advance(field, *section(field, donation), field, lon_w, lat_w, turn_parts, True)
    new_field = advance(section_one, *section(section_one, donation), field, lon_w, lat_w, turn_parts, False)
    return new_field.reshape(1, comps, levels, rows, cols)


def solution(mesh):
    in_specs = (
        P("panel", None, None, "lat", "lon"),
        P("panel", "lat", "lon", None),
        P("panel", "lat", "lon", None),
        P("panel", "lat", "lon", None, None),
        P("panel", "lat", "lon", None),
    )
    out_specs = P("panel", None, None, "lat", "lon")
    return jax.shard_map(
        per_device, mesh=mesh, in_specs=in_specs, out_specs=out_specs, check_vma=False
    )
```

```python
import jax
import jax.numpy as jnp
from jax import lax
from jax.sharding import PartitionSpec as P
from jax.experimental import pallas as pl
from jax.experimental.pallas import tpu as pltpu
import functools

INTERPRET = False

viscosity = 0.05
resistivity = 0.05
diffusivity = 0.05
buoyancy = 0.5
time_step = 0.25

HIGHEST = lax.Precision.HIGHEST


def stencil_kernel(*refs, first):
    if first:
        f_ref, halo_ref, lon_ref, lat_ref, turn_ref, o_ref, don_ref = refs
    else:
        f_ref, halo_ref, base_ref, o_ref = refs
    planes, height, width = f_ref.shape
    comps = planes // 2
    row = lax.broadcasted_iota(jnp.int32, (height, width), 0)
    col = lax.broadcasted_iota(jnp.int32, (height, width), 1)
    tile = lax.broadcasted_iota(jnp.int32, (8, width), 0)

    eye = jnp.where(
        lax.broadcasted_iota(jnp.int32, (height, height), 0) == lax.broadcasted_iota(jnp.int32, (height, height), 1),
        1.0,
        0.0,
    )
    pick_row = lax.broadcasted_iota(jnp.int32, (width, height), 0)

    def columns(k):
        left = halo_ref[k, 4:6, 0:height]
        right = halo_ref[k, 6:8, 0:height]
        rows_of = jnp.where(
            pick_row == 0,
            left[0:1, :],
            jnp.where(pick_row == 1, left[1:2, :], jnp.where(pick_row == 2, right[0:1, :], jnp.where(pick_row == 3, right[1:2, :], 0.0))),
        )
        return lax.dot_general(
            eye, rows_of, (((1,), (1,)), ((), ())), precision=HIGHEST, preferred_element_type=jnp.float32
        )

    def terms(k):
        x = f_ref[k]
        up = halo_ref[k, 0:2, :]
        down = halo_ref[k, 2:4, :]
        sides = columns(k)
        left = sides[:, 0:2]
        right = sides[:, 2:4]
        rolled = pltpu.roll(x, 1, 0)
        lat_m1 = jnp.concatenate([jnp.where(tile == 0, up[1:2, :], rolled[:8]), rolled[8:]], axis=0)
        rolled = pltpu.roll(x, 2, 0)
        top = jnp.where(tile == 0, up[0:1, :], jnp.where(tile == 1, up[1:2, :], rolled[:8]))
        lat_m2 = jnp.concatenate([top, rolled[8:]], axis=0)
        rolled = pltpu.roll(x, height - 1, 0)
        lat_p1 = jnp.concatenate([rolled[: height - 8], jnp.where(tile == 7, down[0:1, :], rolled[height - 8 :])], axis=0)
        rolled = pltpu.roll(x, height - 2, 0)
        bottom = jnp.where(tile == 7, down[1:2, :], jnp.where(tile == 6, down[0:1, :], rolled[height - 8 :]))
        lat_p2 = jnp.concatenate([rolled[: height - 8], bottom], axis=0)
        lon_m1 = jnp.where(col == 0, left[:, 1:2], pltpu.roll(x, 1, 1))
        lon_m2 = jnp.where(col == 0, left[:, 0:1], jnp.where(col == 1, left[:, 1:2], pltpu.roll(x, 2, 1)))
        lon_p1 = jnp.where(col == width - 1, right[:, 0:1], pltpu.roll(x, width - 1, 1))
        lon_p2 = jnp.where(
            col == width - 1, right[:, 1:2], jnp.where(col == width - 2, right[:, 0:1], pltpu.roll(x, width - 2, 1))
        )
        d_lat = (8.0 * (lat_p1 - lat_m1) - (lat_p2 - lat_m2)) * (1.0 / 12.0)
        d_lon = (8.0 * (lon_p1 - lon_m1) - (lon_p2 - lon_m2)) * (1.0 / 12.0)
        lap = lat_p1 + lat_m1 + lon_p1 + lon_m1 - 4.0 * x
        return x, d_lat, d_lon, lap

    for level in range(2):
        def plane(c):
            return c * 2 + level

        def value(c):
            return f_ref[plane(c)]

        def lap_of(c, x, lap):
            above = f_ref[c * 2 + 1] if level == 0 else 0.0
            below = f_ref[c * 2] if level == 1 else 0.0
            return lap + above + below - 2.0 * x

        def store(c, x, rate):
            section = x + time_step * rate
            if first:
                o_ref[plane(c)] = section
            else:
                o_ref[plane(c)] = 0.5 * base_ref[plane(c)] + 0.5 * section

        u1, u2, u4, u5, u6 = value(1), value(2), value(4), value(5), value(6)
        for c in range(3):
            xa, lat_a, lon_a, lap_a = terms(plane(c))
            xb, lat_b, lon_b, lap_b = terms(plane(c + 3))
            adv_u_a = u1 * lat_a + u2 * lon_a
            adv_b_a = u4 * lat_a + u5 * lon_a
            adv_u_b = u1 * lat_b + u2 * lon_b
            adv_b_b = u4 * lat_b + u5 * lon_b
            rate_a = -adv_u_a + adv_b_b + viscosity * lap_of(c, xa, lap_a)
            if c == 0:
                rate_a = rate_a + buoyancy * u6
            rate_b = adv_b_a - adv_u_b + resistivity * lap_of(c + 3, xb, lap_b)
            store(c, xa, rate_a)
            store(c + 3, xb, rate_b)
        x6, lat_6, lon_6, lap_6 = terms(plane(6))
        adv_u_6 = u1 * lat_6 + u2 * lon_6
        store(6, x6, -adv_u_6 + diffusivity * lap_of(6, x6, lap_6))

    if first:
        donate_planes(o_ref[...], lon_ref[...], lat_ref[...], turn_ref, don_ref)


def advance(field, halo, base, lon, lat, turn, first):
    shape = jax.ShapeDtypeStruct(field.shape, field.dtype)
    if first:
        shape = (shape, jax.ShapeDtypeStruct((field.shape[0], lon.shape[1]), jnp.float32))
    return pl.pallas_call(
        functools.partial(stencil_kernel, first=first),
        out_shape=shape,
        interpret=INTERPRET,
    )(*((field, halo, lon, lat, turn) if first else (field, halo, base)))


def donation_weights(cells_ref, frac_ref, rows, cols):
    dons = cells_ref.shape[1]
    cell = cells_ref[...].astype(jnp.float32)
    row = jnp.floor((cell + 0.5) * (1.0 / (cols - 1)))
    col = cell - row * (cols - 1)
    row = row.astype(jnp.int32)
    col = col.astype(jnp.int32)
    frac_t = frac_ref[0:1, :]
    frac_p = frac_ref[1:2, :]
    col_ids = lax.broadcasted_iota(jnp.int32, (cols, dons), 0)
    row_ids = lax.broadcasted_iota(jnp.int32, (rows, dons), 0)
    weight_lon = jnp.where(col_ids == col, 1.0 - frac_p, 0.0) + jnp.where(col_ids == col + 1, frac_p, 0.0)
    weight_lat = jnp.where(row_ids == row, 1.0 - frac_t, 0.0) + jnp.where(row_ids == row + 1, frac_t, 0.0)
    return weight_lon, weight_lat


def donate_planes(field, weight_lon, weight_lat, turn_ref, out_ref):
    planes, rows, cols = field.shape
    cosine = turn_ref[0:1, :]
    sine = turn_ref[1:2, :]
    along = jnp.dot(field.reshape(planes * rows, cols), weight_lon, precision=HIGHEST, preferred_element_type=jnp.float32)
    values = []
    for k in range(planes):
        values.append(jnp.sum(along[k * rows : (k + 1) * rows] * weight_lat, axis=0, keepdims=True))
    for k in range(planes):
        comp, level = divmod(k, 2)
        if comp in (1, 4):
            value = cosine * values[k] - sine * values[k + 2]
        elif comp in (2, 5):
            value = sine * values[k - 2] + cosine * values[k]
        else:
            value = values[k]
        out_ref[k : k + 1, :] = value


def donation_kernel(f_ref, cells_ref, frac_ref, turn_ref, out_ref, lon_ref, lat_ref):
    planes, rows, cols = f_ref.shape
    weight_lon, weight_lat = donation_weights(cells_ref, frac_ref, rows, cols)
    lon_ref[...] = weight_lon
    lat_ref[...] = weight_lat
    donate_planes(f_ref[...], weight_lon, weight_lat, turn_ref, out_ref)


def first_donation(field, cells, frac, turn):
    planes, rows, cols = field.shape
    dons = cells.shape[1]
    return pl.pallas_call(
        donation_kernel,
        out_shape=(
            jax.ShapeDtypeStruct((planes, dons), jnp.float32),
            jax.ShapeDtypeStruct((cols, dons), jnp.float32),
            jax.ShapeDtypeStruct((rows, dons), jnp.float32),
        ),
        interpret=INTERPRET,
    )(field, cells, frac, turn)


def rotate(values, turn):
    cosine = jnp.cos(turn)
    sine = jnp.sin(turn)
    parts = [
        values[0],
        cosine * values[1] - sine * values[2],
        sine * values[1] + cosine * values[2],
        values[3],
        cosine * values[4] - sine * values[5],
        sine * values[4] + cosine * values[5],
        values[6],
    ]
    return jnp.stack(parts)


def per_device(state, source_slot, donor_cell, donor_frac, donor_turn):
    comps = state.shape[1]
    levels = state.shape[2]
    rows = state.shape[3]
    cols = state.shape[4]
    cells = donor_cell[0, 0, 0]
    frac_t = donor_frac[0, 0, 0, 0]
    frac_p = donor_frac[0, 0, 0, 1]
    turn = donor_turn[0, 0, 0]
    slots = source_slot[0, 0, 0]
    lat_pos = lax.axis_index("lat")
    lon_pos = lax.axis_index("lon")
    lat_count = lax.axis_size("lat")
    lon_count = lax.axis_size("lon")
    on_top = lat_pos == 0
    on_bottom = lat_pos == lat_count - 1
    on_left = lon_pos == 0
    on_right = lon_pos == lon_count - 1

    band = 2 * cols
    side = 2 * rows
    lat_slots = jnp.where(on_top, slots[0:band], slots[band : 2 * band])
    lon_slots = jnp.where(on_left, slots[2 * band : 2 * band + side], slots[2 * band + side :])
    wanted = jnp.concatenate([lat_slots, lon_slots])
    total = lat_count * lon_count * cells.shape[0]
    pick = (jnp.arange(total, dtype=jnp.int32)[:, None] == wanted[None, :]).astype(jnp.bfloat16)

    def select(values):
        high = lax.reduce_precision(values, exponent_bits=8, mantissa_bits=7)
        rest = values - high
        middle = lax.reduce_precision(rest, exponent_bits=8, mantissa_bits=7)
        low = rest - middle
        parts = jnp.concatenate([high, middle, low]).astype(jnp.bfloat16)
        picked = jnp.dot(parts, pick, preferred_element_type=jnp.float32)
        count = values.shape[0]
        return picked[:count] + (picked[count : 2 * count] + picked[2 * count :])

    def gather(packet, axis):
        size = lax.axis_size(axis)
        pos = lax.axis_index(axis)
        held = packet[None]
        k = 1
        while k < size:
            other = lax.ppermute(held, axis, [(i, i ^ k) for i in range(size)])
            low = (pos // k) % 2 == 0
            held = jnp.where(low, jnp.concatenate([held, other]), jnp.concatenate([other, held]))
            k *= 2
        return held

    def section(field, donation):
        flat = field
        given = lax.ppermute(donation, "panel", [(0, 1), (1, 0)])
        dons = given.shape[1]
        side_rows = jnp.concatenate([flat[:, :2, :], flat[:, rows - 2 :, :]], axis=1)
        lat_packet = jnp.concatenate([given, side_rows.reshape(comps * levels, -1)], axis=1)
        lat_all = gather(lat_packet, "lat")
        col_given = jnp.transpose(lat_all[:, :, :dons], (1, 0, 2)).reshape(comps * levels, -1)
        side_rows = lat_all[:, :, dons:].reshape(lat_count, comps, levels, 4, cols)
        side_cols = jnp.concatenate([flat[:, :, :2], flat[:, :, cols - 2 :]], axis=2)
        side_cols = jnp.swapaxes(side_cols, 1, 2)
        lon_packet = jnp.concatenate([col_given, side_cols.reshape(comps * levels, -1)], axis=1)
        lon_all = gather(lon_packet, "lon")
        width = col_given.shape[1]
        partner = lon_all[:, :, :width].reshape(lon_count, comps * levels, lat_count, dons)
        partner = jnp.transpose(partner, (1, 2, 0, 3)).reshape(comps * levels, -1)
        side_cols = lon_all[:, :, width:].reshape(lon_count, comps, levels, 4, rows)
        up = lax.dynamic_index_in_dim(side_rows, jnp.maximum(lat_pos - 1, 0), keepdims=False)[:, :, 2:]
        down = lax.dynamic_index_in_dim(side_rows, jnp.minimum(lat_pos + 1, lat_count - 1), keepdims=False)[:, :, :2]
        left = lax.dynamic_index_in_dim(side_cols, jnp.maximum(lon_pos - 1, 0), keepdims=False)[:, :, 2:]
        right = lax.dynamic_index_in_dim(side_cols, jnp.minimum(lon_pos + 1, lon_count - 1), keepdims=False)[:, :, :2]
        rim = select(partner).reshape(comps, levels, -1)
        rim_lat = rim[:, :, :band].reshape(comps, levels, 2, cols)
        rim_lon = rim[:, :, band:].reshape(comps, levels, 2, rows)
        up = jnp.where(on_top, rim_lat, up).reshape(comps * levels, 2, cols)
        down = jnp.where(on_bottom, rim_lat, down).reshape(comps * levels, 2, cols)
        left = jnp.where(on_left, rim_lon, left).reshape(comps * levels, 2, rows)
        right = jnp.where(on_right, rim_lon, right).reshape(comps * levels, 2, rows)
        sides = jnp.pad(jnp.concatenate([left, right], axis=1), ((0, 0), (0, 0), (0, cols - rows)))
        return (jnp.concatenate([up, down, sides], axis=1),)

    field = state[0].reshape(comps * levels, rows, cols)
    turn_parts = jnp.concatenate([jnp.cos(donor_turn[0, 0]), jnp.sin(donor_turn[0, 0])])
    donation, lon_w, lat_w = first_donation(field, donor_cell[0, 0], donor_frac[0, 0, 0], turn_parts)
    section_one, donation = advance(field, *section(field, donation), field, lon_w, lat_w, turn_parts, True)
    new_field = advance(section_one, *section(section_one, donation), field, lon_w, lat_w, turn_parts, False)
    return new_field.reshape(1, comps, levels, rows, cols)


def solution(mesh):
    in_specs = (
        P("panel", None, None, "lat", "lon"),
        P("panel", "lat", "lon", None),
        P("panel", "lat", "lon", None),
        P("panel", "lat", "lon", None, None),
        P("panel", "lat", "lon", None),
    )
    out_specs = P("panel", None, None, "lat", "lon")
    return jax.shard_map(
        per_device, mesh=mesh, in_specs=in_specs, out_specs=out_specs, check_vma=False
    )
```

```python
import jax
import jax.numpy as jnp
from jax import lax
from jax.sharding import PartitionSpec as P
from jax.experimental import pallas as pl
from jax.experimental.pallas import tpu as pltpu
import functools

INTERPRET = False

viscosity = 0.05
resistivity = 0.05
diffusivity = 0.05
buoyancy = 0.5
time_step = 0.25

HIGHEST = lax.Precision.HIGHEST


def stencil_kernel(*refs, first):
    if first:
        f_ref, halo_ref, lon_ref, lat_ref, turn_ref, o_ref, don_ref = refs
    else:
        f_ref, halo_ref, base_ref, o_ref = refs
    planes, height, width = f_ref.shape
    comps = planes // 2
    row = lax.broadcasted_iota(jnp.int32, (height, width), 0)
    col = lax.broadcasted_iota(jnp.int32, (height, width), 1)
    tile = lax.broadcasted_iota(jnp.int32, (8, width), 0)

    eye = jnp.where(
        lax.broadcasted_iota(jnp.int32, (height, height), 0) == lax.broadcasted_iota(jnp.int32, (height, height), 1),
        1.0,
        0.0,
    )
    pick_row = lax.broadcasted_iota(jnp.int32, (width, height), 0)

    def columns(k):
        left = halo_ref[k, 4:6, 0:height]
        right = halo_ref[k, 6:8, 0:height]
        rows_of = jnp.where(
            pick_row == 0,
            left[0:1, :],
            jnp.where(pick_row == 1, left[1:2, :], jnp.where(pick_row == 2, right[0:1, :], jnp.where(pick_row == 3, right[1:2, :], 0.0))),
        )
        return lax.dot_general(
            eye, rows_of, (((1,), (1,)), ((), ())), precision=HIGHEST, preferred_element_type=jnp.float32
        )

    def terms(k):
        x = f_ref[k]
        up = halo_ref[k, 0:2, :]
        down = halo_ref[k, 2:4, :]
        sides = columns(k)
        left = sides[:, 0:2]
        right = sides[:, 2:4]
        rolled = pltpu.roll(x, 1, 0)
        lat_m1 = jnp.concatenate([jnp.where(tile == 0, up[1:2, :], rolled[:8]), rolled[8:]], axis=0)
        rolled = pltpu.roll(x, 2, 0)
        top = jnp.where(tile == 0, up[0:1, :], jnp.where(tile == 1, up[1:2, :], rolled[:8]))
        lat_m2 = jnp.concatenate([top, rolled[8:]], axis=0)
        rolled = pltpu.roll(x, height - 1, 0)
        lat_p1 = jnp.concatenate([rolled[: height - 8], jnp.where(tile == 7, down[0:1, :], rolled[height - 8 :])], axis=0)
        rolled = pltpu.roll(x, height - 2, 0)
        bottom = jnp.where(tile == 7, down[1:2, :], jnp.where(tile == 6, down[0:1, :], rolled[height - 8 :]))
        lat_p2 = jnp.concatenate([rolled[: height - 8], bottom], axis=0)
        lon_m1 = jnp.where(col == 0, left[:, 1:2], pltpu.roll(x, 1, 1))
        lon_m2 = jnp.where(col == 0, left[:, 0:1], jnp.where(col == 1, left[:, 1:2], pltpu.roll(x, 2, 1)))
        lon_p1 = jnp.where(col == width - 1, right[:, 0:1], pltpu.roll(x, width - 1, 1))
        lon_p2 = jnp.where(
            col == width - 1, right[:, 1:2], jnp.where(col == width - 2, right[:, 0:1], pltpu.roll(x, width - 2, 1))
        )
        d_lat = (8.0 * (lat_p1 - lat_m1) - (lat_p2 - lat_m2)) * (1.0 / 12.0)
        d_lon = (8.0 * (lon_p1 - lon_m1) - (lon_p2 - lon_m2)) * (1.0 / 12.0)
        lap = lat_p1 + lat_m1 + lon_p1 + lon_m1 - 4.0 * x
        return x, d_lat, d_lon, lap

    for level in range(2):
        def plane(c):
            return c * 2 + level

        def value(c):
            return f_ref[plane(c)]

        def lap_of(c, x, lap):
            above = f_ref[c * 2 + 1] if level == 0 else 0.0
            below = f_ref[c * 2] if level == 1 else 0.0
            return lap + above + below - 2.0 * x

        def store(c, x, rate):
            section = x + time_step * rate
            if first:
                o_ref[plane(c)] = section
            else:
                o_ref[plane(c)] = 0.5 * base_ref[plane(c)] + 0.5 * section

        u1, u2, u4, u5, u6 = value(1), value(2), value(4), value(5), value(6)
        for c in range(3):
            xa, lat_a, lon_a, lap_a = terms(plane(c))
            xb, lat_b, lon_b, lap_b = terms(plane(c + 3))
            adv_u_a = u1 * lat_a + u2 * lon_a
            adv_b_a = u4 * lat_a + u5 * lon_a
            adv_u_b = u1 * lat_b + u2 * lon_b
            adv_b_b = u4 * lat_b + u5 * lon_b
            rate_a = -adv_u_a + adv_b_b + viscosity * lap_of(c, xa, lap_a)
            if c == 0:
                rate_a = rate_a + buoyancy * u6
            rate_b = adv_b_a - adv_u_b + resistivity * lap_of(c + 3, xb, lap_b)
            store(c, xa, rate_a)
            store(c + 3, xb, rate_b)
        x6, lat_6, lon_6, lap_6 = terms(plane(6))
        adv_u_6 = u1 * lat_6 + u2 * lon_6
        store(6, x6, -adv_u_6 + diffusivity * lap_of(6, x6, lap_6))

    if first:
        donate_planes(lambda k: o_ref[k], planes, lon_ref[...], lat_ref[...], turn_ref, don_ref)


def advance(field, halo, base, lon, lat, turn, first):
    shape = jax.ShapeDtypeStruct(field.shape, field.dtype)
    if first:
        shape = (shape, jax.ShapeDtypeStruct((field.shape[0], lon.shape[1]), jnp.float32))
    return pl.pallas_call(
        functools.partial(stencil_kernel, first=first),
        out_shape=shape,
        interpret=INTERPRET,
    )(*((field, halo, lon, lat, turn) if first else (field, halo, base)))


def donation_weights(cells_ref, frac_ref, rows, cols):
    dons = cells_ref.shape[1]
    cell = cells_ref[...].astype(jnp.float32)
    row = jnp.floor((cell + 0.5) * (1.0 / (cols - 1)))
    col = cell - row * (cols - 1)
    row = row.astype(jnp.int32)
    col = col.astype(jnp.int32)
    frac_t = frac_ref[0:1, :]
    frac_p = frac_ref[1:2, :]
    col_ids = lax.broadcasted_iota(jnp.int32, (cols, dons), 0)
    row_ids = lax.broadcasted_iota(jnp.int32, (rows, dons), 0)
    weight_lon = jnp.where(col_ids == col, 1.0 - frac_p, 0.0) + jnp.where(col_ids == col + 1, frac_p, 0.0)
    weight_lat = jnp.where(row_ids == row, 1.0 - frac_t, 0.0) + jnp.where(row_ids == row + 1, frac_t, 0.0)
    return weight_lon, weight_lat


def donate_planes(plane_of, planes, weight_lon, weight_lat, turn_ref, out_ref):
    cosine = turn_ref[0:1, :]
    sine = turn_ref[1:2, :]
    values = []
    for k in range(planes):
        along = jnp.dot(plane_of(k), weight_lon, precision=HIGHEST, preferred_element_type=jnp.float32)
        values.append(jnp.sum(along * weight_lat, axis=0, keepdims=True))
    for k in range(planes):
        comp, level = divmod(k, 2)
        if comp in (1, 4):
            value = cosine * values[k] - sine * values[k + 2]
        elif comp in (2, 5):
            value = sine * values[k - 2] + cosine * values[k]
        else:
            value = values[k]
        out_ref[k : k + 1, :] = value


def donation_kernel(f_ref, cells_ref, frac_ref, angle_ref, out_ref, lon_ref, lat_ref, turn_ref):
    angle = angle_ref[...]
    turn_ref[0:1, :] = jnp.cos(angle)
    turn_ref[1:2, :] = jnp.sin(angle)
    planes, rows, cols = f_ref.shape
    weight_lon, weight_lat = donation_weights(cells_ref, frac_ref, rows, cols)
    lon_ref[...] = weight_lon
    lat_ref[...] = weight_lat
    donate_planes(lambda k: f_ref[k], planes, weight_lon, weight_lat, turn_ref, out_ref)


def first_donation(field, cells, frac, turn):
    planes, rows, cols = field.shape
    dons = cells.shape[1]
    return pl.pallas_call(
        donation_kernel,
        out_shape=(
            jax.ShapeDtypeStruct((planes, dons), jnp.float32),
            jax.ShapeDtypeStruct((cols, dons), jnp.float32),
            jax.ShapeDtypeStruct((rows, dons), jnp.float32),
            jax.ShapeDtypeStruct((2, dons), jnp.float32),
        ),
        interpret=INTERPRET,
    )(field, cells, frac, turn)


def rotate(values, turn):
    cosine = jnp.cos(turn)
    sine = jnp.sin(turn)
    parts = [
        values[0],
        cosine * values[1] - sine * values[2],
        sine * values[1] + cosine * values[2],
        values[3],
        cosine * values[4] - sine * values[5],
        sine * values[4] + cosine * values[5],
        values[6],
    ]
    return jnp.stack(parts)


def per_device(state, source_slot, donor_cell, donor_frac, donor_turn):
    comps = state.shape[1]
    levels = state.shape[2]
    rows = state.shape[3]
    cols = state.shape[4]
    cells = donor_cell[0, 0, 0]
    frac_t = donor_frac[0, 0, 0, 0]
    frac_p = donor_frac[0, 0, 0, 1]
    turn = donor_turn[0, 0, 0]
    slots = source_slot[0, 0, 0]
    lat_pos = lax.axis_index("lat")
    lon_pos = lax.axis_index("lon")
    lat_count = lax.axis_size("lat")
    lon_count = lax.axis_size("lon")
    on_top = lat_pos == 0
    on_bottom = lat_pos == lat_count - 1
    on_left = lon_pos == 0
    on_right = lon_pos == lon_count - 1

    band = 2 * cols
    side = 2 * rows
    lat_slots = jnp.where(on_top, slots[0:band], slots[band : 2 * band])
    lon_slots = jnp.where(on_left, slots[2 * band : 2 * band + side], slots[2 * band + side :])
    wanted = jnp.concatenate([lat_slots, lon_slots])
    total = lat_count * lon_count * cells.shape[0]
    pick = (jnp.arange(total, dtype=jnp.int32)[:, None] == wanted[None, :]).astype(jnp.bfloat16)

    def select(values):
        high = lax.reduce_precision(values, exponent_bits=8, mantissa_bits=7)
        rest = values - high
        middle = lax.reduce_precision(rest, exponent_bits=8, mantissa_bits=7)
        low = rest - middle
        parts = jnp.concatenate([high, middle, low]).astype(jnp.bfloat16)
        picked = jnp.dot(parts, pick, preferred_element_type=jnp.float32)
        count = values.shape[0]
        return picked[:count] + (picked[count : 2 * count] + picked[2 * count :])

    def gather(packet, axis):
        size = lax.axis_size(axis)
        pos = lax.axis_index(axis)
        held = packet[None]
        k = 1
        while k < size:
            other = lax.ppermute(held, axis, [(i, i ^ k) for i in range(size)])
            low = (pos // k) % 2 == 0
            held = jnp.where(low, jnp.concatenate([held, other]), jnp.concatenate([other, held]))
            k *= 2
        return held

    def section(field, donation):
        flat = field
        given = lax.ppermute(donation, "panel", [(0, 1), (1, 0)])
        dons = given.shape[1]
        side_rows = jnp.concatenate([flat[:, :2, :], flat[:, rows - 2 :, :]], axis=1)
        lat_packet = jnp.concatenate([given, side_rows.reshape(comps * levels, -1)], axis=1)
        lat_all = gather(lat_packet, "lat")
        col_given = jnp.transpose(lat_all[:, :, :dons], (1, 0, 2)).reshape(comps * levels, -1)
        side_rows = lat_all[:, :, dons:].reshape(lat_count, comps, levels, 4, cols)
        side_cols = jnp.concatenate([flat[:, :, :2], flat[:, :, cols - 2 :]], axis=2)
        side_cols = jnp.swapaxes(side_cols, 1, 2)
        lon_packet = jnp.concatenate([col_given, side_cols.reshape(comps * levels, -1)], axis=1)
        lon_all = gather(lon_packet, "lon")
        width = col_given.shape[1]
        partner = lon_all[:, :, :width].reshape(lon_count, comps * levels, lat_count, dons)
        partner = jnp.transpose(partner, (1, 2, 0, 3)).reshape(comps * levels, -1)
        side_cols = lon_all[:, :, width:].reshape(lon_count, comps, levels, 4, rows)
        up = lax.dynamic_index_in_dim(side_rows, jnp.maximum(lat_pos - 1, 0), keepdims=False)[:, :, 2:]
        down = lax.dynamic_index_in_dim(side_rows, jnp.minimum(lat_pos + 1, lat_count - 1), keepdims=False)[:, :, :2]
        left = lax.dynamic_index_in_dim(side_cols, jnp.maximum(lon_pos - 1, 0), keepdims=False)[:, :, 2:]
        right = lax.dynamic_index_in_dim(side_cols, jnp.minimum(lon_pos + 1, lon_count - 1), keepdims=False)[:, :, :2]
        rim = select(partner).reshape(comps, levels, -1)
        rim_lat = rim[:, :, :band].reshape(comps, levels, 2, cols)
        rim_lon = rim[:, :, band:].reshape(comps, levels, 2, rows)
        up = jnp.where(on_top, rim_lat, up).reshape(comps * levels, 2, cols)
        down = jnp.where(on_bottom, rim_lat, down).reshape(comps * levels, 2, cols)
        left = jnp.where(on_left, rim_lon, left).reshape(comps * levels, 2, rows)
        right = jnp.where(on_right, rim_lon, right).reshape(comps * levels, 2, rows)
        sides = jnp.pad(jnp.concatenate([left, right], axis=1), ((0, 0), (0, 0), (0, cols - rows)))
        return (jnp.concatenate([up, down, sides], axis=1),)

    field = state[0].reshape(comps * levels, rows, cols)
    donation, lon_w, lat_w, turn_parts = first_donation(field, donor_cell[0, 0], donor_frac[0, 0, 0], donor_turn[0, 0])
    section_one, donation = advance(field, *section(field, donation), field, lon_w, lat_w, turn_parts, True)
    new_field = advance(section_one, *section(section_one, donation), field, lon_w, lat_w, turn_parts, False)
    return new_field.reshape(1, comps, levels, rows, cols)


def solution(mesh):
    in_specs = (
        P("panel", None, None, "lat", "lon"),
        P("panel", "lat", "lon", None),
        P("panel", "lat", "lon", None),
        P("panel", "lat", "lon", None, None),
        P("panel", "lat", "lon", None),
    )
    out_specs = P("panel", None, None, "lat", "lon")
    return jax.shard_map(
        per_device, mesh=mesh, in_specs=in_specs, out_specs=out_specs, check_vma=False
    )
```

```python
import jax
import jax.numpy as jnp
from jax import lax
from jax.sharding import PartitionSpec as P
from jax.experimental import pallas as pl
from jax.experimental.pallas import tpu as pltpu
import functools

INTERPRET = False

viscosity = 0.05
resistivity = 0.05
diffusivity = 0.05
buoyancy = 0.5
time_step = 0.25

HIGHEST = lax.Precision.HIGHEST


def stencil_kernel(*refs, first):
    if first:
        f_ref, halo_ref, lon_ref, lat_ref, turn_ref, o_ref, don_ref, rows_ref = refs
    else:
        f_ref, halo_ref, base_ref, o_ref = refs
    planes, height, width = f_ref.shape
    comps = planes // 2
    row = lax.broadcasted_iota(jnp.int32, (height, width), 0)
    col = lax.broadcasted_iota(jnp.int32, (height, width), 1)
    tile = lax.broadcasted_iota(jnp.int32, (8, width), 0)

    eye = jnp.where(
        lax.broadcasted_iota(jnp.int32, (height, height), 0) == lax.broadcasted_iota(jnp.int32, (height, height), 1),
        1.0,
        0.0,
    )
    pick_row = lax.broadcasted_iota(jnp.int32, (width, height), 0)

    def columns(k):
        left = halo_ref[k, 4:6, 0:height]
        right = halo_ref[k, 6:8, 0:height]
        rows_of = jnp.where(
            pick_row == 0,
            left[0:1, :],
            jnp.where(pick_row == 1, left[1:2, :], jnp.where(pick_row == 2, right[0:1, :], jnp.where(pick_row == 3, right[1:2, :], 0.0))),
        )
        return lax.dot_general(
            eye, rows_of, (((1,), (1,)), ((), ())), precision=HIGHEST, preferred_element_type=jnp.float32
        )

    def terms(k):
        x = f_ref[k]
        up = halo_ref[k, 0:2, :]
        down = halo_ref[k, 2:4, :]
        sides = columns(k)
        left = sides[:, 0:2]
        right = sides[:, 2:4]
        rolled = pltpu.roll(x, 1, 0)
        lat_m1 = jnp.concatenate([jnp.where(tile == 0, up[1:2, :], rolled[:8]), rolled[8:]], axis=0)
        rolled = pltpu.roll(x, 2, 0)
        top = jnp.where(tile == 0, up[0:1, :], jnp.where(tile == 1, up[1:2, :], rolled[:8]))
        lat_m2 = jnp.concatenate([top, rolled[8:]], axis=0)
        rolled = pltpu.roll(x, height - 1, 0)
        lat_p1 = jnp.concatenate([rolled[: height - 8], jnp.where(tile == 7, down[0:1, :], rolled[height - 8 :])], axis=0)
        rolled = pltpu.roll(x, height - 2, 0)
        bottom = jnp.where(tile == 7, down[1:2, :], jnp.where(tile == 6, down[0:1, :], rolled[height - 8 :]))
        lat_p2 = jnp.concatenate([rolled[: height - 8], bottom], axis=0)
        lon_m1 = jnp.where(col == 0, left[:, 1:2], pltpu.roll(x, 1, 1))
        lon_m2 = jnp.where(col == 0, left[:, 0:1], jnp.where(col == 1, left[:, 1:2], pltpu.roll(x, 2, 1)))
        lon_p1 = jnp.where(col == width - 1, right[:, 0:1], pltpu.roll(x, width - 1, 1))
        lon_p2 = jnp.where(
            col == width - 1, right[:, 1:2], jnp.where(col == width - 2, right[:, 0:1], pltpu.roll(x, width - 2, 1))
        )
        d_lat = (8.0 * (lat_p1 - lat_m1) - (lat_p2 - lat_m2)) * (1.0 / 12.0)
        d_lon = (8.0 * (lon_p1 - lon_m1) - (lon_p2 - lon_m2)) * (1.0 / 12.0)
        lap = lat_p1 + lat_m1 + lon_p1 + lon_m1 - 4.0 * x
        return x, d_lat, d_lon, lap

    for level in range(2):
        def plane(c):
            return c * 2 + level

        def value(c):
            return f_ref[plane(c)]

        def lap_of(c, x, lap):
            above = f_ref[c * 2 + 1] if level == 0 else 0.0
            below = f_ref[c * 2] if level == 1 else 0.0
            return lap + above + below - 2.0 * x

        def store(c, x, rate):
            section = x + time_step * rate
            if first:
                o_ref[plane(c)] = section
                k = plane(c)
                for slot, line in enumerate((0, 1, height - 2, height - 1)):
                    rows_ref[k : k + 1, slot * width : (slot + 1) * width] = section[line : line + 1, :]
            else:
                o_ref[plane(c)] = 0.5 * base_ref[plane(c)] + 0.5 * section

        u1, u2, u4, u5, u6 = value(1), value(2), value(4), value(5), value(6)
        for c in range(3):
            xa, lat_a, lon_a, lap_a = terms(plane(c))
            xb, lat_b, lon_b, lap_b = terms(plane(c + 3))
            adv_u_a = u1 * lat_a + u2 * lon_a
            adv_b_a = u4 * lat_a + u5 * lon_a
            adv_u_b = u1 * lat_b + u2 * lon_b
            adv_b_b = u4 * lat_b + u5 * lon_b
            rate_a = -adv_u_a + adv_b_b + viscosity * lap_of(c, xa, lap_a)
            if c == 0:
                rate_a = rate_a + buoyancy * u6
            rate_b = adv_b_a - adv_u_b + resistivity * lap_of(c + 3, xb, lap_b)
            store(c, xa, rate_a)
            store(c + 3, xb, rate_b)
        x6, lat_6, lon_6, lap_6 = terms(plane(6))
        adv_u_6 = u1 * lat_6 + u2 * lon_6
        store(6, x6, -adv_u_6 + diffusivity * lap_of(6, x6, lap_6))

    if first:
        donate_planes(lambda k: o_ref[k], planes, lon_ref[...], lat_ref[...], turn_ref, don_ref)


def advance(field, halo, base, lon, lat, turn, first):
    shape = jax.ShapeDtypeStruct(field.shape, field.dtype)
    if first:
        shape = (
            shape,
            jax.ShapeDtypeStruct((field.shape[0], lon.shape[1]), jnp.float32),
            jax.ShapeDtypeStruct((field.shape[0], 4 * field.shape[2]), jnp.float32),
        )
    return pl.pallas_call(
        functools.partial(stencil_kernel, first=first),
        out_shape=shape,
        interpret=INTERPRET,
    )(*((field, halo, lon, lat, turn) if first else (field, halo, base)))


def donation_weights(cells_ref, frac_ref, rows, cols):
    dons = cells_ref.shape[1]
    cell = cells_ref[...].astype(jnp.float32)
    row = jnp.floor((cell + 0.5) * (1.0 / (cols - 1)))
    col = cell - row * (cols - 1)
    row = row.astype(jnp.int32)
    col = col.astype(jnp.int32)
    frac_t = frac_ref[0:1, :]
    frac_p = frac_ref[1:2, :]
    col_ids = lax.broadcasted_iota(jnp.int32, (cols, dons), 0)
    row_ids = lax.broadcasted_iota(jnp.int32, (rows, dons), 0)
    weight_lon = jnp.where(col_ids == col, 1.0 - frac_p, 0.0) + jnp.where(col_ids == col + 1, frac_p, 0.0)
    weight_lat = jnp.where(row_ids == row, 1.0 - frac_t, 0.0) + jnp.where(row_ids == row + 1, frac_t, 0.0)
    return weight_lon, weight_lat


def donate_planes(plane_of, planes, weight_lon, weight_lat, turn_ref, out_ref):
    cosine = turn_ref[0:1, :]
    sine = turn_ref[1:2, :]
    values = []
    for k in range(planes):
        along = jnp.dot(plane_of(k), weight_lon, precision=HIGHEST, preferred_element_type=jnp.float32)
        values.append(jnp.sum(along * weight_lat, axis=0, keepdims=True))
    for k in range(planes):
        comp, level = divmod(k, 2)
        if comp in (1, 4):
            value = cosine * values[k] - sine * values[k + 2]
        elif comp in (2, 5):
            value = sine * values[k - 2] + cosine * values[k]
        else:
            value = values[k]
        out_ref[k : k + 1, :] = value


def donation_kernel(f_ref, cells_ref, frac_ref, angle_ref, out_ref, lon_ref, lat_ref, turn_ref):
    angle = angle_ref[...]
    turn_ref[0:1, :] = jnp.cos(angle)
    turn_ref[1:2, :] = jnp.sin(angle)
    planes, rows, cols = f_ref.shape
    weight_lon, weight_lat = donation_weights(cells_ref, frac_ref, rows, cols)
    lon_ref[...] = weight_lon
    lat_ref[...] = weight_lat
    donate_planes(lambda k: f_ref[k], planes, weight_lon, weight_lat, turn_ref, out_ref)


def first_donation(field, cells, frac, turn):
    planes, rows, cols = field.shape
    dons = cells.shape[1]
    return pl.pallas_call(
        donation_kernel,
        out_shape=(
            jax.ShapeDtypeStruct((planes, dons), jnp.float32),
            jax.ShapeDtypeStruct((cols, dons), jnp.float32),
            jax.ShapeDtypeStruct((rows, dons), jnp.float32),
            jax.ShapeDtypeStruct((2, dons), jnp.float32),
        ),
        interpret=INTERPRET,
    )(field, cells, frac, turn)


def rotate(values, turn):
    cosine = jnp.cos(turn)
    sine = jnp.sin(turn)
    parts = [
        values[0],
        cosine * values[1] - sine * values[2],
        sine * values[1] + cosine * values[2],
        values[3],
        cosine * values[4] - sine * values[5],
        sine * values[4] + cosine * values[5],
        values[6],
    ]
    return jnp.stack(parts)


def per_device(state, source_slot, donor_cell, donor_frac, donor_turn):
    comps = state.shape[1]
    levels = state.shape[2]
    rows = state.shape[3]
    cols = state.shape[4]
    cells = donor_cell[0, 0, 0]
    frac_t = donor_frac[0, 0, 0, 0]
    frac_p = donor_frac[0, 0, 0, 1]
    turn = donor_turn[0, 0, 0]
    slots = source_slot[0, 0, 0]
    lat_pos = lax.axis_index("lat")
    lon_pos = lax.axis_index("lon")
    lat_count = lax.axis_size("lat")
    lon_count = lax.axis_size("lon")
    on_top = lat_pos == 0
    on_bottom = lat_pos == lat_count - 1
    on_left = lon_pos == 0
    on_right = lon_pos == lon_count - 1

    band = 2 * cols
    side = 2 * rows
    lat_slots = jnp.where(on_top, slots[0:band], slots[band : 2 * band])
    lon_slots = jnp.where(on_left, slots[2 * band : 2 * band + side], slots[2 * band + side :])
    wanted = jnp.concatenate([lat_slots, lon_slots])
    total = lat_count * lon_count * cells.shape[0]
    pick = (jnp.arange(total, dtype=jnp.int32)[:, None] == wanted[None, :]).astype(jnp.bfloat16)

    def select(values):
        high = lax.reduce_precision(values, exponent_bits=8, mantissa_bits=7)
        rest = values - high
        middle = lax.reduce_precision(rest, exponent_bits=8, mantissa_bits=7)
        low = rest - middle
        parts = jnp.concatenate([high, middle, low]).astype(jnp.bfloat16)
        picked = jnp.dot(parts, pick, preferred_element_type=jnp.float32)
        count = values.shape[0]
        return picked[:count] + (picked[count : 2 * count] + picked[2 * count :])

    def gather(packet, axis):
        size = lax.axis_size(axis)
        pos = lax.axis_index(axis)
        held = packet[None]
        k = 1
        while k < size:
            other = lax.ppermute(held, axis, [(i, i ^ k) for i in range(size)])
            low = (pos // k) % 2 == 0
            held = jnp.where(low, jnp.concatenate([held, other]), jnp.concatenate([other, held]))
            k *= 2
        return held

    def section(field, donation, edge_rows=None):
        flat = field
        given = lax.ppermute(donation, "panel", [(0, 1), (1, 0)])
        dons = given.shape[1]
        if edge_rows is None:
            edge_rows = jnp.concatenate([flat[:, :2, :], flat[:, rows - 2 :, :]], axis=1).reshape(comps * levels, -1)
        lat_packet = jnp.concatenate([given, edge_rows], axis=1)
        lat_all = gather(lat_packet, "lat")
        col_given = jnp.transpose(lat_all[:, :, :dons], (1, 0, 2)).reshape(comps * levels, -1)
        side_rows = lat_all[:, :, dons:].reshape(lat_count, comps, levels, 4, cols)
        side_cols = jnp.concatenate([flat[:, :, :2], flat[:, :, cols - 2 :]], axis=2)
        side_cols = jnp.swapaxes(side_cols, 1, 2)
        lon_packet = jnp.concatenate([col_given, side_cols.reshape(comps * levels, -1)], axis=1)
        lon_all = gather(lon_packet, "lon")
        width = col_given.shape[1]
        partner = lon_all[:, :, :width].reshape(lon_count, comps * levels, lat_count, dons)
        partner = jnp.transpose(partner, (1, 2, 0, 3)).reshape(comps * levels, -1)
        side_cols = lon_all[:, :, width:].reshape(lon_count, comps, levels, 4, rows)
        up = lax.dynamic_index_in_dim(side_rows, jnp.maximum(lat_pos - 1, 0), keepdims=False)[:, :, 2:]
        down = lax.dynamic_index_in_dim(side_rows, jnp.minimum(lat_pos + 1, lat_count - 1), keepdims=False)[:, :, :2]
        left = lax.dynamic_index_in_dim(side_cols, jnp.maximum(lon_pos - 1, 0), keepdims=False)[:, :, 2:]
        right = lax.dynamic_index_in_dim(side_cols, jnp.minimum(lon_pos + 1, lon_count - 1), keepdims=False)[:, :, :2]
        rim = select(partner).reshape(comps, levels, -1)
        rim_lat = rim[:, :, :band].reshape(comps, levels, 2, cols)
        rim_lon = rim[:, :, band:].reshape(comps, levels, 2, rows)
        up = jnp.where(on_top, rim_lat, up).reshape(comps * levels, 2, cols)
        down = jnp.where(on_bottom, rim_lat, down).reshape(comps * levels, 2, cols)
        left = jnp.where(on_left, rim_lon, left).reshape(comps * levels, 2, rows)
        right = jnp.where(on_right, rim_lon, right).reshape(comps * levels, 2, rows)
        sides = jnp.pad(jnp.concatenate([left, right], axis=1), ((0, 0), (0, 0), (0, cols - rows)))
        return (jnp.concatenate([up, down, sides], axis=1),)

    field = state[0].reshape(comps * levels, rows, cols)
    donation, lon_w, lat_w, turn_parts = first_donation(field, donor_cell[0, 0], donor_frac[0, 0, 0], donor_turn[0, 0])
    section_one, donation, edge_rows = advance(field, *section(field, donation), field, lon_w, lat_w, turn_parts, True)
    new_field = advance(section_one, *section(section_one, donation, edge_rows), field, lon_w, lat_w, turn_parts, False)
    return new_field.reshape(1, comps, levels, rows, cols)


def solution(mesh):
    in_specs = (
        P("panel", None, None, "lat", "lon"),
        P("panel", "lat", "lon", None),
        P("panel", "lat", "lon", None),
        P("panel", "lat", "lon", None, None),
        P("panel", "lat", "lon", None),
    )
    out_specs = P("panel", None, None, "lat", "lon")
    return jax.shard_map(
        per_device, mesh=mesh, in_specs=in_specs, out_specs=out_specs, check_vma=False
    )
```

```python
import jax
import jax.numpy as jnp
from jax import lax
from jax.sharding import PartitionSpec as P
from jax.experimental import pallas as pl
from jax.experimental.pallas import tpu as pltpu
import functools

INTERPRET = False

viscosity = 0.05
resistivity = 0.05
diffusivity = 0.05
buoyancy = 0.5
time_step = 0.25

HIGHEST = lax.Precision.HIGHEST


def stencil_kernel(*refs, first):
    if first:
        f_ref, halo_ref, lon_ref, lat_ref, turn_ref, o_ref, don_ref = refs
    else:
        f_ref, halo_ref, base_ref, o_ref = refs
    planes, height, width = f_ref.shape
    comps = planes // 2
    row = lax.broadcasted_iota(jnp.int32, (height, width), 0)
    col = lax.broadcasted_iota(jnp.int32, (height, width), 1)
    tile = lax.broadcasted_iota(jnp.int32, (8, width), 0)

    eye = jnp.where(
        lax.broadcasted_iota(jnp.int32, (height, height), 0) == lax.broadcasted_iota(jnp.int32, (height, height), 1),
        1.0,
        0.0,
    )
    pick_row = lax.broadcasted_iota(jnp.int32, (width, height), 0)

    def columns(k):
        left = halo_ref[k, 4:6, 0:height]
        right = halo_ref[k, 6:8, 0:height]
        rows_of = jnp.where(
            pick_row == 0,
            left[0:1, :],
            jnp.where(pick_row == 1, left[1:2, :], jnp.where(pick_row == 2, right[0:1, :], jnp.where(pick_row == 3, right[1:2, :], 0.0))),
        )
        return lax.dot_general(
            eye, rows_of, (((1,), (1,)), ((), ())), precision=HIGHEST, preferred_element_type=jnp.float32
        )

    def terms(k):
        x = f_ref[k]
        up = halo_ref[k, 0:2, :]
        down = halo_ref[k, 2:4, :]
        sides = columns(k)
        left = sides[:, 0:2]
        right = sides[:, 2:4]
        rolled = pltpu.roll(x, 1, 0)
        lat_m1 = jnp.concatenate([jnp.where(tile == 0, up[1:2, :], rolled[:8]), rolled[8:]], axis=0)
        rolled = pltpu.roll(x, 2, 0)
        top = jnp.where(tile == 0, up[0:1, :], jnp.where(tile == 1, up[1:2, :], rolled[:8]))
        lat_m2 = jnp.concatenate([top, rolled[8:]], axis=0)
        rolled = pltpu.roll(x, height - 1, 0)
        lat_p1 = jnp.concatenate([rolled[: height - 8], jnp.where(tile == 7, down[0:1, :], rolled[height - 8 :])], axis=0)
        rolled = pltpu.roll(x, height - 2, 0)
        bottom = jnp.where(tile == 7, down[1:2, :], jnp.where(tile == 6, down[0:1, :], rolled[height - 8 :]))
        lat_p2 = jnp.concatenate([rolled[: height - 8], bottom], axis=0)
        lon_m1 = jnp.where(col == 0, left[:, 1:2], pltpu.roll(x, 1, 1))
        lon_m2 = jnp.where(col == 0, left[:, 0:1], jnp.where(col == 1, left[:, 1:2], pltpu.roll(x, 2, 1)))
        lon_p1 = jnp.where(col == width - 1, right[:, 0:1], pltpu.roll(x, width - 1, 1))
        lon_p2 = jnp.where(
            col == width - 1, right[:, 1:2], jnp.where(col == width - 2, right[:, 0:1], pltpu.roll(x, width - 2, 1))
        )
        d_lat = (8.0 * (lat_p1 - lat_m1) - (lat_p2 - lat_m2)) * (1.0 / 12.0)
        d_lon = (8.0 * (lon_p1 - lon_m1) - (lon_p2 - lon_m2)) * (1.0 / 12.0)
        lap = lat_p1 + lat_m1 + lon_p1 + lon_m1 - 4.0 * x
        return x, d_lat, d_lon, lap

    for level in range(2):
        def plane(c):
            return c * 2 + level

        def value(c):
            return f_ref[plane(c)]

        def lap_of(c, x, lap):
            above = f_ref[c * 2 + 1] if level == 0 else 0.0
            below = f_ref[c * 2] if level == 1 else 0.0
            return lap + above + below - 2.0 * x

        def store(c, x, rate):
            section = x + time_step * rate
            if first:
                o_ref[plane(c)] = section
                k = plane(c)
                for slot, line in enumerate((0, 1, height - 2, height - 1)):
                    don_ref[k : k + 1, slot * width : (slot + 1) * width] = section[line : line + 1, :]
            else:
                o_ref[plane(c)] = 0.5 * base_ref[plane(c)] + 0.5 * section

        u1, u2, u4, u5, u6 = value(1), value(2), value(4), value(5), value(6)
        for c in range(3):
            xa, lat_a, lon_a, lap_a = terms(plane(c))
            xb, lat_b, lon_b, lap_b = terms(plane(c + 3))
            adv_u_a = u1 * lat_a + u2 * lon_a
            adv_b_a = u4 * lat_a + u5 * lon_a
            adv_u_b = u1 * lat_b + u2 * lon_b
            adv_b_b = u4 * lat_b + u5 * lon_b
            rate_a = -adv_u_a + adv_b_b + viscosity * lap_of(c, xa, lap_a)
            if c == 0:
                rate_a = rate_a + buoyancy * u6
            rate_b = adv_b_a - adv_u_b + resistivity * lap_of(c + 3, xb, lap_b)
            store(c, xa, rate_a)
            store(c + 3, xb, rate_b)
        x6, lat_6, lon_6, lap_6 = terms(plane(6))
        adv_u_6 = u1 * lat_6 + u2 * lon_6
        store(6, x6, -adv_u_6 + diffusivity * lap_of(6, x6, lap_6))

    if first:
        donate_planes(lambda k: o_ref[k], planes, lon_ref[...], lat_ref[...], turn_ref, don_ref, 4 * width)


def advance(field, halo, base, lon, lat, turn, first):
    shape = jax.ShapeDtypeStruct(field.shape, field.dtype)
    if first:
        shape = (
            shape,
            jax.ShapeDtypeStruct((field.shape[0], 4 * field.shape[2] + lon.shape[1]), jnp.float32),
        )
    return pl.pallas_call(
        functools.partial(stencil_kernel, first=first),
        out_shape=shape,
        interpret=INTERPRET,
    )(*((field, halo, lon, lat, turn) if first else (field, halo, base)))


def donation_weights(cells_ref, frac_ref, rows, cols):
    dons = cells_ref.shape[1]
    cell = cells_ref[...].astype(jnp.float32)
    row = jnp.floor((cell + 0.5) * (1.0 / (cols - 1)))
    col = cell - row * (cols - 1)
    row = row.astype(jnp.int32)
    col = col.astype(jnp.int32)
    frac_t = frac_ref[0:1, :]
    frac_p = frac_ref[1:2, :]
    col_ids = lax.broadcasted_iota(jnp.int32, (cols, dons), 0)
    row_ids = lax.broadcasted_iota(jnp.int32, (rows, dons), 0)
    weight_lon = jnp.where(col_ids == col, 1.0 - frac_p, 0.0) + jnp.where(col_ids == col + 1, frac_p, 0.0)
    weight_lat = jnp.where(row_ids == row, 1.0 - frac_t, 0.0) + jnp.where(row_ids == row + 1, frac_t, 0.0)
    return weight_lon, weight_lat


def donate_planes(plane_of, planes, weight_lon, weight_lat, turn_ref, out_ref, start):
    cosine = turn_ref[0:1, :]
    sine = turn_ref[1:2, :]
    values = []
    for k in range(planes):
        along = jnp.dot(plane_of(k), weight_lon, precision=HIGHEST, preferred_element_type=jnp.float32)
        values.append(jnp.sum(along * weight_lat, axis=0, keepdims=True))
    for k in range(planes):
        comp, level = divmod(k, 2)
        if comp in (1, 4):
            value = cosine * values[k] - sine * values[k + 2]
        elif comp in (2, 5):
            value = sine * values[k - 2] + cosine * values[k]
        else:
            value = values[k]
        out_ref[k : k + 1, start : start + value.shape[1]] = value


def donation_kernel(f_ref, cells_ref, frac_ref, angle_ref, out_ref, lon_ref, lat_ref, turn_ref):
    angle = angle_ref[...]
    turn_ref[0:1, :] = jnp.cos(angle)
    turn_ref[1:2, :] = jnp.sin(angle)
    planes, rows, cols = f_ref.shape
    weight_lon, weight_lat = donation_weights(cells_ref, frac_ref, rows, cols)
    lon_ref[...] = weight_lon
    lat_ref[...] = weight_lat
    for k in range(planes):
        for slot, line in enumerate((0, 1, rows - 2, rows - 1)):
            out_ref[k : k + 1, slot * cols : (slot + 1) * cols] = f_ref[k, line : line + 1, :]
    donate_planes(lambda k: f_ref[k], planes, weight_lon, weight_lat, turn_ref, out_ref, 4 * cols)


def first_donation(field, cells, frac, turn):
    planes, rows, cols = field.shape
    dons = cells.shape[1]
    return pl.pallas_call(
        donation_kernel,
        out_shape=(
            jax.ShapeDtypeStruct((planes, 4 * cols + dons), jnp.float32),
            jax.ShapeDtypeStruct((cols, dons), jnp.float32),
            jax.ShapeDtypeStruct((rows, dons), jnp.float32),
            jax.ShapeDtypeStruct((2, dons), jnp.float32),
        ),
        interpret=INTERPRET,
    )(field, cells, frac, turn)


def rotate(values, turn):
    cosine = jnp.cos(turn)
    sine = jnp.sin(turn)
    parts = [
        values[0],
        cosine * values[1] - sine * values[2],
        sine * values[1] + cosine * values[2],
        values[3],
        cosine * values[4] - sine * values[5],
        sine * values[4] + cosine * values[5],
        values[6],
    ]
    return jnp.stack(parts)


def per_device(state, source_slot, donor_cell, donor_frac, donor_turn):
    comps = state.shape[1]
    levels = state.shape[2]
    rows = state.shape[3]
    cols = state.shape[4]
    cells = donor_cell[0, 0, 0]
    frac_t = donor_frac[0, 0, 0, 0]
    frac_p = donor_frac[0, 0, 0, 1]
    turn = donor_turn[0, 0, 0]
    slots = source_slot[0, 0, 0]
    lat_pos = lax.axis_index("lat")
    lon_pos = lax.axis_index("lon")
    lat_count = lax.axis_size("lat")
    lon_count = lax.axis_size("lon")
    on_top = lat_pos == 0
    on_bottom = lat_pos == lat_count - 1
    on_left = lon_pos == 0
    on_right = lon_pos == lon_count - 1

    band = 2 * cols
    side = 2 * rows
    lat_slots = jnp.where(on_top, slots[0:band], slots[band : 2 * band])
    lon_slots = jnp.where(on_left, slots[2 * band : 2 * band + side], slots[2 * band + side :])
    wanted = jnp.concatenate([lat_slots, lon_slots])
    total = lat_count * lon_count * cells.shape[0]
    pick = (jnp.arange(total, dtype=jnp.int32)[:, None] == wanted[None, :]).astype(jnp.bfloat16)

    def select(values):
        high = lax.reduce_precision(values, exponent_bits=8, mantissa_bits=7)
        rest = values - high
        middle = lax.reduce_precision(rest, exponent_bits=8, mantissa_bits=7)
        low = rest - middle
        parts = jnp.concatenate([high, middle, low]).astype(jnp.bfloat16)
        picked = jnp.dot(parts, pick, preferred_element_type=jnp.float32)
        count = values.shape[0]
        return picked[:count] + (picked[count : 2 * count] + picked[2 * count :])

    def gather(packet, axis):
        size = lax.axis_size(axis)
        pos = lax.axis_index(axis)
        held = packet[None]
        k = 1
        while k < size:
            other = lax.ppermute(held, axis, [(i, i ^ k) for i in range(size)])
            low = (pos // k) % 2 == 0
            held = jnp.where(low, jnp.concatenate([held, other]), jnp.concatenate([other, held]))
            k *= 2
        return held

    def section(field, packet):
        flat = field
        edge = 4 * cols
        dons = packet.shape[1] - edge
        lat_all = gather(packet, "lat")
        side_rows = lat_all[:, :, :edge].reshape(lat_count, comps, levels, 4, cols)
        col_given = jnp.transpose(lat_all[:, :, edge:], (1, 0, 2)).reshape(comps * levels, -1)
        side_cols = jnp.concatenate([flat[:, :, :2], flat[:, :, cols - 2 :]], axis=2)
        side_cols = jnp.swapaxes(side_cols, 1, 2)
        lon_packet = jnp.concatenate([col_given, side_cols.reshape(comps * levels, -1)], axis=1)
        lon_all = gather(lon_packet, "lon")
        width = col_given.shape[1]
        own = lon_all[:, :, :width].reshape(lon_count, comps * levels, lat_count, dons)
        own = jnp.transpose(own, (1, 2, 0, 3)).reshape(comps * levels, -1)
        partner = lax.ppermute(own, "panel", [(0, 1), (1, 0)])
        side_cols = lon_all[:, :, width:].reshape(lon_count, comps, levels, 4, rows)
        up = lax.dynamic_index_in_dim(side_rows, jnp.maximum(lat_pos - 1, 0), keepdims=False)[:, :, 2:]
        down = lax.dynamic_index_in_dim(side_rows, jnp.minimum(lat_pos + 1, lat_count - 1), keepdims=False)[:, :, :2]
        left = lax.dynamic_index_in_dim(side_cols, jnp.maximum(lon_pos - 1, 0), keepdims=False)[:, :, 2:]
        right = lax.dynamic_index_in_dim(side_cols, jnp.minimum(lon_pos + 1, lon_count - 1), keepdims=False)[:, :, :2]
        rim = select(partner).reshape(comps, levels, -1)
        rim_lat = rim[:, :, :band].reshape(comps, levels, 2, cols)
        rim_lon = rim[:, :, band:].reshape(comps, levels, 2, rows)
        up = jnp.where(on_top, rim_lat, up).reshape(comps * levels, 2, cols)
        down = jnp.where(on_bottom, rim_lat, down).reshape(comps * levels, 2, cols)
        left = jnp.where(on_left, rim_lon, left).reshape(comps * levels, 2, rows)
        right = jnp.where(on_right, rim_lon, right).reshape(comps * levels, 2, rows)
        sides = jnp.pad(jnp.concatenate([left, right], axis=1), ((0, 0), (0, 0), (0, cols - rows)))
        return (jnp.concatenate([up, down, sides], axis=1),)

    field = state[0].reshape(comps * levels, rows, cols)
    donation, lon_w, lat_w, turn_parts = first_donation(field, donor_cell[0, 0], donor_frac[0, 0, 0], donor_turn[0, 0])
    section_one, donation = advance(field, *section(field, donation), field, lon_w, lat_w, turn_parts, True)
    new_field = advance(section_one, *section(section_one, donation), field, lon_w, lat_w, turn_parts, False)
    return new_field.reshape(1, comps, levels, rows, cols)


def solution(mesh):
    in_specs = (
        P("panel", None, None, "lat", "lon"),
        P("panel", "lat", "lon", None),
        P("panel", "lat", "lon", None),
        P("panel", "lat", "lon", None, None),
        P("panel", "lat", "lon", None),
    )
    out_specs = P("panel", None, None, "lat", "lon")
    return jax.shard_map(
        per_device, mesh=mesh, in_specs=in_specs, out_specs=out_specs, check_vma=False
    )
```

```python
import jax
import jax.numpy as jnp
from jax import lax
from jax.sharding import PartitionSpec as P
from jax.experimental import pallas as pl
from jax.experimental.pallas import tpu as pltpu
import functools

INTERPRET = False

viscosity = 0.05
resistivity = 0.05
diffusivity = 0.05
buoyancy = 0.5
time_step = 0.25

HIGHEST = lax.Precision.HIGHEST


def stencil_kernel(*refs, first):
    if first:
        f_ref, halo_ref, lon_ref, lat_ref, turn_ref, o_ref, don_ref = refs
    else:
        f_ref, halo_ref, base_ref, o_ref = refs
    planes, height, width = f_ref.shape
    comps = planes // 2
    row = lax.broadcasted_iota(jnp.int32, (height, width), 0)
    col = lax.broadcasted_iota(jnp.int32, (height, width), 1)
    tile = lax.broadcasted_iota(jnp.int32, (8, width), 0)

    eye = jnp.where(
        lax.broadcasted_iota(jnp.int32, (height, height), 0) == lax.broadcasted_iota(jnp.int32, (height, height), 1),
        1.0,
        0.0,
    )
    pick_row = lax.broadcasted_iota(jnp.int32, (width, height), 0)

    def columns(k):
        left = halo_ref[k, 4:6, 0:height]
        right = halo_ref[k, 6:8, 0:height]
        rows_of = jnp.where(
            pick_row == 0,
            left[0:1, :],
            jnp.where(pick_row == 1, left[1:2, :], jnp.where(pick_row == 2, right[0:1, :], jnp.where(pick_row == 3, right[1:2, :], 0.0))),
        )
        return lax.dot_general(
            eye, rows_of, (((1,), (1,)), ((), ())), precision=HIGHEST, preferred_element_type=jnp.float32
        )

    def terms(k):
        x = f_ref[k]
        up = halo_ref[k, 0:2, :]
        down = halo_ref[k, 2:4, :]
        sides = columns(k)
        left = sides[:, 0:2]
        right = sides[:, 2:4]
        rolled = pltpu.roll(x, 1, 0)
        lat_m1 = jnp.concatenate([jnp.where(tile == 0, up[1:2, :], rolled[:8]), rolled[8:]], axis=0)
        rolled = pltpu.roll(x, 2, 0)
        top = jnp.where(tile == 0, up[0:1, :], jnp.where(tile == 1, up[1:2, :], rolled[:8]))
        lat_m2 = jnp.concatenate([top, rolled[8:]], axis=0)
        rolled = pltpu.roll(x, height - 1, 0)
        lat_p1 = jnp.concatenate([rolled[: height - 8], jnp.where(tile == 7, down[0:1, :], rolled[height - 8 :])], axis=0)
        rolled = pltpu.roll(x, height - 2, 0)
        bottom = jnp.where(tile == 7, down[1:2, :], jnp.where(tile == 6, down[0:1, :], rolled[height - 8 :]))
        lat_p2 = jnp.concatenate([rolled[: height - 8], bottom], axis=0)
        lon_m1 = jnp.where(col == 0, left[:, 1:2], pltpu.roll(x, 1, 1))
        lon_m2 = jnp.where(col == 0, left[:, 0:1], jnp.where(col == 1, left[:, 1:2], pltpu.roll(x, 2, 1)))
        lon_p1 = jnp.where(col == width - 1, right[:, 0:1], pltpu.roll(x, width - 1, 1))
        lon_p2 = jnp.where(
            col == width - 1, right[:, 1:2], jnp.where(col == width - 2, right[:, 0:1], pltpu.roll(x, width - 2, 1))
        )
        d_lat = (8.0 * (lat_p1 - lat_m1) - (lat_p2 - lat_m2)) * (1.0 / 12.0)
        d_lon = (8.0 * (lon_p1 - lon_m1) - (lon_p2 - lon_m2)) * (1.0 / 12.0)
        lap = lat_p1 + lat_m1 + lon_p1 + lon_m1 - 4.0 * x
        return x, d_lat, d_lon, lap

    for level in range(2):
        def plane(c):
            return c * 2 + level

        def value(c):
            return f_ref[plane(c)]

        def lap_of(c, x, lap):
            above = f_ref[c * 2 + 1] if level == 0 else 0.0
            below = f_ref[c * 2] if level == 1 else 0.0
            return lap + above + below - 2.0 * x

        def store(c, x, rate):
            section = x + time_step * rate
            if first:
                o_ref[plane(c)] = section
            else:
                o_ref[plane(c)] = 0.5 * base_ref[plane(c)] + 0.5 * section

        u1, u2, u4, u5, u6 = value(1), value(2), value(4), value(5), value(6)
        for c in range(3):
            xa, lat_a, lon_a, lap_a = terms(plane(c))
            xb, lat_b, lon_b, lap_b = terms(plane(c + 3))
            adv_u_a = u1 * lat_a + u2 * lon_a
            adv_b_a = u4 * lat_a + u5 * lon_a
            adv_u_b = u1 * lat_b + u2 * lon_b
            adv_b_b = u4 * lat_b + u5 * lon_b
            rate_a = -adv_u_a + adv_b_b + viscosity * lap_of(c, xa, lap_a)
            if c == 0:
                rate_a = rate_a + buoyancy * u6
            rate_b = adv_b_a - adv_u_b + resistivity * lap_of(c + 3, xb, lap_b)
            store(c, xa, rate_a)
            store(c + 3, xb, rate_b)
        x6, lat_6, lon_6, lap_6 = terms(plane(6))
        adv_u_6 = u1 * lat_6 + u2 * lon_6
        store(6, x6, -adv_u_6 + diffusivity * lap_of(6, x6, lap_6))

    if first:
        donate_planes(lambda k: o_ref[k], planes, lon_ref[...], lat_ref[...], turn_ref, don_ref)


def advance(field, halo, base, lon, lat, turn, first):
    shape = jax.ShapeDtypeStruct(field.shape, field.dtype)
    if first:
        shape = (shape, jax.ShapeDtypeStruct((field.shape[0], lon.shape[1]), jnp.float32))
    return pl.pallas_call(
        functools.partial(stencil_kernel, first=first),
        out_shape=shape,
        interpret=INTERPRET,
    )(*((field, halo, lon, lat, turn) if first else (field, halo, base)))


def donation_weights(cells_ref, frac_ref, rows, cols):
    dons = cells_ref.shape[1]
    cell = cells_ref[...].astype(jnp.float32)
    row = jnp.floor((cell + 0.5) * (1.0 / (cols - 1)))
    col = cell - row * (cols - 1)
    row = row.astype(jnp.int32)
    col = col.astype(jnp.int32)
    frac_t = frac_ref[0:1, :]
    frac_p = frac_ref[1:2, :]
    col_ids = lax.broadcasted_iota(jnp.int32, (cols, dons), 0)
    row_ids = lax.broadcasted_iota(jnp.int32, (rows, dons), 0)
    weight_lon = jnp.where(col_ids == col, 1.0 - frac_p, 0.0) + jnp.where(col_ids == col + 1, frac_p, 0.0)
    weight_lat = jnp.where(row_ids == row, 1.0 - frac_t, 0.0) + jnp.where(row_ids == row + 1, frac_t, 0.0)
    return weight_lon, weight_lat


def donate_planes(plane_of, planes, weight_lon, weight_lat, turn_ref, out_ref):
    cosine = turn_ref[0:1, :]
    sine = turn_ref[1:2, :]
    values = []
    for k in range(planes):
        along = jnp.dot(plane_of(k), weight_lon, precision=HIGHEST, preferred_element_type=jnp.float32)
        values.append(jnp.sum(along * weight_lat, axis=0, keepdims=True))
    for k in range(planes):
        comp, level = divmod(k, 2)
        if comp in (1, 4):
            value = cosine * values[k] - sine * values[k + 2]
        elif comp in (2, 5):
            value = sine * values[k - 2] + cosine * values[k]
        else:
            value = values[k]
        out_ref[k : k + 1, :] = value


def donation_kernel(f_ref, cells_ref, frac_ref, angle_ref, out_ref, lon_ref, lat_ref, turn_ref):
    angle = angle_ref[...]
    turn_ref[0:1, :] = jnp.cos(angle)
    turn_ref[1:2, :] = jnp.sin(angle)
    planes, rows, cols = f_ref.shape
    weight_lon, weight_lat = donation_weights(cells_ref, frac_ref, rows, cols)
    lon_ref[...] = weight_lon
    lat_ref[...] = weight_lat
    donate_planes(lambda k: f_ref[k], planes, weight_lon, weight_lat, turn_ref, out_ref)


def first_donation(field, cells, frac, turn):
    planes, rows, cols = field.shape
    dons = cells.shape[1]
    return pl.pallas_call(
        donation_kernel,
        out_shape=(
            jax.ShapeDtypeStruct((planes, dons), jnp.float32),
            jax.ShapeDtypeStruct((cols, dons), jnp.float32),
            jax.ShapeDtypeStruct((rows, dons), jnp.float32),
            jax.ShapeDtypeStruct((2, dons), jnp.float32),
        ),
        interpret=INTERPRET,
    )(field, cells, frac, turn)


def rotate(values, turn):
    cosine = jnp.cos(turn)
    sine = jnp.sin(turn)
    parts = [
        values[0],
        cosine * values[1] - sine * values[2],
        sine * values[1] + cosine * values[2],
        values[3],
        cosine * values[4] - sine * values[5],
        sine * values[4] + cosine * values[5],
        values[6],
    ]
    return jnp.stack(parts)


def per_device(state, source_slot, donor_cell, donor_frac, donor_turn):
    comps = state.shape[1]
    levels = state.shape[2]
    rows = state.shape[3]
    cols = state.shape[4]
    cells = donor_cell[0, 0, 0]
    frac_t = donor_frac[0, 0, 0, 0]
    frac_p = donor_frac[0, 0, 0, 1]
    turn = donor_turn[0, 0, 0]
    slots = source_slot[0, 0, 0]
    lat_pos = lax.axis_index("lat")
    lon_pos = lax.axis_index("lon")
    lat_count = lax.axis_size("lat")
    lon_count = lax.axis_size("lon")
    on_top = lat_pos == 0
    on_bottom = lat_pos == lat_count - 1
    on_left = lon_pos == 0
    on_right = lon_pos == lon_count - 1

    band = 2 * cols
    side = 2 * rows
    lat_slots = jnp.where(on_top, slots[0:band], slots[band : 2 * band])
    lon_slots = jnp.where(on_left, slots[2 * band : 2 * band + side], slots[2 * band + side :])
    wanted = jnp.concatenate([lat_slots, lon_slots])
    total = lat_count * lon_count * cells.shape[0]
    dons_each = cells.shape[0]
    half = lon_count // 2
    chunk = jnp.arange(half * lat_count * dons_each, dtype=jnp.int32)

    def pick_for(base):
        block = chunk // (lat_count * dons_each)
        lat_of = chunk // dons_each % lat_count
        index = (lat_of * lon_count + base + block) * dons_each + chunk % dons_each
        return (index[:, None] == wanted[None, :]).astype(jnp.bfloat16)

    pick_held = pick_for(lon_pos // half * half)
    pick_new = pick_for((lon_pos ^ half) // half * half)

    def select(values, pick):
        high = lax.reduce_precision(values, exponent_bits=8, mantissa_bits=7)
        rest = values - high
        middle = lax.reduce_precision(rest, exponent_bits=8, mantissa_bits=7)
        low = rest - middle
        parts = jnp.concatenate([high, middle, low]).astype(jnp.bfloat16)
        picked = jnp.dot(parts, pick, preferred_element_type=jnp.float32)
        count = values.shape[0]
        return picked[:count] + (picked[count : 2 * count] + picked[2 * count :])

    def gather(packet, axis):
        size = lax.axis_size(axis)
        pos = lax.axis_index(axis)
        held = packet[None]
        k = 1
        while k < size:
            before = held
            other = lax.ppermute(held, axis, [(i, i ^ k) for i in range(size)])
            low = (pos // k) % 2 == 0
            held = jnp.where(low, jnp.concatenate([held, other]), jnp.concatenate([other, held]))
            k *= 2
        return held, before, other

    def section(field, donation):
        flat = field
        given = lax.ppermute(donation, "panel", [(0, 1), (1, 0)])
        dons = given.shape[1]
        side_rows = jnp.concatenate([flat[:, :2, :], flat[:, rows - 2 :, :]], axis=1)
        lat_packet = jnp.concatenate([given, side_rows.reshape(comps * levels, -1)], axis=1)
        lat_all = gather(lat_packet, "lat")[0]
        col_given = jnp.transpose(lat_all[:, :, :dons], (1, 0, 2)).reshape(comps * levels, -1)
        side_rows = lat_all[:, :, dons:].reshape(lat_count, comps, levels, 4, cols)
        side_cols = jnp.concatenate([flat[:, :, :2], flat[:, :, cols - 2 :]], axis=2)
        side_cols = jnp.swapaxes(side_cols, 1, 2)
        lon_packet = jnp.concatenate([col_given, side_cols.reshape(comps * levels, -1)], axis=1)
        lon_all, lon_held, lon_new = gather(lon_packet, "lon")
        width = col_given.shape[1]
        held_part = jnp.transpose(lon_held[:, :, :width], (1, 0, 2)).reshape(comps * levels, -1)
        new_part = jnp.transpose(lon_new[:, :, :width], (1, 0, 2)).reshape(comps * levels, -1)
        side_cols = lon_all[:, :, width:].reshape(lon_count, comps, levels, 4, rows)
        up = lax.dynamic_index_in_dim(side_rows, jnp.maximum(lat_pos - 1, 0), keepdims=False)[:, :, 2:]
        down = lax.dynamic_index_in_dim(side_rows, jnp.minimum(lat_pos + 1, lat_count - 1), keepdims=False)[:, :, :2]
        left = lax.dynamic_index_in_dim(side_cols, jnp.maximum(lon_pos - 1, 0), keepdims=False)[:, :, 2:]
        right = lax.dynamic_index_in_dim(side_cols, jnp.minimum(lon_pos + 1, lon_count - 1), keepdims=False)[:, :, :2]
        rim = (select(held_part, pick_held) + select(new_part, pick_new)).reshape(comps, levels, -1)
        rim_lat = rim[:, :, :band].reshape(comps, levels, 2, cols)
        rim_lon = rim[:, :, band:].reshape(comps, levels, 2, rows)
        up = jnp.where(on_top, rim_lat, up).reshape(comps * levels, 2, cols)
        down = jnp.where(on_bottom, rim_lat, down).reshape(comps * levels, 2, cols)
        left = jnp.where(on_left, rim_lon, left).reshape(comps * levels, 2, rows)
        right = jnp.where(on_right, rim_lon, right).reshape(comps * levels, 2, rows)
        sides = jnp.pad(jnp.concatenate([left, right], axis=1), ((0, 0), (0, 0), (0, cols - rows)))
        return (jnp.concatenate([up, down, sides], axis=1),)

    field = state[0].reshape(comps * levels, rows, cols)
    donation, lon_w, lat_w, turn_parts = first_donation(field, donor_cell[0, 0], donor_frac[0, 0, 0], donor_turn[0, 0])
    section_one, donation = advance(field, *section(field, donation), field, lon_w, lat_w, turn_parts, True)
    new_field = advance(section_one, *section(section_one, donation), field, lon_w, lat_w, turn_parts, False)
    return new_field.reshape(1, comps, levels, rows, cols)


def solution(mesh):
    in_specs = (
        P("panel", None, None, "lat", "lon"),
        P("panel", "lat", "lon", None),
        P("panel", "lat", "lon", None),
        P("panel", "lat", "lon", None, None),
        P("panel", "lat", "lon", None),
    )
    out_specs = P("panel", None, None, "lat", "lon")
    return jax.shard_map(
        per_device, mesh=mesh, in_specs=in_specs, out_specs=out_specs, check_vma=False
    )
```

```python
import jax
import jax.numpy as jnp
from jax import lax
from jax.sharding import PartitionSpec as P
from jax.experimental import pallas as pl
from jax.experimental.pallas import tpu as pltpu
import functools

INTERPRET = False

viscosity = 0.05
resistivity = 0.05
diffusivity = 0.05
buoyancy = 0.5
time_step = 0.25

HIGHEST = lax.Precision.HIGHEST


def stencil_kernel(*refs, first):
    if first:
        f_ref, halo_ref, lon_ref, lat_ref, turn_ref, o_ref, don_ref = refs
    else:
        f_ref, halo_ref, base_ref, o_ref = refs
    planes, height, width = f_ref.shape
    comps = planes // 2
    row = lax.broadcasted_iota(jnp.int32, (height, width), 0)
    col = lax.broadcasted_iota(jnp.int32, (height, width), 1)
    tile = lax.broadcasted_iota(jnp.int32, (8, width), 0)

    eye = jnp.where(
        lax.broadcasted_iota(jnp.int32, (height, height), 0) == lax.broadcasted_iota(jnp.int32, (height, height), 1),
        1.0,
        0.0,
    )
    pick_row = lax.broadcasted_iota(jnp.int32, (width, height), 0)

    def columns(k):
        left = halo_ref[k, 4:6, 0:height]
        right = halo_ref[k, 6:8, 0:height]
        rows_of = jnp.where(
            pick_row == 0,
            left[0:1, :],
            jnp.where(pick_row == 1, left[1:2, :], jnp.where(pick_row == 2, right[0:1, :], jnp.where(pick_row == 3, right[1:2, :], 0.0))),
        )
        return lax.dot_general(
            eye, rows_of, (((1,), (1,)), ((), ())), precision=HIGHEST, preferred_element_type=jnp.float32
        )

    def terms(k):
        x = f_ref[k]
        up = halo_ref[k, 0:2, :]
        down = halo_ref[k, 2:4, :]
        sides = columns(k)
        left = sides[:, 0:2]
        right = sides[:, 2:4]
        rolled = pltpu.roll(x, 1, 0)
        lat_m1 = jnp.concatenate([jnp.where(tile == 0, up[1:2, :], rolled[:8]), rolled[8:]], axis=0)
        rolled = pltpu.roll(x, 2, 0)
        top = jnp.where(tile == 0, up[0:1, :], jnp.where(tile == 1, up[1:2, :], rolled[:8]))
        lat_m2 = jnp.concatenate([top, rolled[8:]], axis=0)
        rolled = pltpu.roll(x, height - 1, 0)
        lat_p1 = jnp.concatenate([rolled[: height - 8], jnp.where(tile == 7, down[0:1, :], rolled[height - 8 :])], axis=0)
        rolled = pltpu.roll(x, height - 2, 0)
        bottom = jnp.where(tile == 7, down[1:2, :], jnp.where(tile == 6, down[0:1, :], rolled[height - 8 :]))
        lat_p2 = jnp.concatenate([rolled[: height - 8], bottom], axis=0)
        lon_m1 = jnp.where(col == 0, left[:, 1:2], pltpu.roll(x, 1, 1))
        lon_m2 = jnp.where(col == 0, left[:, 0:1], jnp.where(col == 1, left[:, 1:2], pltpu.roll(x, 2, 1)))
        lon_p1 = jnp.where(col == width - 1, right[:, 0:1], pltpu.roll(x, width - 1, 1))
        lon_p2 = jnp.where(
            col == width - 1, right[:, 1:2], jnp.where(col == width - 2, right[:, 0:1], pltpu.roll(x, width - 2, 1))
        )
        d_lat = (8.0 * (lat_p1 - lat_m1) - (lat_p2 - lat_m2)) * (1.0 / 12.0)
        d_lon = (8.0 * (lon_p1 - lon_m1) - (lon_p2 - lon_m2)) * (1.0 / 12.0)
        lap = lat_p1 + lat_m1 + lon_p1 + lon_m1 - 4.0 * x
        return x, d_lat, d_lon, lap

    for level in range(2):
        def plane(c):
            return c * 2 + level

        def value(c):
            return f_ref[plane(c)]

        def lap_of(c, x, lap):
            above = f_ref[c * 2 + 1] if level == 0 else 0.0
            below = f_ref[c * 2] if level == 1 else 0.0
            return lap + above + below - 2.0 * x

        def store(c, x, rate):
            section = x + time_step * rate
            if first:
                o_ref[plane(c)] = section
            else:
                o_ref[plane(c)] = 0.5 * base_ref[plane(c)] + 0.5 * section

        u1, u2, u4, u5, u6 = value(1), value(2), value(4), value(5), value(6)
        for c in range(3):
            xa, lat_a, lon_a, lap_a = terms(plane(c))
            xb, lat_b, lon_b, lap_b = terms(plane(c + 3))
            adv_u_a = u1 * lat_a + u2 * lon_a
            adv_b_a = u4 * lat_a + u5 * lon_a
            adv_u_b = u1 * lat_b + u2 * lon_b
            adv_b_b = u4 * lat_b + u5 * lon_b
            rate_a = -adv_u_a + adv_b_b + viscosity * lap_of(c, xa, lap_a)
            if c == 0:
                rate_a = rate_a + buoyancy * u6
            rate_b = adv_b_a - adv_u_b + resistivity * lap_of(c + 3, xb, lap_b)
            store(c, xa, rate_a)
            store(c + 3, xb, rate_b)
        x6, lat_6, lon_6, lap_6 = terms(plane(6))
        adv_u_6 = u1 * lat_6 + u2 * lon_6
        store(6, x6, -adv_u_6 + diffusivity * lap_of(6, x6, lap_6))

    if first:
        donate_planes(lambda k: o_ref[k], planes, lon_ref[...], lat_ref[...], turn_ref, don_ref)


def advance(field, halo, base, lon, lat, turn, first):
    shape = jax.ShapeDtypeStruct(field.shape, field.dtype)
    if first:
        shape = (shape, jax.ShapeDtypeStruct((field.shape[0], lon.shape[1]), jnp.float32))
    return pl.pallas_call(
        functools.partial(stencil_kernel, first=first),
        out_shape=shape,
        interpret=INTERPRET,
    )(*((field, halo, lon, lat, turn) if first else (field, halo, base)))


def donation_weights(cells_ref, frac_ref, rows, cols):
    dons = cells_ref.shape[1]
    cell = cells_ref[...].astype(jnp.float32)
    row = jnp.floor((cell + 0.5) * (1.0 / (cols - 1)))
    col = cell - row * (cols - 1)
    row = row.astype(jnp.int32)
    col = col.astype(jnp.int32)
    frac_t = frac_ref[0:1, :]
    frac_p = frac_ref[1:2, :]
    col_ids = lax.broadcasted_iota(jnp.int32, (cols, dons), 0)
    row_ids = lax.broadcasted_iota(jnp.int32, (rows, dons), 0)
    weight_lon = jnp.where(col_ids == col, 1.0 - frac_p, 0.0) + jnp.where(col_ids == col + 1, frac_p, 0.0)
    weight_lat = jnp.where(row_ids == row, 1.0 - frac_t, 0.0) + jnp.where(row_ids == row + 1, frac_t, 0.0)
    return weight_lon, weight_lat


def donate_planes(plane_of, planes, weight_lon, weight_lat, turn_ref, out_ref):
    cosine = turn_ref[0:1, :]
    sine = turn_ref[1:2, :]
    values = []
    for k in range(planes):
        along = jnp.dot(plane_of(k), weight_lon, precision=HIGHEST, preferred_element_type=jnp.float32)
        values.append(jnp.sum(along * weight_lat, axis=0, keepdims=True))
    for k in range(planes):
        comp, level = divmod(k, 2)
        if comp in (1, 4):
            value = cosine * values[k] - sine * values[k + 2]
        elif comp in (2, 5):
            value = sine * values[k - 2] + cosine * values[k]
        else:
            value = values[k]
        out_ref[k : k + 1, :] = value


def donation_kernel(f_ref, cells_ref, frac_ref, angle_ref, out_ref, lon_ref, lat_ref, turn_ref):
    angle = angle_ref[...]
    turn_ref[0:1, :] = jnp.cos(angle)
    turn_ref[1:2, :] = jnp.sin(angle)
    planes, rows, cols = f_ref.shape
    weight_lon, weight_lat = donation_weights(cells_ref, frac_ref, rows, cols)
    lon_ref[...] = weight_lon
    lat_ref[...] = weight_lat
    donate_planes(lambda k: f_ref[k], planes, weight_lon, weight_lat, turn_ref, out_ref)


def first_donation(field, cells, frac, turn):
    planes, rows, cols = field.shape
    dons = cells.shape[1]
    return pl.pallas_call(
        donation_kernel,
        out_shape=(
            jax.ShapeDtypeStruct((planes, dons), jnp.float32),
            jax.ShapeDtypeStruct((cols, dons), jnp.float32),
            jax.ShapeDtypeStruct((rows, dons), jnp.float32),
            jax.ShapeDtypeStruct((2, dons), jnp.float32),
        ),
        interpret=INTERPRET,
    )(field, cells, frac, turn)


def rotate(values, turn):
    cosine = jnp.cos(turn)
    sine = jnp.sin(turn)
    parts = [
        values[0],
        cosine * values[1] - sine * values[2],
        sine * values[1] + cosine * values[2],
        values[3],
        cosine * values[4] - sine * values[5],
        sine * values[4] + cosine * values[5],
        values[6],
    ]
    return jnp.stack(parts)


def per_device(state, source_slot, donor_cell, donor_frac, donor_turn):
    comps = state.shape[1]
    levels = state.shape[2]
    rows = state.shape[3]
    cols = state.shape[4]
    cells = donor_cell[0, 0, 0]
    frac_t = donor_frac[0, 0, 0, 0]
    frac_p = donor_frac[0, 0, 0, 1]
    turn = donor_turn[0, 0, 0]
    slots = source_slot[0, 0, 0]
    lat_pos = lax.axis_index("lat")
    lon_pos = lax.axis_index("lon")
    lat_count = lax.axis_size("lat")
    lon_count = lax.axis_size("lon")
    on_top = lat_pos == 0
    on_bottom = lat_pos == lat_count - 1
    on_left = lon_pos == 0
    on_right = lon_pos == lon_count - 1

    band = 2 * cols
    side = 2 * rows
    lat_slots = jnp.where(on_top, slots[0:band], slots[band : 2 * band])
    lon_slots = jnp.where(on_left, slots[2 * band : 2 * band + side], slots[2 * band + side :])
    wanted = jnp.concatenate([lat_slots, lon_slots])
    total = lat_count * lon_count * cells.shape[0]
    dons_each = cells.shape[0]
    half = lon_count // 2
    chunk = jnp.arange(half * lat_count * dons_each, dtype=jnp.int32)

    lon_bits = lon_count.bit_length() - 1

    def reverse(value, bits):
        return sum(((value >> i) & 1) << (bits - 1 - i) for i in range(bits))

    def pick_for(low_bit):
        block = chunk // (lat_count * dons_each)
        device = low_bit + reverse(block, lon_bits - 1) * 2
        lat_of = chunk // dons_each % lat_count
        index = (lat_of * lon_count + device) * dons_each + chunk % dons_each
        return (index[:, None] == wanted[None, :]).astype(jnp.bfloat16)

    pick_held = pick_for(lon_pos % 2)
    pick_new = pick_for(1 - lon_pos % 2)

    def select(values, pick):
        high = lax.reduce_precision(values, exponent_bits=8, mantissa_bits=7)
        rest = values - high
        middle = lax.reduce_precision(rest, exponent_bits=8, mantissa_bits=7)
        low = rest - middle
        parts = jnp.concatenate([high, middle, low]).astype(jnp.bfloat16)
        picked = jnp.dot(parts, pick, preferred_element_type=jnp.float32)
        count = values.shape[0]
        return picked[:count] + (picked[count : 2 * count] + picked[2 * count :])

    def gather(packet, axis, far_first=False):
        size = lax.axis_size(axis)
        pos = lax.axis_index(axis)
        held = packet[None]
        steps = []
        k = 1
        while k < size:
            steps.append(k)
            k *= 2
        if far_first:
            steps.reverse()
        for k in steps:
            before = held
            other = lax.ppermute(held, axis, [(i, i ^ k) for i in range(size)])
            low = (pos // k) % 2 == 0
            held = jnp.where(low, jnp.concatenate([held, other]), jnp.concatenate([other, held]))
        return held, before, other

    def section(field, donation):
        flat = field
        given = lax.ppermute(donation, "panel", [(0, 1), (1, 0)])
        dons = given.shape[1]
        side_rows = jnp.concatenate([flat[:, :2, :], flat[:, rows - 2 :, :]], axis=1)
        lat_packet = jnp.concatenate([given, side_rows.reshape(comps * levels, -1)], axis=1)
        lat_all = gather(lat_packet, "lat")[0]
        col_given = jnp.transpose(lat_all[:, :, :dons], (1, 0, 2)).reshape(comps * levels, -1)
        side_rows = lat_all[:, :, dons:].reshape(lat_count, comps, levels, 4, cols)
        side_cols = jnp.concatenate([flat[:, :, :2], flat[:, :, cols - 2 :]], axis=2)
        side_cols = jnp.swapaxes(side_cols, 1, 2)
        lon_packet = jnp.concatenate([col_given, side_cols.reshape(comps * levels, -1)], axis=1)
        lon_all, lon_held, lon_new = gather(lon_packet, "lon", far_first=True)
        width = col_given.shape[1]
        held_part = jnp.transpose(lon_held[:, :, :width], (1, 0, 2)).reshape(comps * levels, -1)
        new_part = jnp.transpose(lon_new[:, :, :width], (1, 0, 2)).reshape(comps * levels, -1)
        side_cols = lon_all[:, :, width:].reshape(lon_count, comps, levels, 4, rows)
        up = lax.dynamic_index_in_dim(side_rows, jnp.maximum(lat_pos - 1, 0), keepdims=False)[:, :, 2:]
        down = lax.dynamic_index_in_dim(side_rows, jnp.minimum(lat_pos + 1, lat_count - 1), keepdims=False)[:, :, :2]
        left_at = reverse(jnp.maximum(lon_pos - 1, 0), lon_bits)
        right_at = reverse(jnp.minimum(lon_pos + 1, lon_count - 1), lon_bits)
        left = lax.dynamic_index_in_dim(side_cols, left_at, keepdims=False)[:, :, 2:]
        right = lax.dynamic_index_in_dim(side_cols, right_at, keepdims=False)[:, :, :2]
        rim = (select(held_part, pick_held) + select(new_part, pick_new)).reshape(comps, levels, -1)
        rim_lat = rim[:, :, :band].reshape(comps, levels, 2, cols)
        rim_lon = rim[:, :, band:].reshape(comps, levels, 2, rows)
        up = jnp.where(on_top, rim_lat, up).reshape(comps * levels, 2, cols)
        down = jnp.where(on_bottom, rim_lat, down).reshape(comps * levels, 2, cols)
        left = jnp.where(on_left, rim_lon, left).reshape(comps * levels, 2, rows)
        right = jnp.where(on_right, rim_lon, right).reshape(comps * levels, 2, rows)
        sides = jnp.pad(jnp.concatenate([left, right], axis=1), ((0, 0), (0, 0), (0, cols - rows)))
        return (jnp.concatenate([up, down, sides], axis=1),)

    field = state[0].reshape(comps * levels, rows, cols)
    donation, lon_w, lat_w, turn_parts = first_donation(field, donor_cell[0, 0], donor_frac[0, 0, 0], donor_turn[0, 0])
    section_one, donation = advance(field, *section(field, donation), field, lon_w, lat_w, turn_parts, True)
    new_field = advance(section_one, *section(section_one, donation), field, lon_w, lat_w, turn_parts, False)
    return new_field.reshape(1, comps, levels, rows, cols)


def solution(mesh):
    in_specs = (
        P("panel", None, None, "lat", "lon"),
        P("panel", "lat", "lon", None),
        P("panel", "lat", "lon", None),
        P("panel", "lat", "lon", None, None),
        P("panel", "lat", "lon", None),
    )
    out_specs = P("panel", None, None, "lat", "lon")
    return jax.shard_map(
        per_device, mesh=mesh, in_specs=in_specs, out_specs=out_specs, check_vma=False
    )
```

```python
import jax
import jax.numpy as jnp
from jax import lax
from jax.sharding import PartitionSpec as P
from jax.experimental import pallas as pl
from jax.experimental.pallas import tpu as pltpu
import functools

INTERPRET = False

viscosity = 0.05
resistivity = 0.05
diffusivity = 0.05
buoyancy = 0.5
time_step = 0.25

HIGHEST = lax.Precision.HIGHEST


def stencil_kernel(*refs, first):
    if first:
        f_ref, halo_ref, lon_ref, lat_ref, turn_ref, o_ref, don_ref = refs
    else:
        f_ref, halo_ref, base_ref, o_ref = refs
    planes, height, width = f_ref.shape
    comps = planes // 2
    row = lax.broadcasted_iota(jnp.int32, (height, width), 0)
    col = lax.broadcasted_iota(jnp.int32, (height, width), 1)
    tile = lax.broadcasted_iota(jnp.int32, (8, width), 0)

    eye = jnp.where(
        lax.broadcasted_iota(jnp.int32, (height, height), 0) == lax.broadcasted_iota(jnp.int32, (height, height), 1),
        1.0,
        0.0,
    )
    pick_row = lax.broadcasted_iota(jnp.int32, (width, height), 0)

    def columns(k):
        left = halo_ref[k, 4:6, 0:height]
        right = halo_ref[k, 6:8, 0:height]
        rows_of = jnp.where(
            pick_row == 0,
            left[0:1, :],
            jnp.where(pick_row == 1, left[1:2, :], jnp.where(pick_row == 2, right[0:1, :], jnp.where(pick_row == 3, right[1:2, :], 0.0))),
        )
        return lax.dot_general(
            eye, rows_of, (((1,), (1,)), ((), ())), precision=HIGHEST, preferred_element_type=jnp.float32
        )

    def terms(k):
        x = f_ref[k]
        up = halo_ref[k, 0:2, :]
        down = halo_ref[k, 2:4, :]
        sides = columns(k)
        left = sides[:, 0:2]
        right = sides[:, 2:4]
        rolled = pltpu.roll(x, 1, 0)
        lat_m1 = jnp.concatenate([jnp.where(tile == 0, up[1:2, :], rolled[:8]), rolled[8:]], axis=0)
        rolled = pltpu.roll(x, 2, 0)
        top = jnp.where(tile == 0, up[0:1, :], jnp.where(tile == 1, up[1:2, :], rolled[:8]))
        lat_m2 = jnp.concatenate([top, rolled[8:]], axis=0)
        rolled = pltpu.roll(x, height - 1, 0)
        lat_p1 = jnp.concatenate([rolled[: height - 8], jnp.where(tile == 7, down[0:1, :], rolled[height - 8 :])], axis=0)
        rolled = pltpu.roll(x, height - 2, 0)
        bottom = jnp.where(tile == 7, down[1:2, :], jnp.where(tile == 6, down[0:1, :], rolled[height - 8 :]))
        lat_p2 = jnp.concatenate([rolled[: height - 8], bottom], axis=0)
        lon_m1 = jnp.where(col == 0, left[:, 1:2], pltpu.roll(x, 1, 1))
        lon_m2 = jnp.where(col == 0, left[:, 0:1], jnp.where(col == 1, left[:, 1:2], pltpu.roll(x, 2, 1)))
        lon_p1 = jnp.where(col == width - 1, right[:, 0:1], pltpu.roll(x, width - 1, 1))
        lon_p2 = jnp.where(
            col == width - 1, right[:, 1:2], jnp.where(col == width - 2, right[:, 0:1], pltpu.roll(x, width - 2, 1))
        )
        d_lat = (8.0 * (lat_p1 - lat_m1) - (lat_p2 - lat_m2)) * (1.0 / 12.0)
        d_lon = (8.0 * (lon_p1 - lon_m1) - (lon_p2 - lon_m2)) * (1.0 / 12.0)
        lap = lat_p1 + lat_m1 + lon_p1 + lon_m1 - 4.0 * x
        return x, d_lat, d_lon, lap

    for level in range(2):
        def plane(c):
            return c * 2 + level

        def value(c):
            return f_ref[plane(c)]

        def lap_of(c, x, lap):
            above = f_ref[c * 2 + 1] if level == 0 else 0.0
            below = f_ref[c * 2] if level == 1 else 0.0
            return lap + above + below - 2.0 * x

        def store(c, x, rate):
            section = x + time_step * rate
            if first:
                o_ref[plane(c)] = section
            else:
                o_ref[plane(c)] = 0.5 * base_ref[plane(c)] + 0.5 * section

        u1, u2, u4, u5, u6 = value(1), value(2), value(4), value(5), value(6)
        for c in range(3):
            xa, lat_a, lon_a, lap_a = terms(plane(c))
            xb, lat_b, lon_b, lap_b = terms(plane(c + 3))
            adv_u_a = u1 * lat_a + u2 * lon_a
            adv_b_a = u4 * lat_a + u5 * lon_a
            adv_u_b = u1 * lat_b + u2 * lon_b
            adv_b_b = u4 * lat_b + u5 * lon_b
            rate_a = -adv_u_a + adv_b_b + viscosity * lap_of(c, xa, lap_a)
            if c == 0:
                rate_a = rate_a + buoyancy * u6
            rate_b = adv_b_a - adv_u_b + resistivity * lap_of(c + 3, xb, lap_b)
            store(c, xa, rate_a)
            store(c + 3, xb, rate_b)
        x6, lat_6, lon_6, lap_6 = terms(plane(6))
        adv_u_6 = u1 * lat_6 + u2 * lon_6
        store(6, x6, -adv_u_6 + diffusivity * lap_of(6, x6, lap_6))

    if first:
        donate_planes(lambda k: o_ref[k], planes, lon_ref[...], lat_ref[...], turn_ref, don_ref)


def advance(field, halo, base, lon, lat, turn, first):
    shape = jax.ShapeDtypeStruct(field.shape, field.dtype)
    if first:
        shape = (shape, jax.ShapeDtypeStruct((field.shape[0], lon.shape[1]), jnp.float32))
    return pl.pallas_call(
        functools.partial(stencil_kernel, first=first),
        out_shape=shape,
        interpret=INTERPRET,
    )(*((field, halo, lon, lat, turn) if first else (field, halo, base)))


def donation_weights(cells_ref, frac_ref, rows, cols):
    dons = cells_ref.shape[1]
    cell = cells_ref[...].astype(jnp.float32)
    row = jnp.floor((cell + 0.5) * (1.0 / (cols - 1)))
    col = cell - row * (cols - 1)
    row = row.astype(jnp.int32)
    col = col.astype(jnp.int32)
    frac_t = frac_ref[0:1, :]
    frac_p = frac_ref[1:2, :]
    col_ids = lax.broadcasted_iota(jnp.int32, (cols, dons), 0)
    row_ids = lax.broadcasted_iota(jnp.int32, (rows, dons), 0)
    weight_lon = jnp.where(col_ids == col, 1.0 - frac_p, 0.0) + jnp.where(col_ids == col + 1, frac_p, 0.0)
    weight_lat = jnp.where(row_ids == row, 1.0 - frac_t, 0.0) + jnp.where(row_ids == row + 1, frac_t, 0.0)
    return weight_lon, weight_lat


def donate_planes(plane_of, planes, weight_lon, weight_lat, turn_ref, out_ref):
    cosine = turn_ref[0:1, :]
    sine = turn_ref[1:2, :]
    values = []
    for k in range(planes):
        along = jnp.dot(plane_of(k), weight_lon, precision=HIGHEST, preferred_element_type=jnp.float32)
        values.append(jnp.sum(along * weight_lat, axis=0, keepdims=True))
    for k in range(planes):
        comp, level = divmod(k, 2)
        if comp in (1, 4):
            value = cosine * values[k] - sine * values[k + 2]
        elif comp in (2, 5):
            value = sine * values[k - 2] + cosine * values[k]
        else:
            value = values[k]
        out_ref[k : k + 1, :] = value


def donation_kernel(f_ref, cells_ref, frac_ref, angle_ref, out_ref, lon_ref, lat_ref, turn_ref):
    angle = angle_ref[...]
    turn_ref[0:1, :] = jnp.cos(angle)
    turn_ref[1:2, :] = jnp.sin(angle)
    planes, rows, cols = f_ref.shape
    weight_lon, weight_lat = donation_weights(cells_ref, frac_ref, rows, cols)
    lon_ref[...] = weight_lon
    lat_ref[...] = weight_lat
    donate_planes(lambda k: f_ref[k], planes, weight_lon, weight_lat, turn_ref, out_ref)


def first_donation(field, cells, frac, turn):
    planes, rows, cols = field.shape
    dons = cells.shape[1]
    return pl.pallas_call(
        donation_kernel,
        out_shape=(
            jax.ShapeDtypeStruct((planes, dons), jnp.float32),
            jax.ShapeDtypeStruct((cols, dons), jnp.float32),
            jax.ShapeDtypeStruct((rows, dons), jnp.float32),
            jax.ShapeDtypeStruct((2, dons), jnp.float32),
        ),
        interpret=INTERPRET,
    )(field, cells, frac, turn)


def rotate(values, turn):
    cosine = jnp.cos(turn)
    sine = jnp.sin(turn)
    parts = [
        values[0],
        cosine * values[1] - sine * values[2],
        sine * values[1] + cosine * values[2],
        values[3],
        cosine * values[4] - sine * values[5],
        sine * values[4] + cosine * values[5],
        values[6],
    ]
    return jnp.stack(parts)


def per_device(state, source_slot, donor_cell, donor_frac, donor_turn):
    comps = state.shape[1]
    levels = state.shape[2]
    rows = state.shape[3]
    cols = state.shape[4]
    cells = donor_cell[0, 0, 0]
    frac_t = donor_frac[0, 0, 0, 0]
    frac_p = donor_frac[0, 0, 0, 1]
    turn = donor_turn[0, 0, 0]
    slots = source_slot[0, 0, 0]
    lat_pos = lax.axis_index("lat")
    lon_pos = lax.axis_index("lon")
    lat_count = lax.axis_size("lat")
    lon_count = lax.axis_size("lon")
    on_top = lat_pos == 0
    on_bottom = lat_pos == lat_count - 1
    on_left = lon_pos == 0
    on_right = lon_pos == lon_count - 1

    band = 2 * cols
    side = 2 * rows
    lat_slots = jnp.where(on_top, slots[0:band], slots[band : 2 * band])
    lon_slots = jnp.where(on_left, slots[2 * band : 2 * band + side], slots[2 * band + side :])
    wanted = jnp.concatenate([lat_slots, lon_slots])
    total = lat_count * lon_count * cells.shape[0]
    dons_each = cells.shape[0]
    half = lon_count // 2
    chunk = jnp.arange(half * lat_count * dons_each, dtype=jnp.int32)

    lon_bits = lon_count.bit_length() - 1
    lat_bits = lat_count.bit_length() - 1

    def reverse(value, bits):
        return sum(((value >> i) & 1) << (bits - 1 - i) for i in range(bits))

    def pick_for(low_bit):
        block = chunk // (lat_count * dons_each)
        device = low_bit + reverse(block, lon_bits - 1) * 2
        lat_of = reverse(chunk // dons_each % lat_count, lat_bits)
        index = (lat_of * lon_count + device) * dons_each + chunk % dons_each
        return (index[:, None] == wanted[None, :]).astype(jnp.bfloat16)

    pick_held = pick_for(lon_pos % 2)
    pick_new = pick_for(1 - lon_pos % 2)

    def select(values, pick):
        high = lax.reduce_precision(values, exponent_bits=8, mantissa_bits=7)
        rest = values - high
        middle = lax.reduce_precision(rest, exponent_bits=8, mantissa_bits=7)
        low = rest - middle
        parts = jnp.concatenate([high, middle, low]).astype(jnp.bfloat16)
        picked = jnp.dot(parts, pick, preferred_element_type=jnp.float32)
        count = values.shape[0]
        return picked[:count] + (picked[count : 2 * count] + picked[2 * count :])

    def gather(packet, axis, far_first=False):
        size = lax.axis_size(axis)
        pos = lax.axis_index(axis)
        held = packet[None]
        steps = []
        k = 1
        while k < size:
            steps.append(k)
            k *= 2
        if far_first:
            steps.reverse()
        for k in steps:
            before = held
            other = lax.ppermute(held, axis, [(i, i ^ k) for i in range(size)])
            low = (pos // k) % 2 == 0
            held = jnp.where(low, jnp.concatenate([held, other]), jnp.concatenate([other, held]))
        return held, before, other

    def section(field, donation):
        flat = field
        given = lax.ppermute(donation, "panel", [(0, 1), (1, 0)])
        dons = given.shape[1]
        side_rows = jnp.concatenate([flat[:, :2, :], flat[:, rows - 2 :, :]], axis=1)
        lat_packet = jnp.concatenate([given, side_rows.reshape(comps * levels, -1)], axis=1)
        lat_all = gather(lat_packet, "lat", far_first=True)[0]
        col_given = jnp.transpose(lat_all[:, :, :dons], (1, 0, 2)).reshape(comps * levels, -1)
        side_rows = lat_all[:, :, dons:].reshape(lat_count, comps, levels, 4, cols)
        side_cols = jnp.concatenate([flat[:, :, :2], flat[:, :, cols - 2 :]], axis=2)
        side_cols = jnp.swapaxes(side_cols, 1, 2)
        lon_packet = jnp.concatenate([col_given, side_cols.reshape(comps * levels, -1)], axis=1)
        lon_all, lon_held, lon_new = gather(lon_packet, "lon", far_first=True)
        width = col_given.shape[1]
        held_part = jnp.transpose(lon_held[:, :, :width], (1, 0, 2)).reshape(comps * levels, -1)
        new_part = jnp.transpose(lon_new[:, :, :width], (1, 0, 2)).reshape(comps * levels, -1)
        side_cols = lon_all[:, :, width:].reshape(lon_count, comps, levels, 4, rows)
        up_at = reverse(jnp.maximum(lat_pos - 1, 0), lat_bits)
        down_at = reverse(jnp.minimum(lat_pos + 1, lat_count - 1), lat_bits)
        up = lax.dynamic_index_in_dim(side_rows, up_at, keepdims=False)[:, :, 2:]
        down = lax.dynamic_index_in_dim(side_rows, down_at, keepdims=False)[:, :, :2]
        left_at = reverse(jnp.maximum(lon_pos - 1, 0), lon_bits)
        right_at = reverse(jnp.minimum(lon_pos + 1, lon_count - 1), lon_bits)
        left = lax.dynamic_index_in_dim(side_cols, left_at, keepdims=False)[:, :, 2:]
        right = lax.dynamic_index_in_dim(side_cols, right_at, keepdims=False)[:, :, :2]
        rim = (select(held_part, pick_held) + select(new_part, pick_new)).reshape(comps, levels, -1)
        rim_lat = rim[:, :, :band].reshape(comps, levels, 2, cols)
        rim_lon = rim[:, :, band:].reshape(comps, levels, 2, rows)
        up = jnp.where(on_top, rim_lat, up).reshape(comps * levels, 2, cols)
        down = jnp.where(on_bottom, rim_lat, down).reshape(comps * levels, 2, cols)
        left = jnp.where(on_left, rim_lon, left).reshape(comps * levels, 2, rows)
        right = jnp.where(on_right, rim_lon, right).reshape(comps * levels, 2, rows)
        sides = jnp.pad(jnp.concatenate([left, right], axis=1), ((0, 0), (0, 0), (0, cols - rows)))
        return (jnp.concatenate([up, down, sides], axis=1),)

    field = state[0].reshape(comps * levels, rows, cols)
    donation, lon_w, lat_w, turn_parts = first_donation(field, donor_cell[0, 0], donor_frac[0, 0, 0], donor_turn[0, 0])
    section_one, donation = advance(field, *section(field, donation), field, lon_w, lat_w, turn_parts, True)
    new_field = advance(section_one, *section(section_one, donation), field, lon_w, lat_w, turn_parts, False)
    return new_field.reshape(1, comps, levels, rows, cols)


def solution(mesh):
    in_specs = (
        P("panel", None, None, "lat", "lon"),
        P("panel", "lat", "lon", None),
        P("panel", "lat", "lon", None),
        P("panel", "lat", "lon", None, None),
        P("panel", "lat", "lon", None),
    )
    out_specs = P("panel", None, None, "lat", "lon")
    return jax.shard_map(
        per_device, mesh=mesh, in_specs=in_specs, out_specs=out_specs, check_vma=False
    )
```
